32 devices in a mesh: dom: 8 (over z, x), pme: 4 (over y, core).
Axes of the slice: x: 2, y: 2, z: 4, core: 2. Of those that a mesh axis runs over, the one named last changes fastest.
Arguments:
- feats: bfloat16 [8192, 128], P(('dom', 'pme')), may hold values from -6 to 6
- coords: float32 [3, 8192], P(None, ('dom', 'pme')), may hold values from 0 to 3
- nbrs: int32 [8192, 48], P(('dom', 'pme')), may hold values from 0 to 767, as said below
- owner: int32 [8192, 1], P(('dom', 'pme')), may hold values from 0 to 31; in each aligned block of 256 rows (0 to 255, 256 to 511, ...) at most 16 rows name the same one
- cell: int32 [8192], P(('dom', 'pme')), may hold values from 0 to 262143
- w_self: bfloat16 [2, 128, 128], replicated, may hold values from -0.5 to 0.5
- w_nbr: bfloat16 [2, 128, 128], replicated, may hold values from -0.5 to 0.5
- w_rad: float32 [2, 8, 128], replicated, may hold values from -2 to 2
- w_msg: bfloat16 [2, 128, 128], replicated, may hold values from -0.5 to 0.5
- w_out: bfloat16 [2, 128, 128], replicated, may hold values from -0.5 to 0.5
- norm_gain: float32 [2, 128], replicated, may hold values from 0.1 to 1.9
- w_charge: float32 [128], replicated, may hold values from -0.5 to 0.5
- w_energy: float32 [128], replicated, may hold values from -0.5 to 0.5
Outputs:
- energy_ml: float32 [8192], P(('dom', 'pme'))
- energy_el: float32 [8192], P(('dom', 'pme'))
The draws below stay inside these ranges and needn't reach their ends.
Inputs may be any that keep to these rules, and one draw needn't show every extreme that they name: `nbrs`: entry k of an atom's list is a row of its domain's previous 256 atoms, own 256 atoms and next 256 atoms laid end to end, never the atom itself. The owner is numbered dom index times the size of pme plus pme index; among the 256 atoms of one domain at most 16 have the same owner.
All inputs are finite; a program needn't handle non-finite values.
Results may differ from the reference program's by a relative error of at most 0.017.
Values may be sent and summed in bfloat16 or wider, within the bound.
No kernel may reach another device: no remote copies, remote signals or barrier semaphores. Data moves between devices by JAX's collectives and lax.ppermute only.
A program may use at most 128 MiB of HBM per device.

```python
import math
import jax
import jax.numpy as jnp
import numpy as np
from jax import lax

F = 128
NB = 8
K = 48
LAYERS = 2
GX = 256
GY = 256
GZ = 128
ATOM_DEV = 256
ATOMS = 8192
CAP = 16
CELLS = 262144
N_DOM = 8
N_PME = 4
DEVICES = 32


def draw_nbrs(key, part):
    local = jnp.arange(ATOMS, dtype=jnp.int32) % ATOM_DEV
    offset = jax.random.randint(key, (ATOMS, K), -ATOM_DEV, ATOM_DEV, dtype=jnp.int32)
    offset = offset + (offset >= 0).astype(jnp.int32)
    column = jnp.arange(K, dtype=jnp.int32)[None, :]
    offset = jnp.where((local[:, None] == 0) & (column == 0), -ATOM_DEV, offset)
    offset = jnp.where((local[:, None] == ATOM_DEV - 1) & (column == 0), ATOM_DEV, offset)
    return (local[:, None] + ATOM_DEV + offset).astype(jnp.int32)


def place_ends(result, stream_key, least, high):
    index_at = [jax.random.randint(jax.random.fold_in(stream_key, axis), (), 0, length) for axis, length in enumerate(result.shape)]
    longest = result.shape.index(max(result.shape))
    beside = index_at[:longest] + [(index_at[longest] + 1) % result.shape[longest]] + index_at[longest + 1:]
    return result.at[tuple(index_at)].set(least).at[tuple(beside)].set(high)


def block_scale(key, shape, pieces, smallest, high):
    loudness, own = 1.0, jax.random.fold_in(key, 6)
    for dim, blocks in pieces:
        steps = jnp.exp(jax.random.uniform(jax.random.fold_in(own, dim), (blocks,), jnp.float32, smallest / len(pieces), high / len(pieces)))
        loudness = loudness * jnp.repeat(steps, shape[dim] // blocks).reshape([-1 if axis == dim else 1 for axis in range(len(shape))])
    return loudness


def routed_block(stream_key, own, number, rows, number_of, top, bound, slope):
    ranking = jax.random.permutation(stream_key, number_of)
    heavy_load, usual = shares(number_of, rows * top, bound, slope, True), shares(number_of, rows * top, bound, slope, False)
    places = jnp.arange(number_of)

    def named(lengths, offset_by):
        used = int((lengths > 0).sum())
        fixed = max(1, used // 4)
        passed = fixed + (places - fixed + offset_by * (used - fixed)) % max(1, number_of - fixed)
        return jnp.zeros((number_of,), jnp.int32).at[ranking[jnp.where(places < fixed, places, passed)]].set(jnp.asarray(lengths, jnp.int32))

    lengths = jnp.where(number % 4 == 0, named(heavy_load, number // 4), named(usual, number - number // 4 - 1))
    mixed = jax.random.permutation(jax.random.fold_in(own, 3), number_of)
    giver, sink = mixed[0:number_of // 2 * 2:2], mixed[1:number_of // 2 * 2:2]
    margin = jnp.minimum(lengths[giver] - 1, bound - lengths[sink]) // 2
    margin = jnp.where((giver == ranking[0]) | (sink == ranking[0]) | (lengths[sink] == 0), 0, jnp.maximum(margin, 0))
    passed = jax.random.randint(jax.random.fold_in(own, 4), (number_of // 2,), 0, 1 << 20) % (margin + 1)
    lengths = lengths.at[giver].add(-passed).at[sink].add(passed)
    members = jnp.searchsorted(jnp.cumsum(lengths), jnp.arange(rows * top), side="right").astype(jnp.int32)
    listing = members.reshape(top, rows).T
    listing = listing[jax.random.permutation(jax.random.fold_in(own, 1), rows)]
    offset_by = jax.random.randint(jax.random.fold_in(own, 2), (rows, 1), 0, top)
    return jnp.take_along_axis(listing, (jnp.arange(top)[None, :] + offset_by) % top, axis=1)


def shares(count, total, reach, slope, full):
    weights = [(1 << 20) // math.isqrt(rank ** slope) + 1 for rank in range(1, count + 1)]
    largest = reach if full else min(reach, max(-(-total // count), total * weights[0] // sum(weights)))
    least = 1 if total - largest >= count - 1 else 0
    holding, surplus = [largest] + [least] * (count - 1), total - largest - least * (count - 1)
    while surplus > 0:
        free = [i for i in range(1, count) if holding[i] < largest] or [i for i in range(1, count) if holding[i] < reach]
        mass, remaining = sum([weights[i] for i in free]), surplus
        for i in free:
            extra = min(reach - holding[i], max(1, remaining * weights[i] // mass), surplus)
            holding[i] = holding[i] + extra
            surplus = surplus - extra
    return np.array(holding)


def noise(stream_key, extent, scale, bound, split=(), kind=jnp.bfloat16):
    values = scale * jax.random.normal(stream_key, extent, jnp.float32)
    if split:
        values = values * block_scale(stream_key, extent, split, -0.22, 0.18)
    return jnp.clip(values, -bound, bound).astype(kind)


def setup_inputs(seed: int = 0) -> dict:
    splits = jax.random.split(jax.random.key(seed), 14)
    feats = noise(splits[0], (ATOMS, F), 1.0, 6.0, ((0, 32),))
    coords = jnp.clip(3.0 * jax.random.uniform(splits[1], (3, ATOMS), jnp.float32) ** block_scale(splits[1], (3, ATOMS), ((1, 32),), -0.2, 0.2), 0.0, 3.0)
    nbrs = draw_nbrs(jax.random.fold_in(splits[13], 71), 0)
    owner_keys = jax.random.split(jax.random.fold_in(splits[3], 1), ATOMS // ATOM_DEV)
    owner_turns = jax.random.permutation(jax.random.fold_in(splits[3], 3), ATOMS // ATOM_DEV)
    owner = jax.vmap(lambda own, number: routed_block(jax.random.fold_in(splits[3], 2), own, number, ATOM_DEV, DEVICES, 1, CAP, 2))(owner_keys, owner_turns).reshape((ATOMS, 1))
    cell = place_ends(jax.random.randint(splits[4], (ATOMS,), 0, CELLS), jax.random.fold_in(splits[4], 1), 0, CELLS - 1).astype(jnp.int32)
    w_self = noise(splits[5], (LAYERS, F, F), F ** -0.5, 0.5)
    w_nbr = noise(splits[6], (LAYERS, F, F), F ** -0.5, 0.5)
    w_rad = noise(splits[7], (LAYERS, NB, F), NB ** -0.5, 2.0, (), jnp.float32)
    w_msg = noise(splits[8], (LAYERS, F, F), F ** -0.5, 0.5)
    w_out = noise(splits[9], (LAYERS, F, F), F ** -0.5, 0.5)
    norm_gain = jnp.clip(1.0 + 0.18 * jax.random.normal(splits[10], (LAYERS, F), jnp.float32), 0.1, 1.9)
    w_charge = noise(splits[11], (F,), F ** -0.5, 0.5, (), jnp.float32)
    w_energy = noise(splits[12], (F,), F ** -0.5, 0.5, (), jnp.float32)
    return dict(feats=feats, coords=coords, nbrs=nbrs, owner=owner, cell=cell, w_self=w_self, w_nbr=w_nbr, w_rad=w_rad, w_msg=w_msg, w_out=w_out, norm_gain=norm_gain, w_charge=w_charge, w_energy=w_energy)


slab_depth = 3.0
radial_width = 0.75
ewald_beta = 1.2
norm_eps = 1e-05
highest = lax.Precision.HIGHEST

def radial_terms(dist):
    centres = radial_width * (jnp.arange(NB, dtype=jnp.float32) + 1.0)
    return jnp.exp(-jnp.square((dist[None] - centres[:, None, None]) / radial_width))

def block_update(own_term, wide_term, h_own, pos_own, pos_wide, neigh, w_rad, w_msg, w_out, gain):
    rows, fanout = neigh.shape
    width = own_term.shape[1]
    delta = pos_wide[:, neigh] - pos_own[:, :, None]
    dist = jnp.sqrt(lax.optimization_barrier(jnp.sum(delta * delta, axis=0)) + 1.0)
    radial = radial_terms(dist)
    pre = own_term[:, None, :] + wide_term[neigh] + jnp.einsum('nak,nf->akf', radial, w_rad, precision=highest)
    message = jax.nn.silu(pre).astype(jnp.bfloat16)
    mixed = jnp.dot(message.reshape(rows * fanout, width), w_msg, preferred_element_type=jnp.float32)
    mixed = mixed.reshape(rows, fanout, width)
    scalar = lax.optimization_barrier(jnp.sum(mixed, axis=1)) / fanout
    unit = delta / dist[None]
    vector = jnp.einsum('cak,akf->caf', unit, mixed, precision=highest) / fanout
    total = scalar + lax.optimization_barrier(jnp.sum(vector * vector, axis=0))
    normed = total * lax.rsqrt(lax.optimization_barrier(jnp.mean(total * total, axis=-1, keepdims=True)) + norm_eps) * gain
    active = jax.nn.silu(normed).astype(jnp.bfloat16)
    update = jnp.dot(active, w_out, preferred_element_type=jnp.float32)
    return (h_own.astype(jnp.float32) + update).astype(jnp.bfloat16)

def wave_square(count, start, full):
    index = start + jnp.arange(count, dtype=jnp.int32)
    folded = jnp.where(index < full // 2, index, index - full).astype(jnp.float32)
    scaled = folded * (2.0 * math.pi / full)
    return scaled * scaled

def green(wave_x, wave_y, wave_z):
    ksq = wave_x[:, None, None] + wave_y[None, :, None] + wave_z[None, None, :]
    safe = jnp.where(ksq > 0, ksq, 1.0)
    return jnp.where(ksq > 0, 4.0 * math.pi * jnp.exp(-ksq / (4.0 * ewald_beta * ewald_beta)) / safe, 0.0)

def reference(feats, coords, nbrs, owner, cell, w_self, w_nbr, w_rad, w_msg, w_out, norm_gain, w_charge, w_energy):
    domains = feats.shape[0] // ATOM_DEV
    width = feats.shape[1]
    pos = coords.reshape(3, domains, ATOM_DEV).transpose(1, 0, 2)
    lift = jnp.zeros((3, 1), jnp.float32).at[2, 0].set(slab_depth)
    pos_wide = jnp.concatenate([jnp.roll(pos, 1, axis=0) - lift, pos, jnp.roll(pos, -1, axis=0) + lift], axis=2)
    neigh = nbrs.reshape(domains, ATOM_DEV, K)
    hidden = feats.reshape(domains, ATOM_DEV, width)
    for layer_idx in range(LAYERS):
        wide = jnp.concatenate([jnp.roll(hidden, 1, axis=0), hidden, jnp.roll(hidden, -1, axis=0)], axis=1)

        def one_domain(parts):
            h_own, h_wide, p_own, p_wide, nb_list = parts
            own_term = jnp.dot(h_own, w_self[layer_idx], preferred_element_type=jnp.float32)
            wide_term = jnp.dot(h_wide, w_nbr[layer_idx], preferred_element_type=jnp.float32)
            return block_update(own_term, wide_term, h_own, p_own, p_wide, nb_list, w_rad[layer_idx], w_msg[layer_idx], w_out[layer_idx], norm_gain[layer_idx])
        hidden = lax.map(one_domain, (hidden, wide, pos, pos_wide, neigh))
    flat_hidden = hidden.reshape(-1, width).astype(jnp.float32)
    energy_ml = jnp.dot(flat_hidden, w_energy, precision=highest)
    charge = jnp.dot(flat_hidden, w_charge, precision=highest)
    block_x = GX // N_DOM
    block_y = GY // N_PME
    dest = owner[:, 0]
    grid_x = dest // N_PME * block_x + cell // (block_y * GZ)
    grid_y = dest % N_PME * block_y + cell // GZ % block_y
    grid_z = cell % GZ
    density = jnp.zeros((GX, GY, GZ), jnp.float32).at[grid_x, grid_y, grid_z].add(charge)
    kernel = green(wave_square(GX, 0, GX), wave_square(GY, 0, GY), wave_square(GZ, 0, GZ))
    spectrum = jnp.fft.fftn(density) * kernel
    potential = jnp.real(jnp.fft.ifftn(spectrum))
    at_atoms = potential[grid_x, grid_y, grid_z]
    energy_el = 0.5 * charge * at_atoms
    return (energy_ml, energy_el)
```

```python
import math

import jax
import jax.numpy as jnp
import numpy as np
from jax import lax
from jax.sharding import PartitionSpec as P

NB = 8
LAYERS = 2
GX = 256
GY = 256
GZ = 128


slab_depth = 3.0
radial_width = 0.75
ewald_beta = 1.2
norm_eps = 1e-05
highest = lax.Precision.HIGHEST
AXES = ("dom", "pme")


def to_bf16_exact(x):
    return lax.reduce_precision(x, exponent_bits=8, mantissa_bits=7)


def split2(x):
    hi = to_bf16_exact(x)
    lo = x - hi
    return hi.astype(jnp.bfloat16), lo.astype(jnp.bfloat16)


def split3(x):
    hi = to_bf16_exact(x)
    rest = x - hi
    mid = to_bf16_exact(rest)
    lo = rest - mid
    return hi.astype(jnp.bfloat16), mid.astype(jnp.bfloat16), lo.astype(jnp.bfloat16)


def halo(shard):
    devices = lax.axis_size(AXES)
    up = [(i, (i + 1) % devices) for i in range(devices)]
    down = [(j, i) for i, j in up]
    before = lax.ppermute(shard, AXES, up)
    after = lax.ppermute(shard, AXES, down)
    return jnp.concatenate([before, shard, after], axis=0)


def silu(x):
    return x * jax.nn.sigmoid(x)


def dft_pair(length):
    k = np.arange(length, dtype=np.int64)
    angle = (np.outer(k, k) % length).astype(np.float64) * (2.0 * math.pi / length)
    return np.cos(angle), np.sin(angle)


def wave_square(count, start, full):
    index = start + jnp.arange(count, dtype=jnp.int32)
    folded = jnp.where(index < full // 2, index, index - full).astype(jnp.float32)
    scaled = folded * (2.0 * math.pi / full)
    return scaled * scaled


def green(wave_x, wave_y, wave_z):
    ksq = wave_x[:, None, None] + wave_y[None, :, None] + wave_z[None, None, :]
    safe = jnp.where(ksq > 0, ksq, 1.0)
    return jnp.where(
        ksq > 0, 4.0 * math.pi * jnp.exp(-ksq / (4.0 * ewald_beta * ewald_beta)) / safe, 0.0
    )


def mm(a, b):
    return jnp.dot(a, b, preferred_element_type=jnp.float32)


def forward_combine(p, forward):
    c_re, c_im = p[0, ..., 0, :], p[0, ..., 1, :]
    s_re, s_im = p[1, ..., 0, :], p[1, ..., 1, :]
    if forward:
        return jnp.stack([c_re + s_im, c_im - s_re], axis=-2)
    return jnp.stack([c_re - s_im, c_im + s_re], axis=-2)


def solve_field(density, n_dom, n_pme, dom_index, pme_index):
    by, bx, _ = density.shape
    kls = GZ // n_pme
    kyls = GY // n_dom
    cz, sz = dft_pair(GZ)
    fz = np.stack([cz, -sz], axis=1).reshape(GZ, 2, n_pme, kls).transpose(0, 2, 1, 3)
    fz = jnp.asarray(fz.reshape(GZ, 2 * GZ), jnp.bfloat16)
    d_hi, d_lo = split2(density.reshape(by * bx, GZ))
    a = mm(d_hi, fz) + mm(d_lo, fz)
    a = a.reshape(by, bx, n_pme, 2 * kls).transpose(2, 0, 1, 3).astype(jnp.bfloat16)
    r1 = lax.all_to_all(a, "pme", 0, 0, tiled=True)
    r1 = r1.reshape(GY, bx * 2 * kls)
    cy, sy = dft_pair(GY)
    fy = jnp.asarray(np.concatenate([cy, sy], axis=0), jnp.bfloat16)
    p = mm(fy, r1).reshape(2, GY, bx, 2, kls)
    y = forward_combine(p, True)
    y = y.reshape(n_dom, kyls, bx, 2, kls).transpose(0, 2, 1, 3, 4).astype(jnp.bfloat16)
    r2 = lax.all_to_all(y, "dom", 0, 0, tiled=True)
    r2 = r2.reshape(GX, kyls * 2 * kls)
    cx, sx = dft_pair(GX)
    fx = jnp.asarray(np.concatenate([cx, sx], axis=0), jnp.bfloat16)
    p2 = mm(fx, r2).reshape(2, GX, kyls, 2, kls)
    z = forward_combine(p2, True)
    kernel = green(
        wave_square(GX, 0, GX),
        wave_square(kyls, dom_index * kyls, GY),
        wave_square(kls, pme_index * kls, GZ),
    ) * (1.0 / (GX * GY * GZ))
    z = (z * kernel[:, :, None, :]).astype(jnp.bfloat16)
    p3 = mm(fx, z.reshape(GX, kyls * 2 * kls)).reshape(2, GX, kyls, 2, kls)
    w = forward_combine(p3, False)
    w = w.reshape(n_dom, bx, kyls, 2, kls).transpose(0, 2, 1, 3, 4).astype(jnp.bfloat16)
    r3 = lax.all_to_all(w, "dom", 0, 0, tiled=True)
    r3 = r3.reshape(GY, bx * 2 * kls)
    p4 = mm(fy, r3).reshape(2, GY, bx, 2, kls)
    v = forward_combine(p4, False)
    v = v.reshape(n_pme, by, bx, 2, kls).astype(jnp.bfloat16)
    r4 = lax.all_to_all(v, "pme", 0, 0, tiled=True)
    r4 = r4.reshape(n_pme, by * bx, 2 * kls)
    ez = np.stack([cz, -sz], axis=0).reshape(2, n_pme, kls, GZ).transpose(1, 0, 2, 3)
    ez = jnp.asarray(ez.reshape(n_pme, 2 * kls, GZ), jnp.bfloat16)
    phi = jnp.einsum("bnc,bcz->nz", r4, ez, preferred_element_type=jnp.float32)
    return phi.reshape(-1)


def gnn_layer(hidden, gathered, unit_w, radial_parts, w_self, w_nbr, w_rad, w_msg, w_out, gain):
    atoms, width = hidden.shape
    fanout = gathered.shape[0] // atoms
    gathered_h = gathered[:, :width].astype(jnp.bfloat16)
    r_hi, r_lo = radial_parts
    w_hi, w_lo = split2(w_rad)
    lhs = jnp.concatenate([gathered_h, r_hi, r_lo, r_hi], axis=1)
    rhs = jnp.concatenate([w_nbr, w_hi, w_hi, w_lo], axis=0)
    own_term = mm(hidden, w_self)
    pre = mm(lhs, rhs).reshape(atoms, fanout, width) + own_term[:, None, :]
    message = to_bf16_exact(silu(pre))
    sums = jnp.sum(unit_w[:, :, :, None] * message[:, :, None, :], axis=1)
    s_hi, s_lo = split2(sums.reshape(atoms * 4, width))
    mixed = (mm(s_hi, w_msg) + mm(s_lo, w_msg)).reshape(atoms, 4, width) / fanout
    total = mixed[:, 0] + jnp.sum(mixed[:, 1:] * mixed[:, 1:], axis=1)
    normed = total * lax.rsqrt(jnp.mean(total * total, axis=-1, keepdims=True) + norm_eps) * gain
    active = silu(normed).astype(jnp.bfloat16)
    update = mm(active, w_out)
    return (hidden.astype(jnp.float32) + update).astype(jnp.bfloat16)


def per_device(
    feats,
    coords,
    nbrs,
    owner,
    cell,
    w_self,
    w_nbr,
    w_rad,
    w_msg,
    w_out,
    norm_gain,
    w_charge,
    w_energy,
):
    atoms, width = feats.shape
    fanout = nbrs.shape[1]
    n_dom = lax.axis_size("dom")
    n_pme = lax.axis_size("pme")
    devices = n_dom * n_pme
    wide_rows = 3 * atoms
    pos_own = coords.T
    p_hi, p_mid, p_lo = split3(pos_own)
    wide0 = halo(jnp.concatenate([feats, p_hi, p_mid, p_lo], axis=1))
    flat_nbrs = nbrs.reshape(-1)
    onehot = (flat_nbrs[:, None] == jnp.arange(wide_rows, dtype=jnp.int32)[None, :]).astype(
        jnp.bfloat16
    )
    hidden = feats
    unit_w = None
    radial_parts = None
    for layer_idx in range(LAYERS):
        table = wide0 if layer_idx == 0 else halo(hidden)
        gathered = mm(onehot, table)
        if layer_idx == 0:
            gp = gathered[:, width:]
            pos_j = gp[:, 0:3] + gp[:, 3:6] + gp[:, 6:9]
            lift = jnp.where(flat_nbrs < atoms, -slab_depth, jnp.where(flat_nbrs >= 2 * atoms, slab_depth, 0.0))
            pos_j = pos_j.at[:, 2].add(lift)
            delta = pos_j.reshape(atoms, fanout, 3) - pos_own[:, None, :]
            dist = jnp.sqrt(jnp.sum(delta * delta, axis=-1) + 1.0)
            centres = radial_width * (jnp.arange(NB, dtype=jnp.float32) + 1.0)
            radial = jnp.exp(-jnp.square((dist[:, :, None] - centres) / radial_width))
            radial_parts = split2(radial.reshape(atoms * fanout, NB))
            unit = delta / dist[:, :, None]
            unit_w = jnp.concatenate([jnp.ones((atoms, fanout, 1), jnp.float32), unit], axis=-1)
        hidden = gnn_layer(
            hidden,
            gathered,
            unit_w,
            radial_parts,
            w_self[layer_idx],
            w_nbr[layer_idx],
            w_rad[layer_idx],
            w_msg[layer_idx],
            w_out[layer_idx],
            norm_gain[layer_idx],
        )
    flat_hidden = hidden.astype(jnp.float32)
    readout = jnp.dot(flat_hidden, jnp.stack([w_energy, w_charge], axis=1), precision=highest)
    energy_ml = readout[:, 0]
    charge = readout[:, 1]
    capacity = max(2, 2 * atoms // devices)
    dest = owner[:, 0]
    matches = (dest[:, None] == jnp.arange(devices, dtype=jnp.int32)[None, :]).astype(jnp.int32)
    slot = jnp.sum((jnp.cumsum(matches, axis=0) - matches) * matches, axis=1)
    where_to = dest * capacity + slot
    payload = jnp.stack([charge, cell.astype(jnp.float32)], axis=1)
    outgoing = jnp.zeros((devices * capacity, 2), jnp.float32).at[where_to].set(payload)
    incoming = lax.all_to_all(outgoing, AXES, 0, 0, tiled=True)
    bx = GX // n_dom
    by = GY // n_pme
    cells_here = incoming[:, 1].astype(jnp.int32)
    xl = cells_here // (by * GZ)
    yl = cells_here // GZ % by
    zz = cells_here % GZ
    index_here = (yl * bx + xl) * GZ + zz
    density = jnp.zeros((by * bx * GZ,), jnp.float32).at[index_here].add(incoming[:, 0])
    potential = solve_field(
        density.reshape(by, bx, GZ), n_dom, n_pme, lax.axis_index("dom"), lax.axis_index("pme")
    )
    sampled = potential[index_here]
    returned = lax.all_to_all(sampled, AXES, 0, 0, tiled=True)
    at_atoms = returned[where_to]
    energy_el = 0.5 * charge * at_atoms
    return (energy_ml, energy_el)


def solution(mesh):
    in_specs = (
        P(("dom", "pme"), None),
        P(None, ("dom", "pme")),
        P(("dom", "pme"), None),
        P(("dom", "pme"), None),
        P(("dom", "pme")),
        P(),
        P(),
        P(),
        P(),
        P(),
        P(),
        P(),
        P(),
    )
    out_specs = (P(("dom", "pme")), P(("dom", "pme")))
    return jax.shard_map(
        per_device, mesh=mesh, in_specs=in_specs, out_specs=out_specs, check_vma=False
    )
```

```python
import math

import jax
import jax.numpy as jnp
import numpy as np
from jax import lax
from jax.sharding import PartitionSpec as P

NB = 8
LAYERS = 2
GX = 256
GY = 256
GZ = 128


slab_depth = 3.0
radial_width = 0.75
ewald_beta = 1.2
norm_eps = 1e-05
highest = lax.Precision.HIGHEST
AXES = ("dom", "pme")


def to_bf16_exact(x):
    return lax.reduce_precision(x, exponent_bits=8, mantissa_bits=7)


def split2(x):
    hi = to_bf16_exact(x)
    lo = x - hi
    return hi.astype(jnp.bfloat16), lo.astype(jnp.bfloat16)


def split3(x):
    hi = to_bf16_exact(x)
    rest = x - hi
    mid = to_bf16_exact(rest)
    lo = rest - mid
    return hi.astype(jnp.bfloat16), mid.astype(jnp.bfloat16), lo.astype(jnp.bfloat16)


def halo(shard):
    devices = lax.axis_size(AXES)
    up = [(i, (i + 1) % devices) for i in range(devices)]
    down = [(j, i) for i, j in up]
    before = lax.ppermute(shard, AXES, up)
    after = lax.ppermute(shard, AXES, down)
    return jnp.concatenate([before, shard, after], axis=0)


def silu(x):
    return x * jax.nn.sigmoid(x)


def dft_pair(length):
    k = np.arange(length, dtype=np.int64)
    angle = (np.outer(k, k) % length).astype(np.float64) * (2.0 * math.pi / length)
    return np.cos(angle), np.sin(angle)


def wave_square(count, start, full):
    index = start + jnp.arange(count, dtype=jnp.int32)
    folded = jnp.where(index < full // 2, index, index - full).astype(jnp.float32)
    scaled = folded * (2.0 * math.pi / full)
    return scaled * scaled


def green(wave_x, wave_y, wave_z):
    ksq = wave_x[:, None, None] + wave_y[None, :, None] + wave_z[None, None, :]
    safe = jnp.where(ksq > 0, ksq, 1.0)
    return jnp.where(
        ksq > 0, 4.0 * math.pi * jnp.exp(-ksq / (4.0 * ewald_beta * ewald_beta)) / safe, 0.0
    )


def mm(a, b):
    return jnp.dot(a, b, preferred_element_type=jnp.float32)


def combine(p, forward):
    rows, cols = p.shape
    c, s = p[: rows // 2], p[rows // 2 :]
    c_re, c_im = c[:, : cols // 2], c[:, cols // 2 :]
    s_re, s_im = s[:, : cols // 2], s[:, cols // 2 :]
    if forward:
        return jnp.stack([c_re + s_im, c_im - s_re])
    return jnp.stack([c_re - s_im, c_im + s_re])


def solve_field(density, n_dom, n_pme, dom_index, pme_index):
    _, cols = density.shape
    by = GY // n_pme
    bx = GX // n_dom
    kls = GZ // n_pme
    kyls = GY // n_dom
    cz, sz = dft_pair(GZ)
    fz = np.concatenate([cz, -sz], axis=0)
    fz2 = jnp.asarray(np.concatenate([fz, fz], axis=1), jnp.bfloat16)
    d_hi, d_lo = split2(density)
    a = mm(fz2, jnp.concatenate([d_hi, d_lo], axis=0))
    a = a.reshape(2, n_pme, kls, by, bx).transpose(1, 3, 0, 2, 4)
    a = a.reshape(n_pme, by, 2 * kls * bx).astype(jnp.bfloat16)
    r1 = lax.all_to_all(a, "pme", 0, 0, tiled=True).reshape(GY, 2 * kls * bx)
    cy, sy = dft_pair(GY)
    fy = jnp.asarray(np.concatenate([cy, sy], axis=0), jnp.bfloat16)
    y = combine(mm(fy, r1), True)
    y = y.reshape(2, n_dom, kyls, kls, bx).transpose(1, 4, 0, 2, 3)
    y = y.reshape(n_dom, bx, 2 * kyls * kls).astype(jnp.bfloat16)
    r2 = lax.all_to_all(y, "dom", 0, 0, tiled=True).reshape(GX, 2 * kyls * kls)
    cx, sx = dft_pair(GX)
    fx = jnp.asarray(np.concatenate([cx, sx], axis=0), jnp.bfloat16)
    z = combine(mm(fx, r2), True)
    kernel = green(
        wave_square(GX, 0, GX),
        wave_square(kyls, dom_index * kyls, GY),
        wave_square(kls, pme_index * kls, GZ),
    ) * (1.0 / (GX * GY * GZ))
    z = z * kernel.reshape(1, GX, kyls * kls)
    z = jnp.concatenate([z[0], z[1]], axis=1).astype(jnp.bfloat16)
    w = combine(mm(fx, z), False)
    w = w.reshape(2, n_dom, bx, kyls, kls).transpose(1, 3, 0, 2, 4)
    w = w.reshape(n_dom, kyls, 2 * bx * kls).astype(jnp.bfloat16)
    r3 = lax.all_to_all(w, "dom", 0, 0, tiled=True).reshape(GY, 2 * bx * kls)
    v = combine(mm(fy, r3), False)
    v = v.reshape(2, n_pme, by, bx, kls).transpose(1, 0, 4, 2, 3)
    v = v.reshape(n_pme, 2 * kls, by * bx).astype(jnp.bfloat16)
    r4 = lax.all_to_all(v, "pme", 0, 0, tiled=True).reshape(2 * GZ, by * bx)
    ez = np.stack([cz, -sz], axis=0).reshape(2, n_pme, kls, GZ).transpose(1, 0, 2, 3)
    ez = jnp.asarray(ez.reshape(2 * GZ, GZ).T, jnp.bfloat16)
    phi = mm(ez, r4)
    return phi.reshape(-1)


def gnn_layer(hidden, gathered, unit_w, radial_parts, w_self, w_nbr, w_rad, w_msg, w_out, gain):
    atoms, width = hidden.shape
    fanout = gathered.shape[0] // atoms
    gathered_h = gathered[:, :width].astype(jnp.bfloat16)
    r_hi, r_lo = radial_parts
    w_hi, w_lo = split2(w_rad)
    lhs = jnp.concatenate([gathered_h, r_hi, r_lo, r_hi], axis=1)
    rhs = jnp.concatenate([w_nbr, w_hi, w_hi, w_lo], axis=0)
    own_term = mm(hidden, w_self)
    pre = mm(lhs, rhs).reshape(atoms, fanout, width) + own_term[:, None, :]
    message = to_bf16_exact(silu(pre))
    sums = jnp.sum(unit_w[:, :, :, None] * message[:, :, None, :], axis=1)
    s_hi, s_lo = split2(sums.reshape(atoms * 4, width))
    mixed = (mm(s_hi, w_msg) + mm(s_lo, w_msg)).reshape(atoms, 4, width) / fanout
    total = mixed[:, 0] + jnp.sum(mixed[:, 1:] * mixed[:, 1:], axis=1)
    normed = total * lax.rsqrt(jnp.mean(total * total, axis=-1, keepdims=True) + norm_eps) * gain
    active = silu(normed).astype(jnp.bfloat16)
    update = mm(active, w_out)
    return (hidden.astype(jnp.float32) + update).astype(jnp.bfloat16)


def per_device(
    feats,
    coords,
    nbrs,
    owner,
    cell,
    w_self,
    w_nbr,
    w_rad,
    w_msg,
    w_out,
    norm_gain,
    w_charge,
    w_energy,
):
    atoms, width = feats.shape
    fanout = nbrs.shape[1]
    n_dom = lax.axis_size("dom")
    n_pme = lax.axis_size("pme")
    devices = n_dom * n_pme
    wide_rows = 3 * atoms
    pos_own = coords.T
    p_hi, p_mid, p_lo = split3(pos_own)
    wide0 = halo(jnp.concatenate([feats, p_hi, p_mid, p_lo], axis=1))
    flat_nbrs = nbrs.reshape(-1)
    onehot = (flat_nbrs[:, None] == jnp.arange(wide_rows, dtype=jnp.int32)[None, :]).astype(
        jnp.bfloat16
    )
    hidden = feats
    unit_w = None
    radial_parts = None
    for layer_idx in range(LAYERS):
        table = wide0 if layer_idx == 0 else halo(hidden)
        gathered = mm(onehot, table)
        if layer_idx == 0:
            gp = gathered[:, width:]
            pos_j = gp[:, 0:3] + gp[:, 3:6] + gp[:, 6:9]
            lift = jnp.where(flat_nbrs < atoms, -slab_depth, jnp.where(flat_nbrs >= 2 * atoms, slab_depth, 0.0))
            pos_j = pos_j.at[:, 2].add(lift)
            delta = pos_j.reshape(atoms, fanout, 3) - pos_own[:, None, :]
            dist = jnp.sqrt(jnp.sum(delta * delta, axis=-1) + 1.0)
            centres = radial_width * (jnp.arange(NB, dtype=jnp.float32) + 1.0)
            radial = jnp.exp(-jnp.square((dist[:, :, None] - centres) / radial_width))
            radial_parts = split2(radial.reshape(atoms * fanout, NB))
            unit = delta / dist[:, :, None]
            unit_w = jnp.concatenate([jnp.ones((atoms, fanout, 1), jnp.float32), unit], axis=-1)
        hidden = gnn_layer(
            hidden,
            gathered,
            unit_w,
            radial_parts,
            w_self[layer_idx],
            w_nbr[layer_idx],
            w_rad[layer_idx],
            w_msg[layer_idx],
            w_out[layer_idx],
            norm_gain[layer_idx],
        )
    flat_hidden = hidden.astype(jnp.float32)
    readout = jnp.dot(flat_hidden, jnp.stack([w_energy, w_charge], axis=1), precision=highest)
    energy_ml = readout[:, 0]
    charge = readout[:, 1]
    capacity = max(2, 2 * atoms // devices)
    dest = owner[:, 0]
    matches = (dest[:, None] == jnp.arange(devices, dtype=jnp.int32)[None, :]).astype(jnp.int32)
    slot = jnp.sum((jnp.cumsum(matches, axis=0) - matches) * matches, axis=1)
    where_to = dest * capacity + slot
    payload = jnp.stack([charge, cell.astype(jnp.float32)], axis=1)
    outgoing = jnp.zeros((devices * capacity, 2), jnp.float32).at[where_to].set(payload)
    incoming = lax.all_to_all(outgoing, AXES, 0, 0, tiled=True)
    bx = GX // n_dom
    by = GY // n_pme
    cells_here = incoming[:, 1].astype(jnp.int32)
    xl = cells_here // (by * GZ)
    yl = cells_here // GZ % by
    zz = cells_here % GZ
    index_here = (zz * by + yl) * bx + xl
    density = jnp.zeros((by * bx * GZ,), jnp.float32).at[index_here].add(incoming[:, 0])
    potential = solve_field(
        density.reshape(GZ, by * bx), n_dom, n_pme, lax.axis_index("dom"), lax.axis_index("pme")
    )
    sampled = potential[index_here]
    returned = lax.all_to_all(sampled, AXES, 0, 0, tiled=True)
    at_atoms = returned[where_to]
    energy_el = 0.5 * charge * at_atoms
    return (energy_ml, energy_el)


def solution(mesh):
    in_specs = (
        P(("dom", "pme"), None),
        P(None, ("dom", "pme")),
        P(("dom", "pme"), None),
        P(("dom", "pme"), None),
        P(("dom", "pme")),
        P(),
        P(),
        P(),
        P(),
        P(),
        P(),
        P(),
        P(),
    )
    out_specs = (P(("dom", "pme")), P(("dom", "pme")))
    return jax.shard_map(
        per_device, mesh=mesh, in_specs=in_specs, out_specs=out_specs, check_vma=False
    )
```

```python
import math

import jax
import jax.numpy as jnp
import numpy as np
from jax import lax
from jax.sharding import PartitionSpec as P

NB = 8
LAYERS = 2
GX = 256
GY = 256
GZ = 128


slab_depth = 3.0
radial_width = 0.75
ewald_beta = 1.2
norm_eps = 1e-05
highest = lax.Precision.HIGHEST
AXES = ("dom", "pme")


def to_bf16_exact(x):
    return lax.reduce_precision(x, exponent_bits=8, mantissa_bits=7)


def split2(x):
    hi = to_bf16_exact(x)
    lo = x - hi
    return hi.astype(jnp.bfloat16), lo.astype(jnp.bfloat16)


def split3(x):
    hi = to_bf16_exact(x)
    rest = x - hi
    mid = to_bf16_exact(rest)
    lo = rest - mid
    return hi.astype(jnp.bfloat16), mid.astype(jnp.bfloat16), lo.astype(jnp.bfloat16)


def halo(shard):
    devices = lax.axis_size(AXES)
    up = [(i, (i + 1) % devices) for i in range(devices)]
    down = [(j, i) for i, j in up]
    before = lax.ppermute(shard, AXES, up)
    after = lax.ppermute(shard, AXES, down)
    return jnp.concatenate([before, shard, after], axis=0)


def silu(x):
    return x * jax.nn.sigmoid(x)


def dft_pair(length):
    k = np.arange(length, dtype=np.int64)
    angle = (np.outer(k, k) % length).astype(np.float64) * (2.0 * math.pi / length)
    return np.cos(angle), np.sin(angle)


def wave_square(count, start, full):
    index = start + jnp.arange(count, dtype=jnp.int32)
    folded = jnp.where(index < full // 2, index, index - full).astype(jnp.float32)
    scaled = folded * (2.0 * math.pi / full)
    return scaled * scaled


def green(wave_x, wave_y, wave_z):
    ksq = wave_x[:, None, None] + wave_y[None, :, None] + wave_z[None, None, :]
    safe = jnp.where(ksq > 0, ksq, 1.0)
    return jnp.where(
        ksq > 0, 4.0 * math.pi * jnp.exp(-ksq / (4.0 * ewald_beta * ewald_beta)) / safe, 0.0
    )


def mm(a, b):
    return jnp.dot(a, b, preferred_element_type=jnp.float32)


def combine(p, forward):
    rows, cols = p.shape
    c, s = p[: rows // 2], p[rows // 2 :]
    c_re, c_im = c[:, : cols // 2], c[:, cols // 2 :]
    s_re, s_im = s[:, : cols // 2], s[:, cols // 2 :]
    if forward:
        return c_re + s_im, c_im - s_re
    return c_re - s_im, c_im + s_re


def regroup(parts, split, perm, shape, axis):
    moved = [x.astype(jnp.bfloat16).reshape(split).transpose(perm).reshape(shape) for x in parts]
    return jnp.concatenate(moved, axis=axis)


def solve_field(density, n_dom, n_pme, dom_index, pme_index):
    by = GY // n_pme
    bx = GX // n_dom
    kls = GZ // n_pme
    kyls = GY // n_dom
    cz, sz = dft_pair(GZ)
    fz = np.concatenate([cz, -sz], axis=0)
    fz2 = jnp.asarray(np.concatenate([fz, fz], axis=1), jnp.bfloat16)
    d_hi, d_lo = split2(density)
    a = mm(fz2, jnp.concatenate([d_hi, d_lo], axis=0))
    a = regroup(
        (a[:GZ], a[GZ:]), (n_pme, kls, by, bx), (0, 2, 1, 3), (n_pme, by, kls * bx), 2
    )
    r1 = lax.all_to_all(a, "pme", 0, 0, tiled=True).reshape(GY, 2 * kls * bx)
    cy, sy = dft_pair(GY)
    fy = jnp.asarray(np.concatenate([cy, sy], axis=0), jnp.bfloat16)
    y = regroup(
        combine(mm(fy, r1), True), (n_dom, kyls, kls, bx), (0, 3, 1, 2), (n_dom, bx, kyls * kls), 2
    )
    r2 = lax.all_to_all(y, "dom", 0, 0, tiled=True).reshape(GX, 2 * kyls * kls)
    cx, sx = dft_pair(GX)
    fx = jnp.asarray(np.concatenate([cx, sx], axis=0), jnp.bfloat16)
    z_re, z_im = combine(mm(fx, r2), True)
    kernel = green(
        wave_square(GX, 0, GX),
        wave_square(kyls, dom_index * kyls, GY),
        wave_square(kls, pme_index * kls, GZ),
    ).reshape(GX, kyls * kls) * (1.0 / (GX * GY * GZ))
    z = jnp.concatenate([z_re * kernel, z_im * kernel], axis=1).astype(jnp.bfloat16)
    w = regroup(
        combine(mm(fx, z), False), (n_dom, bx, kyls, kls), (0, 2, 1, 3), (n_dom, kyls, bx * kls), 2
    )
    r3 = lax.all_to_all(w, "dom", 0, 0, tiled=True).reshape(GY, 2 * bx * kls)
    v = regroup(
        combine(mm(fy, r3), False), (n_pme, by, bx, kls), (0, 3, 1, 2), (n_pme, kls, by * bx), 1
    )
    r4 = lax.all_to_all(v, "pme", 0, 0, tiled=True).reshape(2 * GZ, by * bx)
    ez = np.stack([cz, -sz], axis=0).reshape(2, n_pme, kls, GZ).transpose(1, 0, 2, 3)
    ez = jnp.asarray(ez.reshape(2 * GZ, GZ).T, jnp.bfloat16)
    phi = mm(ez, r4)
    return phi.reshape(-1)


def gnn_layer(hidden, gathered, unit_w, radial_parts, w_self, w_nbr, w_rad, w_msg, w_out, gain):
    atoms, width = hidden.shape
    fanout = gathered.shape[0] // atoms
    gathered_h = gathered[:, :width].astype(jnp.bfloat16)
    r_hi, r_lo = radial_parts
    w_hi, w_lo = split2(w_rad)
    lhs = jnp.concatenate([gathered_h, r_hi, r_lo, r_hi], axis=1)
    rhs = jnp.concatenate([w_nbr, w_hi, w_hi, w_lo], axis=0)
    own_term = mm(hidden, w_self)
    pre = mm(lhs, rhs).reshape(atoms, fanout, width) + own_term[:, None, :]
    message = to_bf16_exact(silu(pre))
    sums = jnp.sum(unit_w[:, :, :, None] * message[:, :, None, :], axis=1)
    s_hi, s_lo = split2(sums.reshape(atoms * 4, width))
    mixed = (mm(s_hi, w_msg) + mm(s_lo, w_msg)).reshape(atoms, 4, width) / fanout
    total = mixed[:, 0] + jnp.sum(mixed[:, 1:] * mixed[:, 1:], axis=1)
    normed = total * lax.rsqrt(jnp.mean(total * total, axis=-1, keepdims=True) + norm_eps) * gain
    active = silu(normed).astype(jnp.bfloat16)
    update = mm(active, w_out)
    return (hidden.astype(jnp.float32) + update).astype(jnp.bfloat16)


def per_device(
    feats,
    coords,
    nbrs,
    owner,
    cell,
    w_self,
    w_nbr,
    w_rad,
    w_msg,
    w_out,
    norm_gain,
    w_charge,
    w_energy,
):
    atoms, width = feats.shape
    fanout = nbrs.shape[1]
    n_dom = lax.axis_size("dom")
    n_pme = lax.axis_size("pme")
    devices = n_dom * n_pme
    wide_rows = 3 * atoms
    pos_own = coords.T
    p_hi, p_mid, p_lo = split3(pos_own)
    wide0 = halo(jnp.concatenate([feats, p_hi, p_mid, p_lo], axis=1))
    flat_nbrs = nbrs.reshape(-1)
    onehot = (flat_nbrs[:, None] == jnp.arange(wide_rows, dtype=jnp.int32)[None, :]).astype(
        jnp.bfloat16
    )
    hidden = feats
    unit_w = None
    radial_parts = None
    for layer_idx in range(LAYERS):
        table = wide0 if layer_idx == 0 else halo(hidden)
        gathered = mm(onehot, table)
        if layer_idx == 0:
            gp = gathered[:, width:]
            pos_j = gp[:, 0:3] + gp[:, 3:6] + gp[:, 6:9]
            lift = jnp.where(flat_nbrs < atoms, -slab_depth, jnp.where(flat_nbrs >= 2 * atoms, slab_depth, 0.0))
            pos_j = pos_j.at[:, 2].add(lift)
            delta = pos_j.reshape(atoms, fanout, 3) - pos_own[:, None, :]
            dist = jnp.sqrt(jnp.sum(delta * delta, axis=-1) + 1.0)
            centres = radial_width * (jnp.arange(NB, dtype=jnp.float32) + 1.0)
            radial = jnp.exp(-jnp.square((dist[:, :, None] - centres) / radial_width))
            radial_parts = split2(radial.reshape(atoms * fanout, NB))
            unit = delta / dist[:, :, None]
            unit_w = jnp.concatenate([jnp.ones((atoms, fanout, 1), jnp.float32), unit], axis=-1)
        hidden = gnn_layer(
            hidden,
            gathered,
            unit_w,
            radial_parts,
            w_self[layer_idx],
            w_nbr[layer_idx],
            w_rad[layer_idx],
            w_msg[layer_idx],
            w_out[layer_idx],
            norm_gain[layer_idx],
        )
    flat_hidden = hidden.astype(jnp.float32)
    readout = jnp.dot(flat_hidden, jnp.stack([w_energy, w_charge], axis=1), precision=highest)
    energy_ml = readout[:, 0]
    charge = readout[:, 1]
    capacity = max(2, 2 * atoms // devices)
    dest = owner[:, 0]
    matches = (dest[:, None] == jnp.arange(devices, dtype=jnp.int32)[None, :]).astype(jnp.int32)
    slot = jnp.sum((jnp.cumsum(matches, axis=0) - matches) * matches, axis=1)
    where_to = dest * capacity + slot
    payload = jnp.stack([charge, cell.astype(jnp.float32)], axis=1)
    outgoing = jnp.zeros((devices * capacity, 2), jnp.float32).at[where_to].set(payload)
    incoming = lax.all_to_all(outgoing, AXES, 0, 0, tiled=True)
    bx = GX // n_dom
    by = GY // n_pme
    cells_here = incoming[:, 1].astype(jnp.int32)
    xl = cells_here // (by * GZ)
    yl = cells_here // GZ % by
    zz = cells_here % GZ
    index_here = (zz * by + yl) * bx + xl
    density = jnp.zeros((by * bx * GZ,), jnp.float32).at[index_here].add(incoming[:, 0])
    potential = solve_field(
        density.reshape(GZ, by * bx), n_dom, n_pme, lax.axis_index("dom"), lax.axis_index("pme")
    )
    sampled = potential[index_here]
    returned = lax.all_to_all(sampled, AXES, 0, 0, tiled=True)
    at_atoms = returned[where_to]
    energy_el = 0.5 * charge * at_atoms
    return (energy_ml, energy_el)


def solution(mesh):
    in_specs = (
        P(("dom", "pme"), None),
        P(None, ("dom", "pme")),
        P(("dom", "pme"), None),
        P(("dom", "pme"), None),
        P(("dom", "pme")),
        P(),
        P(),
        P(),
        P(),
        P(),
        P(),
        P(),
        P(),
    )
    out_specs = (P(("dom", "pme")), P(("dom", "pme")))
    return jax.shard_map(
        per_device, mesh=mesh, in_specs=in_specs, out_specs=out_specs, check_vma=False
    )
```

```python
import math

import jax
import jax.numpy as jnp
import numpy as np
from jax import lax
from jax.sharding import PartitionSpec as P

NB = 8
LAYERS = 2
GX = 256
GY = 256
GZ = 128


slab_depth = 3.0
radial_width = 0.75
ewald_beta = 1.2
norm_eps = 1e-05
highest = lax.Precision.HIGHEST
AXES = ("dom", "pme")


def to_bf16_exact(x):
    return lax.reduce_precision(x, exponent_bits=8, mantissa_bits=7)


def split2(x):
    hi = to_bf16_exact(x)
    lo = x - hi
    return hi.astype(jnp.bfloat16), lo.astype(jnp.bfloat16)


def split3(x):
    hi = to_bf16_exact(x)
    rest = x - hi
    mid = to_bf16_exact(rest)
    lo = rest - mid
    return hi.astype(jnp.bfloat16), mid.astype(jnp.bfloat16), lo.astype(jnp.bfloat16)


def halo(shard):
    devices = lax.axis_size(AXES)
    up = [(i, (i + 1) % devices) for i in range(devices)]
    down = [(j, i) for i, j in up]
    before = lax.ppermute(shard, AXES, up)
    after = lax.ppermute(shard, AXES, down)
    return jnp.concatenate([before, shard, after], axis=0)


def silu(x):
    return x * jax.nn.sigmoid(x)


def dft_pair(length):
    k = np.arange(length, dtype=np.int64)
    angle = (np.outer(k, k) % length).astype(np.float64) * (2.0 * math.pi / length)
    return np.cos(angle), np.sin(angle)


def wave_square(count, start, full):
    index = start + jnp.arange(count, dtype=jnp.int32)
    folded = jnp.where(index < full // 2, index, index - full).astype(jnp.float32)
    scaled = folded * (2.0 * math.pi / full)
    return scaled * scaled


def green(wave_x, wave_y, wave_z):
    ksq = wave_x[:, None, None] + wave_y[None, :, None] + wave_z[None, None, :]
    safe = jnp.where(ksq > 0, ksq, 1.0)
    return jnp.where(
        ksq > 0, 4.0 * math.pi * jnp.exp(-ksq / (4.0 * ewald_beta * ewald_beta)) / safe, 0.0
    )


def mm(a, b):
    return jnp.dot(a, b, preferred_element_type=jnp.float32)


def combine(p, forward):
    rows, cols = p.shape
    c, s = p[: rows // 2], p[rows // 2 :]
    c_re, c_im = c[:, : cols // 2], c[:, cols // 2 :]
    s_re, s_im = s[:, : cols // 2], s[:, cols // 2 :]
    if forward:
        return c_re + s_im, c_im - s_re
    return c_re - s_im, c_im + s_re


def regroup(parts, split, perm, shape, axis):
    moved = [x.astype(jnp.bfloat16).reshape(split).transpose(perm).reshape(shape) for x in parts]
    return jnp.concatenate(moved, axis=axis)


def solve_field(density, devices, dev_index):
    xps = GX // devices
    kyls = GY // devices
    cz, sz = dft_pair(GZ)
    fa = jnp.asarray(np.concatenate([cz, -sz], axis=1), jnp.bfloat16)
    d_hi, d_lo = split2(density)
    a = mm(d_hi, fa) + mm(d_lo, fa)
    a_re = a[:, :GZ].reshape(GY, xps, GZ).astype(jnp.bfloat16)
    a_im = a[:, GZ:].reshape(GY, xps, GZ).astype(jnp.bfloat16)
    cy, sy = dft_pair(GY)
    fy = jnp.asarray(np.concatenate([cy, sy], axis=0), jnp.bfloat16)
    p = jnp.einsum("ky,ypz->kpz", fy, a_re, preferred_element_type=jnp.float32)
    q = jnp.einsum("ky,ypz->kpz", fy, a_im, preferred_element_type=jnp.float32)
    y_re = p[:GY] + q[GY:]
    y_im = q[:GY] - p[GY:]

    def by_dest(t):
        return t.reshape(devices, kyls, xps, GZ).transpose(0, 2, 1, 3)

    sent = jnp.stack([by_dest(y_re), by_dest(y_im)], axis=2).astype(jnp.bfloat16)
    r2 = lax.all_to_all(sent, AXES, 0, 0, tiled=True)
    cx, sx = dft_pair(GX)
    fx = jnp.asarray(np.concatenate([cx, sx], axis=0), jnp.bfloat16)
    p2 = jnp.einsum("kpx,pxrjz->krjz", fx.reshape(2 * GX, devices, xps), r2, preferred_element_type=jnp.float32)
    z_re = p2[:GX, 0] + p2[GX:, 1]
    z_im = p2[:GX, 1] - p2[GX:, 0]
    kernel = green(
        wave_square(GX, 0, GX), wave_square(kyls, dev_index * kyls, GY), wave_square(GZ, 0, GZ)
    ) * (1.0 / (GX * GY * GZ))
    z = jnp.stack([z_re * kernel, z_im * kernel], axis=1).astype(jnp.bfloat16)
    p3 = jnp.einsum("xk,krjz->xrjz", fx, z, preferred_element_type=jnp.float32)
    w_re = p3[:GX, 0] - p3[GX:, 1]
    w_im = p3[:GX, 1] + p3[GX:, 0]
    back = jnp.stack(
        [w_re.reshape(devices, xps, kyls, GZ), w_im.reshape(devices, xps, kyls, GZ)], axis=2
    ).astype(jnp.bfloat16)
    r3 = lax.all_to_all(back, AXES, 0, 0, tiled=True)
    r3 = r3.transpose(2, 1, 0, 3, 4).reshape(2 * xps, GY, GZ)
    p4 = jnp.einsum("yk,bkz->ybz", fy, r3, preferred_element_type=jnp.float32).reshape(2 * GY, 2, xps, GZ)
    v_re = p4[:GY, 0] - p4[GY:, 1]
    v_im = p4[:GY, 1] + p4[GY:, 0]
    ez = jnp.asarray(np.concatenate([cz, -sz], axis=0), jnp.bfloat16)
    v = jnp.concatenate([v_re, v_im], axis=-1).reshape(GY * xps, 2 * GZ).astype(jnp.bfloat16)
    phi = mm(v, ez)
    return phi.reshape(-1)


def gnn_layer(hidden, gathered, unit_w, radial_parts, w_self, w_nbr, w_rad, w_msg, w_out, gain):
    atoms, width = hidden.shape
    fanout = gathered.shape[0] // atoms
    gathered_h = gathered[:, :width].astype(jnp.bfloat16)
    r_hi, r_lo = radial_parts
    w_hi, w_lo = split2(w_rad)
    lhs = jnp.concatenate([gathered_h, r_hi, r_lo, r_hi], axis=1)
    rhs = jnp.concatenate([w_nbr, w_hi, w_hi, w_lo], axis=0)
    own_term = mm(hidden, w_self)
    pre = mm(lhs, rhs).reshape(atoms, fanout, width) + own_term[:, None, :]
    message = to_bf16_exact(silu(pre))
    sums = jnp.sum(unit_w[:, :, :, None] * message[:, :, None, :], axis=1)
    s_hi, s_lo = split2(sums.reshape(atoms * 4, width))
    mixed = (mm(s_hi, w_msg) + mm(s_lo, w_msg)).reshape(atoms, 4, width) / fanout
    total = mixed[:, 0] + jnp.sum(mixed[:, 1:] * mixed[:, 1:], axis=1)
    normed = total * lax.rsqrt(jnp.mean(total * total, axis=-1, keepdims=True) + norm_eps) * gain
    active = silu(normed).astype(jnp.bfloat16)
    update = mm(active, w_out)
    return (hidden.astype(jnp.float32) + update).astype(jnp.bfloat16)


def per_device(
    feats,
    coords,
    nbrs,
    owner,
    cell,
    w_self,
    w_nbr,
    w_rad,
    w_msg,
    w_out,
    norm_gain,
    w_charge,
    w_energy,
):
    atoms, width = feats.shape
    fanout = nbrs.shape[1]
    n_dom = lax.axis_size("dom")
    n_pme = lax.axis_size("pme")
    devices = n_dom * n_pme
    wide_rows = 3 * atoms
    pos_own = coords.T
    p_hi, p_mid, p_lo = split3(pos_own)
    wide0 = halo(jnp.concatenate([feats, p_hi, p_mid, p_lo], axis=1))
    flat_nbrs = nbrs.reshape(-1)
    onehot = (flat_nbrs[:, None] == jnp.arange(wide_rows, dtype=jnp.int32)[None, :]).astype(
        jnp.bfloat16
    )
    hidden = feats
    unit_w = None
    radial_parts = None
    for layer_idx in range(LAYERS):
        table = wide0 if layer_idx == 0 else halo(hidden)
        gathered = mm(onehot, table)
        if layer_idx == 0:
            gp = gathered[:, width:]
            pos_j = gp[:, 0:3] + gp[:, 3:6] + gp[:, 6:9]
            lift = jnp.where(flat_nbrs < atoms, -slab_depth, jnp.where(flat_nbrs >= 2 * atoms, slab_depth, 0.0))
            pos_j = pos_j.at[:, 2].add(lift)
            delta = pos_j.reshape(atoms, fanout, 3) - pos_own[:, None, :]
            dist = jnp.sqrt(jnp.sum(delta * delta, axis=-1) + 1.0)
            centres = radial_width * (jnp.arange(NB, dtype=jnp.float32) + 1.0)
            radial = jnp.exp(-jnp.square((dist[:, :, None] - centres) / radial_width))
            radial_parts = split2(radial.reshape(atoms * fanout, NB))
            unit = delta / dist[:, :, None]
            unit_w = jnp.concatenate([jnp.ones((atoms, fanout, 1), jnp.float32), unit], axis=-1)
        hidden = gnn_layer(
            hidden,
            gathered,
            unit_w,
            radial_parts,
            w_self[layer_idx],
            w_nbr[layer_idx],
            w_rad[layer_idx],
            w_msg[layer_idx],
            w_out[layer_idx],
            norm_gain[layer_idx],
        )
    flat_hidden = hidden.astype(jnp.float32)
    readout = jnp.dot(flat_hidden, jnp.stack([w_energy, w_charge], axis=1), precision=highest)
    energy_ml = readout[:, 0]
    charge = readout[:, 1]
    capacity = max(2, 2 * atoms // devices) * n_pme
    bx = GX // n_dom
    by = GY // n_pme
    xps = GX // devices
    dest_owner = owner[:, 0]
    grid_x = dest_owner // n_pme * bx + cell // (by * GZ)
    grid_y = dest_owner % n_pme * by + cell // GZ % by
    grid_z = cell % GZ
    dest = grid_x // xps
    slab_cell = (grid_y * xps + grid_x % xps) * GZ + grid_z
    matches = (dest[:, None] == jnp.arange(devices, dtype=jnp.int32)[None, :]).astype(jnp.int32)
    slot = jnp.sum((jnp.cumsum(matches, axis=0) - matches) * matches, axis=1)
    where_to = dest * capacity + slot
    payload = jnp.stack([charge, slab_cell.astype(jnp.float32)], axis=1)
    outgoing = jnp.zeros((devices * capacity, 2), jnp.float32).at[where_to].set(payload)
    incoming = lax.all_to_all(outgoing, AXES, 0, 0, tiled=True)
    cells_here = incoming[:, 1].astype(jnp.int32)
    density = jnp.zeros((GY * xps * GZ,), jnp.float32).at[cells_here].add(incoming[:, 0])
    dev_index = lax.axis_index("dom") * n_pme + lax.axis_index("pme")
    potential = solve_field(density.reshape(GY * xps, GZ), devices, dev_index)
    sampled = potential[cells_here]
    returned = lax.all_to_all(sampled, AXES, 0, 0, tiled=True)
    at_atoms = returned[where_to]
    energy_el = 0.5 * charge * at_atoms
    return (energy_ml, energy_el)


def solution(mesh):
    in_specs = (
        P(("dom", "pme"), None),
        P(None, ("dom", "pme")),
        P(("dom", "pme"), None),
        P(("dom", "pme"), None),
        P(("dom", "pme")),
        P(),
        P(),
        P(),
        P(),
        P(),
        P(),
        P(),
        P(),
    )
    out_specs = (P(("dom", "pme")), P(("dom", "pme")))
    return jax.shard_map(
        per_device, mesh=mesh, in_specs=in_specs, out_specs=out_specs, check_vma=False
    )
```

```python
import math

import jax
import jax.numpy as jnp
import numpy as np
from jax import lax
from jax.sharding import PartitionSpec as P

NB = 8
LAYERS = 2
GX = 256
GY = 256
GZ = 128


slab_depth = 3.0
radial_width = 0.75
ewald_beta = 1.2
norm_eps = 1e-05
highest = lax.Precision.HIGHEST
AXES = ("dom", "pme")


def to_bf16_exact(x):
    return lax.reduce_precision(x, exponent_bits=8, mantissa_bits=7)


def split2(x):
    hi = to_bf16_exact(x)
    lo = x - hi
    return hi.astype(jnp.bfloat16), lo.astype(jnp.bfloat16)


def split3(x):
    hi = to_bf16_exact(x)
    rest = x - hi
    mid = to_bf16_exact(rest)
    lo = rest - mid
    return hi.astype(jnp.bfloat16), mid.astype(jnp.bfloat16), lo.astype(jnp.bfloat16)


def halo(shard):
    devices = lax.axis_size(AXES)
    up = [(i, (i + 1) % devices) for i in range(devices)]
    down = [(j, i) for i, j in up]
    before = lax.ppermute(shard, AXES, up)
    after = lax.ppermute(shard, AXES, down)
    return jnp.concatenate([before, shard, after], axis=0)


def silu(x):
    return x * jax.nn.sigmoid(x)


def dft_pair(length):
    k = np.arange(length, dtype=np.int64)
    angle = (np.outer(k, k) % length).astype(np.float64) * (2.0 * math.pi / length)
    return np.cos(angle), np.sin(angle)


def wave_square(count, start, full):
    index = start + jnp.arange(count, dtype=jnp.int32)
    folded = jnp.where(index < full // 2, index, index - full).astype(jnp.float32)
    scaled = folded * (2.0 * math.pi / full)
    return scaled * scaled


def green(wave_x, wave_y, wave_z):
    ksq = wave_x[:, None, None] + wave_y[None, :, None] + wave_z[None, None, :]
    safe = jnp.where(ksq > 0, ksq, 1.0)
    return jnp.where(
        ksq > 0, 4.0 * math.pi * jnp.exp(-ksq / (4.0 * ewald_beta * ewald_beta)) / safe, 0.0
    )


def mm(a, b):
    return jnp.dot(a, b, preferred_element_type=jnp.float32)


def combine(p, forward):
    rows, cols = p.shape
    c, s = p[: rows // 2], p[rows // 2 :]
    c_re, c_im = c[:, : cols // 2], c[:, cols // 2 :]
    s_re, s_im = s[:, : cols // 2], s[:, cols // 2 :]
    if forward:
        return c_re + s_im, c_im - s_re
    return c_re - s_im, c_im + s_re


def regroup(parts, split, perm, shape, axis):
    moved = [x.astype(jnp.bfloat16).reshape(split).transpose(perm).reshape(shape) for x in parts]
    return jnp.concatenate(moved, axis=axis)


def solve_field(density, devices, dev_index):
    xps = GX // devices
    kyls = GY // devices
    cz, sz = dft_pair(GZ)
    fa = jnp.asarray(np.concatenate([cz, -sz], axis=1), jnp.bfloat16)
    d_hi, d_lo = split2(density)
    a = mm(d_hi, fa) + mm(d_lo, fa)
    a_re = a[:, :GZ].reshape(GY, xps, GZ).astype(jnp.bfloat16)
    a_im = a[:, GZ:].reshape(GY, xps, GZ).astype(jnp.bfloat16)
    cy, sy = dft_pair(GY)
    fy = jnp.asarray(np.concatenate([cy, sy], axis=0), jnp.bfloat16)
    p = jnp.einsum("ky,ypz->kpz", fy, a_re, preferred_element_type=jnp.float32)
    q = jnp.einsum("ky,ypz->kpz", fy, a_im, preferred_element_type=jnp.float32)
    y_re = p[:GY] + q[GY:]
    y_im = q[:GY] - p[GY:]

    def by_dest(t):
        return t.reshape(devices, kyls, xps, GZ).transpose(0, 2, 1, 3)

    sent = jnp.stack([by_dest(y_re), by_dest(y_im)], axis=2).astype(jnp.bfloat16)
    r2 = lax.all_to_all(sent, AXES, 0, 0, tiled=True)
    cx, sx = dft_pair(GX)
    fx = jnp.asarray(np.concatenate([cx, sx], axis=0), jnp.bfloat16)
    p2 = jnp.einsum("kpx,pxrjz->krjz", fx.reshape(2 * GX, devices, xps), r2, preferred_element_type=jnp.float32)
    z_re = p2[:GX, 0] + p2[GX:, 1]
    z_im = p2[:GX, 1] - p2[GX:, 0]
    kernel = green(
        wave_square(GX, 0, GX), wave_square(kyls, dev_index * kyls, GY), wave_square(GZ, 0, GZ)
    ) * (1.0 / (GX * GY * GZ))
    z = jnp.stack([z_re * kernel, z_im * kernel], axis=1).astype(jnp.bfloat16)
    p3 = jnp.einsum("xk,krjz->xrjz", fx, z, preferred_element_type=jnp.float32)
    w_re = p3[:GX, 0] - p3[GX:, 1]
    w_im = p3[:GX, 1] + p3[GX:, 0]
    back = jnp.stack(
        [w_re.reshape(devices, xps, kyls, GZ), w_im.reshape(devices, xps, kyls, GZ)], axis=2
    ).astype(jnp.bfloat16)
    r3 = lax.all_to_all(back, AXES, 0, 0, tiled=True)
    r3 = r3.transpose(2, 1, 0, 3, 4).reshape(2 * xps, GY, GZ)
    p4 = jnp.einsum("yk,bkz->ybz", fy, r3, preferred_element_type=jnp.float32).reshape(2 * GY, 2, xps, GZ)
    v_re = p4[:GY, 0] - p4[GY:, 1]
    v_im = p4[:GY, 1] + p4[GY:, 0]
    return jnp.concatenate([v_re, v_im], axis=-1).reshape(GY * xps, 2 * GZ).astype(jnp.bfloat16)


def gnn_layer(hidden, gathered, unit_w, radial_parts, w_self, w_nbr, w_rad, w_msg, w_out, gain):
    atoms, width = hidden.shape
    fanout = gathered.shape[0] // atoms
    gathered_h = gathered[:, :width].astype(jnp.bfloat16)
    r_hi, r_lo = radial_parts
    w_hi, w_lo = split2(w_rad)
    lhs = jnp.concatenate([gathered_h, r_hi, r_lo, r_hi], axis=1)
    rhs = jnp.concatenate([w_nbr, w_hi, w_hi, w_lo], axis=0)
    own_term = mm(hidden, w_self)
    pre = mm(lhs, rhs).reshape(atoms, fanout, width) + own_term[:, None, :]
    message = to_bf16_exact(silu(pre))
    sums = jnp.sum(unit_w[:, :, :, None] * message[:, :, None, :], axis=1)
    s_hi, s_lo = split2(sums.reshape(atoms * 4, width))
    mixed = (mm(s_hi, w_msg) + mm(s_lo, w_msg)).reshape(atoms, 4, width) / fanout
    total = mixed[:, 0] + jnp.sum(mixed[:, 1:] * mixed[:, 1:], axis=1)
    normed = total * lax.rsqrt(jnp.mean(total * total, axis=-1, keepdims=True) + norm_eps) * gain
    active = silu(normed).astype(jnp.bfloat16)
    update = mm(active, w_out)
    return (hidden.astype(jnp.float32) + update).astype(jnp.bfloat16)


def per_device(
    feats,
    coords,
    nbrs,
    owner,
    cell,
    w_self,
    w_nbr,
    w_rad,
    w_msg,
    w_out,
    norm_gain,
    w_charge,
    w_energy,
):
    atoms, width = feats.shape
    fanout = nbrs.shape[1]
    n_dom = lax.axis_size("dom")
    n_pme = lax.axis_size("pme")
    devices = n_dom * n_pme
    wide_rows = 3 * atoms
    pos_own = coords.T
    p_hi, p_mid, p_lo = split3(pos_own)
    wide0 = halo(jnp.concatenate([feats, p_hi, p_mid, p_lo], axis=1))
    flat_nbrs = nbrs.reshape(-1)
    onehot = (flat_nbrs[:, None] == jnp.arange(wide_rows, dtype=jnp.int32)[None, :]).astype(
        jnp.bfloat16
    )
    hidden = feats
    unit_w = None
    radial_parts = None
    for layer_idx in range(LAYERS):
        table = wide0 if layer_idx == 0 else halo(hidden)
        gathered = mm(onehot, table)
        if layer_idx == 0:
            gp = gathered[:, width:]
            pos_j = gp[:, 0:3] + gp[:, 3:6] + gp[:, 6:9]
            lift = jnp.where(flat_nbrs < atoms, -slab_depth, jnp.where(flat_nbrs >= 2 * atoms, slab_depth, 0.0))
            pos_j = pos_j.at[:, 2].add(lift)
            delta = pos_j.reshape(atoms, fanout, 3) - pos_own[:, None, :]
            dist = jnp.sqrt(jnp.sum(delta * delta, axis=-1) + 1.0)
            centres = radial_width * (jnp.arange(NB, dtype=jnp.float32) + 1.0)
            radial = jnp.exp(-jnp.square((dist[:, :, None] - centres) / radial_width))
            radial_parts = split2(radial.reshape(atoms * fanout, NB))
            unit = delta / dist[:, :, None]
            unit_w = jnp.concatenate([jnp.ones((atoms, fanout, 1), jnp.float32), unit], axis=-1)
        hidden = gnn_layer(
            hidden,
            gathered,
            unit_w,
            radial_parts,
            w_self[layer_idx],
            w_nbr[layer_idx],
            w_rad[layer_idx],
            w_msg[layer_idx],
            w_out[layer_idx],
            norm_gain[layer_idx],
        )
    flat_hidden = hidden.astype(jnp.float32)
    readout = jnp.dot(flat_hidden, jnp.stack([w_energy, w_charge], axis=1), precision=highest)
    energy_ml = readout[:, 0]
    charge = readout[:, 1]
    capacity = max(2, 2 * atoms // devices) * n_pme
    bx = GX // n_dom
    by = GY // n_pme
    xps = GX // devices
    dest_owner = owner[:, 0]
    grid_x = dest_owner // n_pme * bx + cell // (by * GZ)
    grid_y = dest_owner % n_pme * by + cell // GZ % by
    grid_z = cell % GZ
    dest = grid_x // xps
    slab_cell = (grid_y * xps + grid_x % xps) * GZ + grid_z
    matches = (dest[:, None] == jnp.arange(devices, dtype=jnp.int32)[None, :]).astype(jnp.int32)
    slot = jnp.sum((jnp.cumsum(matches, axis=0) - matches) * matches, axis=1)
    where_to = dest * capacity + slot
    payload = jnp.stack([charge, slab_cell.astype(jnp.float32)], axis=1)
    outgoing = jnp.zeros((devices * capacity, 2), jnp.float32).at[where_to].set(payload)
    incoming = lax.all_to_all(outgoing, AXES, 0, 0, tiled=True)
    cells_here = incoming[:, 1].astype(jnp.int32)
    rows_here = cells_here // GZ
    z_here = cells_here % GZ
    n_rows = GY * xps
    oh_rows = (jnp.arange(n_rows, dtype=jnp.int32)[:, None] == rows_here[None, :]).astype(jnp.bfloat16)
    oh_z = z_here[:, None] == jnp.arange(GZ, dtype=jnp.int32)[None, :]
    q_hi, q_lo = split2(incoming[:, 0])
    zero = jnp.zeros((), jnp.bfloat16)
    qz = jnp.concatenate(
        [jnp.where(oh_z, q_hi[:, None], zero), jnp.where(oh_z, q_lo[:, None], zero)], axis=1
    )
    dparts = mm(oh_rows, qz)
    density = dparts[:, :GZ] + dparts[:, GZ:]
    dev_index = lax.axis_index("dom") * n_pme + lax.axis_index("pme")
    spectrum_rows = solve_field(density, devices, dev_index)
    picked = lax.dot_general(
        oh_rows, spectrum_rows, (((0,), (0,)), ((), ())), preferred_element_type=jnp.float32
    )
    cz, sz = dft_pair(GZ)
    ez_t = jnp.asarray(np.concatenate([cz, -sz], axis=1), jnp.bfloat16)
    ez_rows = mm(oh_z.astype(jnp.bfloat16), ez_t)
    sampled = jnp.sum(picked * ez_rows, axis=1)
    returned = lax.all_to_all(sampled, AXES, 0, 0, tiled=True)
    at_atoms = returned[where_to]
    energy_el = 0.5 * charge * at_atoms
    return (energy_ml, energy_el)


def solution(mesh):
    in_specs = (
        P(("dom", "pme"), None),
        P(None, ("dom", "pme")),
        P(("dom", "pme"), None),
        P(("dom", "pme"), None),
        P(("dom", "pme")),
        P(),
        P(),
        P(),
        P(),
        P(),
        P(),
        P(),
        P(),
    )
    out_specs = (P(("dom", "pme")), P(("dom", "pme")))
    return jax.shard_map(
        per_device, mesh=mesh, in_specs=in_specs, out_specs=out_specs, check_vma=False
    )
```

```python
import math

import jax
import jax.numpy as jnp
import numpy as np
from jax import lax
from jax.sharding import PartitionSpec as P

NB = 8
LAYERS = 2
GX = 256
GY = 256
GZ = 128


slab_depth = 3.0
radial_width = 0.75
ewald_beta = 1.2
norm_eps = 1e-05
highest = lax.Precision.HIGHEST
AXES = ("dom", "pme")


def to_bf16_exact(x):
    return lax.reduce_precision(x, exponent_bits=8, mantissa_bits=7)


def split2(x):
    hi = to_bf16_exact(x)
    lo = x - hi
    return hi.astype(jnp.bfloat16), lo.astype(jnp.bfloat16)


def split3(x):
    hi = to_bf16_exact(x)
    rest = x - hi
    mid = to_bf16_exact(rest)
    lo = rest - mid
    return hi.astype(jnp.bfloat16), mid.astype(jnp.bfloat16), lo.astype(jnp.bfloat16)


def halo(shard):
    devices = lax.axis_size(AXES)
    up = [(i, (i + 1) % devices) for i in range(devices)]
    down = [(j, i) for i, j in up]
    before = lax.ppermute(shard, AXES, up)
    after = lax.ppermute(shard, AXES, down)
    return jnp.concatenate([before, shard, after], axis=0)


def silu(x):
    return x * jax.nn.sigmoid(x)


def dft_pair(length):
    k = np.arange(length, dtype=np.int64)
    angle = (np.outer(k, k) % length).astype(np.float64) * (2.0 * math.pi / length)
    return np.cos(angle), np.sin(angle)


def wave_square(count, start, full):
    index = start + jnp.arange(count, dtype=jnp.int32)
    folded = jnp.where(index < full // 2, index, index - full).astype(jnp.float32)
    scaled = folded * (2.0 * math.pi / full)
    return scaled * scaled


def green(wave_x, wave_y, wave_z):
    ksq = wave_x[:, None, None] + wave_y[None, :, None] + wave_z[None, None, :]
    safe = jnp.where(ksq > 0, ksq, 1.0)
    return jnp.where(
        ksq > 0, 4.0 * math.pi * jnp.exp(-ksq / (4.0 * ewald_beta * ewald_beta)) / safe, 0.0
    )


def mm(a, b):
    return jnp.dot(a, b, preferred_element_type=jnp.float32)


def combine(p, forward):
    rows, cols = p.shape
    c, s = p[: rows // 2], p[rows // 2 :]
    c_re, c_im = c[:, : cols // 2], c[:, cols // 2 :]
    s_re, s_im = s[:, : cols // 2], s[:, cols // 2 :]
    if forward:
        return c_re + s_im, c_im - s_re
    return c_re - s_im, c_im + s_re


def regroup(parts, split, perm, shape, axis):
    moved = [x.astype(jnp.bfloat16).reshape(split).transpose(perm).reshape(shape) for x in parts]
    return jnp.concatenate(moved, axis=axis)


def solve_field(density, devices, dev_index):
    xps = GX // devices
    kyls = GY // devices
    cz, sz = dft_pair(GZ)
    fa = jnp.asarray(np.concatenate([cz, -sz], axis=1), jnp.bfloat16)
    d_hi, d_lo = split2(density)
    a = mm(d_hi, fa) + mm(d_lo, fa)
    a_re = a[:, :GZ].reshape(GY, xps, GZ).astype(jnp.bfloat16)
    a_im = a[:, GZ:].reshape(GY, xps, GZ).astype(jnp.bfloat16)
    cy, sy = dft_pair(GY)
    fy = jnp.asarray(np.concatenate([cy, sy], axis=0), jnp.bfloat16)
    p = jnp.einsum("ky,ypz->kpz", fy, a_re, preferred_element_type=jnp.float32)
    q = jnp.einsum("ky,ypz->kpz", fy, a_im, preferred_element_type=jnp.float32)
    y_re = p[:GY] + q[GY:]
    y_im = q[:GY] - p[GY:]

    def by_dest(t):
        return t.reshape(devices, kyls, xps, GZ).transpose(0, 2, 1, 3)

    sent = jnp.stack([by_dest(y_re), by_dest(y_im)], axis=2).astype(jnp.bfloat16)
    r2 = lax.all_to_all(sent, AXES, 0, 0, tiled=True)
    cx, sx = dft_pair(GX)
    fx = jnp.asarray(np.concatenate([cx, sx], axis=0), jnp.bfloat16)
    p2 = jnp.einsum("kpx,pxrjz->krjz", fx.reshape(2 * GX, devices, xps), r2, preferred_element_type=jnp.float32)
    z_re = p2[:GX, 0] + p2[GX:, 1]
    z_im = p2[:GX, 1] - p2[GX:, 0]
    kernel = green(
        wave_square(GX, 0, GX), wave_square(kyls, dev_index * kyls, GY), wave_square(GZ, 0, GZ)
    ) * (1.0 / (GX * GY * GZ))
    z = jnp.stack([z_re * kernel, z_im * kernel], axis=1).astype(jnp.bfloat16)
    p3 = jnp.einsum("xk,krjz->xrjz", fx, z, preferred_element_type=jnp.float32)
    w_re = p3[:GX, 0] - p3[GX:, 1]
    w_im = p3[:GX, 1] + p3[GX:, 0]
    back = jnp.stack(
        [w_re.reshape(devices, xps, kyls, GZ), w_im.reshape(devices, xps, kyls, GZ)], axis=2
    ).astype(jnp.bfloat16)
    r3 = lax.all_to_all(back, AXES, 0, 0, tiled=True)
    r3 = r3.transpose(2, 1, 0, 3, 4).reshape(2 * xps, GY, GZ)
    p4 = jnp.einsum("yk,bkz->ybz", fy, r3, preferred_element_type=jnp.float32).reshape(2 * GY, 2, xps, GZ)
    v_re = p4[:GY, 0] - p4[GY:, 1]
    v_im = p4[:GY, 1] + p4[GY:, 0]
    return jnp.concatenate([v_re, v_im], axis=-1).reshape(GY * xps, 2 * GZ).astype(jnp.bfloat16)


def gnn_layer(hidden, gathered, unit_w, radial_parts, w_self, w_nbr, w_rad, w_msg, w_out, gain):
    atoms, width = hidden.shape
    fanout = gathered.shape[0] // atoms
    gathered_h = gathered[:, :width].astype(jnp.bfloat16)
    r_hi, r_lo = radial_parts
    w_hi, w_lo = split2(w_rad)
    lhs = jnp.concatenate([gathered_h, r_hi, r_lo, r_hi], axis=1)
    rhs = jnp.concatenate([w_nbr, w_hi, w_hi, w_lo], axis=0)
    own_term = mm(hidden, w_self)
    pre = mm(lhs, rhs).reshape(atoms, fanout, width) + own_term[:, None, :]
    message = silu(pre).astype(jnp.bfloat16)
    parts = jnp.einsum("akc,akf->acf", unit_w, message, preferred_element_type=jnp.float32)
    sums = jnp.concatenate([parts[:, :1], parts[:, 1:4] + parts[:, 4:7]], axis=1)
    s_hi, s_lo = split2(sums.reshape(atoms * 4, width))
    mixed = (mm(s_hi, w_msg) + mm(s_lo, w_msg)).reshape(atoms, 4, width) / fanout
    total = mixed[:, 0] + jnp.sum(mixed[:, 1:] * mixed[:, 1:], axis=1)
    normed = total * lax.rsqrt(jnp.mean(total * total, axis=-1, keepdims=True) + norm_eps) * gain
    active = silu(normed).astype(jnp.bfloat16)
    update = mm(active, w_out)
    return (hidden.astype(jnp.float32) + update).astype(jnp.bfloat16)


def per_device(
    feats,
    coords,
    nbrs,
    owner,
    cell,
    w_self,
    w_nbr,
    w_rad,
    w_msg,
    w_out,
    norm_gain,
    w_charge,
    w_energy,
):
    atoms, width = feats.shape
    fanout = nbrs.shape[1]
    n_dom = lax.axis_size("dom")
    n_pme = lax.axis_size("pme")
    devices = n_dom * n_pme
    wide_rows = 3 * atoms
    pos_own = coords.T
    p_hi, p_mid, p_lo = split3(pos_own)
    wide0 = halo(jnp.concatenate([feats, p_hi, p_mid, p_lo], axis=1))
    flat_nbrs = nbrs.reshape(-1)
    onehot = (flat_nbrs[:, None] == jnp.arange(wide_rows, dtype=jnp.int32)[None, :]).astype(
        jnp.bfloat16
    )
    hidden = feats
    unit_w = None
    radial_parts = None
    for layer_idx in range(LAYERS):
        table = wide0 if layer_idx == 0 else halo(hidden)
        gathered = mm(onehot, table)
        if layer_idx == 0:
            gp = gathered[:, width:]
            pos_j = gp[:, 0:3] + gp[:, 3:6] + gp[:, 6:9]
            lift = jnp.where(flat_nbrs < atoms, -slab_depth, jnp.where(flat_nbrs >= 2 * atoms, slab_depth, 0.0))
            pos_j = pos_j.at[:, 2].add(lift)
            delta = pos_j.reshape(atoms, fanout, 3) - pos_own[:, None, :]
            dist = jnp.sqrt(jnp.sum(delta * delta, axis=-1) + 1.0)
            centres = radial_width * (jnp.arange(NB, dtype=jnp.float32) + 1.0)
            radial = jnp.exp(-jnp.square((dist[:, :, None] - centres) / radial_width))
            radial_parts = split2(radial.reshape(atoms * fanout, NB))
            unit = delta / dist[:, :, None]
            u_hi, u_lo = split2(unit)
            unit_w = jnp.concatenate(
                [jnp.ones((atoms, fanout, 1), jnp.bfloat16), u_hi, u_lo, jnp.zeros((atoms, fanout, 1), jnp.bfloat16)],
                axis=-1,
            )
        hidden = gnn_layer(
            hidden,
            gathered,
            unit_w,
            radial_parts,
            w_self[layer_idx],
            w_nbr[layer_idx],
            w_rad[layer_idx],
            w_msg[layer_idx],
            w_out[layer_idx],
            norm_gain[layer_idx],
        )
    flat_hidden = hidden.astype(jnp.float32)
    readout = jnp.dot(flat_hidden, jnp.stack([w_energy, w_charge], axis=1), precision=highest)
    energy_ml = readout[:, 0]
    charge = readout[:, 1]
    capacity = max(2, 2 * atoms // devices) * n_pme
    bx = GX // n_dom
    by = GY // n_pme
    xps = GX // devices
    dest_owner = owner[:, 0]
    grid_x = dest_owner // n_pme * bx + cell // (by * GZ)
    grid_y = dest_owner % n_pme * by + cell // GZ % by
    grid_z = cell % GZ
    dest = grid_x // xps
    slab_cell = (grid_y * xps + grid_x % xps) * GZ + grid_z
    matches = (dest[:, None] == jnp.arange(devices, dtype=jnp.int32)[None, :]).astype(jnp.int32)
    slot = jnp.sum((jnp.cumsum(matches, axis=0) - matches) * matches, axis=1)
    where_to = dest * capacity + slot
    payload = jnp.stack([charge, slab_cell.astype(jnp.float32)], axis=1)
    outgoing = jnp.zeros((devices * capacity, 2), jnp.float32).at[where_to].set(payload)
    incoming = lax.all_to_all(outgoing, AXES, 0, 0, tiled=True)
    cells_here = incoming[:, 1].astype(jnp.int32)
    rows_here = cells_here // GZ
    z_here = cells_here % GZ
    n_rows = GY * xps
    oh_rows = (jnp.arange(n_rows, dtype=jnp.int32)[:, None] == rows_here[None, :]).astype(jnp.bfloat16)
    oh_z = z_here[:, None] == jnp.arange(GZ, dtype=jnp.int32)[None, :]
    q_hi, q_lo = split2(incoming[:, 0])
    zero = jnp.zeros((), jnp.bfloat16)
    qz = jnp.concatenate(
        [jnp.where(oh_z, q_hi[:, None], zero), jnp.where(oh_z, q_lo[:, None], zero)], axis=1
    )
    dparts = mm(oh_rows, qz)
    density = dparts[:, :GZ] + dparts[:, GZ:]
    dev_index = lax.axis_index("dom") * n_pme + lax.axis_index("pme")
    spectrum_rows = solve_field(density, devices, dev_index)
    picked = lax.dot_general(
        oh_rows, spectrum_rows, (((0,), (0,)), ((), ())), preferred_element_type=jnp.float32
    )
    cz, sz = dft_pair(GZ)
    ez_t = jnp.asarray(np.concatenate([cz, -sz], axis=1), jnp.bfloat16)
    ez_rows = mm(oh_z.astype(jnp.bfloat16), ez_t)
    sampled = jnp.sum(picked * ez_rows, axis=1)
    returned = lax.all_to_all(sampled, AXES, 0, 0, tiled=True)
    at_atoms = returned[where_to]
    energy_el = 0.5 * charge * at_atoms
    return (energy_ml, energy_el)


def solution(mesh):
    in_specs = (
        P(("dom", "pme"), None),
        P(None, ("dom", "pme")),
        P(("dom", "pme"), None),
        P(("dom", "pme"), None),
        P(("dom", "pme")),
        P(),
        P(),
        P(),
        P(),
        P(),
        P(),
        P(),
        P(),
    )
    out_specs = (P(("dom", "pme")), P(("dom", "pme")))
    return jax.shard_map(
        per_device, mesh=mesh, in_specs=in_specs, out_specs=out_specs, check_vma=False
    )
```

```python
import math

import jax
import jax.numpy as jnp
import numpy as np
from jax import lax
from jax.sharding import PartitionSpec as P

NB = 8
LAYERS = 2
GX = 256
GY = 256
GZ = 128


slab_depth = 3.0
radial_width = 0.75
ewald_beta = 1.2
norm_eps = 1e-05
highest = lax.Precision.HIGHEST
AXES = ("dom", "pme")


def to_bf16_exact(x):
    return lax.reduce_precision(x, exponent_bits=8, mantissa_bits=7)


def split2(x):
    hi = to_bf16_exact(x)
    lo = x - hi
    return hi.astype(jnp.bfloat16), lo.astype(jnp.bfloat16)


def split3(x):
    hi = to_bf16_exact(x)
    rest = x - hi
    mid = to_bf16_exact(rest)
    lo = rest - mid
    return hi.astype(jnp.bfloat16), mid.astype(jnp.bfloat16), lo.astype(jnp.bfloat16)


def halo_parts(shard):
    devices = lax.axis_size(AXES)
    up = [(i, (i + 1) % devices) for i in range(devices)]
    down = [(j, i) for i, j in up]
    return lax.ppermute(shard, AXES, up), lax.ppermute(shard, AXES, down)


def silu(x):
    return x * jax.nn.sigmoid(x)


def dft_pair(length):
    k = np.arange(length, dtype=np.int64)
    angle = (np.outer(k, k) % length).astype(np.float64) * (2.0 * math.pi / length)
    return np.cos(angle), np.sin(angle)


def wave_square(count, start, full):
    index = start + jnp.arange(count, dtype=jnp.int32)
    folded = jnp.where(index < full // 2, index, index - full).astype(jnp.float32)
    scaled = folded * (2.0 * math.pi / full)
    return scaled * scaled


def green(wave_x, wave_y, wave_z):
    ksq = wave_x[:, None, None] + wave_y[None, :, None] + wave_z[None, None, :]
    safe = jnp.where(ksq > 0, ksq, 1.0)
    return jnp.where(
        ksq > 0, 4.0 * math.pi * jnp.exp(-ksq / (4.0 * ewald_beta * ewald_beta)) / safe, 0.0
    )


def mm(a, b):
    return jnp.dot(a, b, preferred_element_type=jnp.float32)


def combine(p, forward):
    rows, cols = p.shape
    c, s = p[: rows // 2], p[rows // 2 :]
    c_re, c_im = c[:, : cols // 2], c[:, cols // 2 :]
    s_re, s_im = s[:, : cols // 2], s[:, cols // 2 :]
    if forward:
        return c_re + s_im, c_im - s_re
    return c_re - s_im, c_im + s_re


def regroup(parts, split, perm, shape, axis):
    moved = [x.astype(jnp.bfloat16).reshape(split).transpose(perm).reshape(shape) for x in parts]
    return jnp.concatenate(moved, axis=axis)


def solve_field(density, devices, dev_index):
    xps = GX // devices
    kyls = GY // devices
    cz, sz = dft_pair(GZ)
    fa = jnp.asarray(np.concatenate([cz, -sz], axis=1), jnp.bfloat16)
    d_hi, d_lo = split2(density)
    a = mm(d_hi, fa) + mm(d_lo, fa)
    a_re = a[:, :GZ].reshape(GY, xps, GZ).astype(jnp.bfloat16)
    a_im = a[:, GZ:].reshape(GY, xps, GZ).astype(jnp.bfloat16)
    cy, sy = dft_pair(GY)
    fy = jnp.asarray(np.concatenate([cy, sy], axis=0), jnp.bfloat16)
    p = jnp.einsum("ky,ypz->kpz", fy, a_re, preferred_element_type=jnp.float32)
    q = jnp.einsum("ky,ypz->kpz", fy, a_im, preferred_element_type=jnp.float32)
    y_re = p[:GY] + q[GY:]
    y_im = q[:GY] - p[GY:]

    def by_dest(t):
        return t.reshape(devices, kyls, xps, GZ).transpose(0, 2, 1, 3)

    sent = jnp.stack([by_dest(y_re), by_dest(y_im)], axis=2).astype(jnp.bfloat16)
    r2 = lax.all_to_all(sent, AXES, 0, 0, tiled=True)
    cx, sx = dft_pair(GX)
    fx = fy if GX == GY else jnp.asarray(np.concatenate([cx, sx], axis=0), jnp.bfloat16)
    p2 = jnp.einsum("kpx,pxrjz->krjz", fx.reshape(2 * GX, devices, xps), r2, preferred_element_type=jnp.float32)
    z_re = p2[:GX, 0] + p2[GX:, 1]
    z_im = p2[:GX, 1] - p2[GX:, 0]
    kernel = green(
        wave_square(GX, 0, GX), wave_square(kyls, dev_index * kyls, GY), wave_square(GZ, 0, GZ)
    ) * (1.0 / (GX * GY * GZ))
    z = jnp.stack([z_re * kernel, z_im * kernel], axis=1).astype(jnp.bfloat16)
    p3 = jnp.einsum("xk,krjz->xrjz", fx, z, preferred_element_type=jnp.float32)
    w_re = p3[:GX, 0] - p3[GX:, 1]
    w_im = p3[:GX, 1] + p3[GX:, 0]
    back = jnp.stack(
        [w_re.reshape(devices, xps, kyls, GZ), w_im.reshape(devices, xps, kyls, GZ)], axis=2
    ).astype(jnp.bfloat16)
    r3 = lax.all_to_all(back, AXES, 0, 0, tiled=True)
    r3 = r3.transpose(2, 1, 0, 3, 4).reshape(2 * xps, GY, GZ)
    p4 = jnp.einsum("yk,bkz->ybz", fy, r3, preferred_element_type=jnp.float32).reshape(2 * GY, 2, xps, GZ)
    v_re = p4[:GY, 0] - p4[GY:, 1]
    v_im = p4[:GY, 1] + p4[GY:, 0]
    return jnp.concatenate([v_re, v_im], axis=-1).reshape(GY * xps, 2 * GZ).astype(jnp.bfloat16)


def gnn_layer(hidden, gathered, unit_w, radial_parts, w_self, w_nbr, w_rad, w_msg, w_out, gain):
    atoms, width = hidden.shape
    fanout = gathered.shape[0] // atoms
    gathered_h = gathered[:, :width].astype(jnp.bfloat16)
    r_hi, r_lo = radial_parts
    w_hi, w_lo = split2(w_rad)
    lhs = jnp.concatenate([gathered_h, r_hi, r_lo, r_hi], axis=1)
    rhs = jnp.concatenate([w_nbr, w_hi, w_hi, w_lo], axis=0)
    own_term = mm(hidden, w_self)
    pre = mm(lhs, rhs).reshape(atoms, fanout, width) + own_term[:, None, :]
    message = silu(pre).astype(jnp.bfloat16)
    parts = jnp.einsum("akc,akf->acf", unit_w, message, preferred_element_type=jnp.float32)
    sums = jnp.concatenate([parts[:, :1], parts[:, 1:4] + parts[:, 4:7]], axis=1)
    s_hi, s_lo = split2(sums.reshape(atoms * 4, width))
    mixed = (mm(s_hi, w_msg) + mm(s_lo, w_msg)).reshape(atoms, 4, width) / fanout
    total = mixed[:, 0] + jnp.sum(mixed[:, 1:] * mixed[:, 1:], axis=1)
    normed = total * lax.rsqrt(jnp.mean(total * total, axis=-1, keepdims=True) + norm_eps) * gain
    active = silu(normed).astype(jnp.bfloat16)
    update = mm(active, w_out)
    return (hidden.astype(jnp.float32) + update).astype(jnp.bfloat16)


def per_device(
    feats,
    coords,
    nbrs,
    owner,
    cell,
    w_self,
    w_nbr,
    w_rad,
    w_msg,
    w_out,
    norm_gain,
    w_charge,
    w_energy,
):
    atoms, width = feats.shape
    fanout = nbrs.shape[1]
    n_dom = lax.axis_size("dom")
    n_pme = lax.axis_size("pme")
    devices = n_dom * n_pme
    pos_own = coords.T
    p_hi, p_mid, p_lo = split3(pos_own)
    flat_nbrs = nbrs.reshape(-1)
    blocks = [
        (flat_nbrs[:, None] == (b * atoms + jnp.arange(atoms, dtype=jnp.int32))[None, :]).astype(
            jnp.bfloat16
        )
        for b in range(3)
    ]

    def gather_wide(own):
        before, after = halo_parts(own)
        return mm(blocks[1], own) + mm(blocks[0], before) + mm(blocks[2], after)

    hidden = feats
    unit_w = None
    radial_parts = None
    for layer_idx in range(LAYERS):
        if layer_idx == 0:
            gathered = gather_wide(jnp.concatenate([feats, p_hi, p_mid, p_lo], axis=1))
            gpt = gathered[:, width:].T
            lift = jnp.where(
                flat_nbrs < atoms, -slab_depth, jnp.where(flat_nbrs >= 2 * atoms, slab_depth, 0.0)
            )
            pos_jt = gpt[0:3] + gpt[3:6] + gpt[6:9]
            pos_jt = jnp.concatenate([pos_jt[:2], pos_jt[2:] + lift[None, :]], axis=0)
            delta_t = pos_jt - jnp.repeat(coords, fanout, axis=1)
            dist = jnp.sqrt(jnp.sum(delta_t * delta_t, axis=0) + 1.0)
            centres = radial_width * (jnp.arange(NB, dtype=jnp.float32) + 1.0)
            radial_t = jnp.exp(-jnp.square((dist[None, :] - centres[:, None]) / radial_width))
            r_hi_t, r_lo_t = split2(radial_t)
            radial_parts = (r_hi_t.T, r_lo_t.T)
            u_hi, u_lo = split2(delta_t / dist[None, :])
            pairs = flat_nbrs.shape[0]
            unit_w = jnp.concatenate(
                [jnp.ones((1, pairs), jnp.bfloat16), u_hi, u_lo, jnp.zeros((1, pairs), jnp.bfloat16)],
                axis=0,
            ).T.reshape(atoms, fanout, 8)
        else:
            gathered = gather_wide(hidden)
        hidden = gnn_layer(
            hidden,
            gathered,
            unit_w,
            radial_parts,
            w_self[layer_idx],
            w_nbr[layer_idx],
            w_rad[layer_idx],
            w_msg[layer_idx],
            w_out[layer_idx],
            norm_gain[layer_idx],
        )
    flat_hidden = hidden.astype(jnp.float32)
    readout = jnp.dot(flat_hidden, jnp.stack([w_energy, w_charge], axis=1), precision=highest)
    energy_ml = readout[:, 0]
    charge = readout[:, 1]
    capacity = max(2, 2 * atoms // devices) * n_pme
    bx = GX // n_dom
    by = GY // n_pme
    xps = GX // devices
    dest_owner = owner[:, 0]
    grid_x = dest_owner // n_pme * bx + cell // (by * GZ)
    grid_y = dest_owner % n_pme * by + cell // GZ % by
    grid_z = cell % GZ
    dest = grid_x // xps
    slab_cell = (grid_y * xps + grid_x % xps) * GZ + grid_z
    matches = (dest[:, None] == jnp.arange(devices, dtype=jnp.int32)[None, :]).astype(jnp.int32)
    slot = jnp.sum((jnp.cumsum(matches, axis=0) - matches) * matches, axis=1)
    where_to = dest * capacity + slot
    payload = jnp.stack([charge, slab_cell.astype(jnp.float32)], axis=1)
    outgoing = jnp.zeros((devices * capacity, 2), jnp.float32).at[where_to].set(payload)
    incoming = lax.all_to_all(outgoing, AXES, 0, 0, tiled=True)
    cells_here = incoming[:, 1].astype(jnp.int32)
    rows_here = cells_here // GZ
    z_here = cells_here % GZ
    n_rows = GY * xps
    oh_rows = (jnp.arange(n_rows, dtype=jnp.int32)[:, None] == rows_here[None, :]).astype(jnp.bfloat16)
    oh_z = z_here[:, None] == jnp.arange(GZ, dtype=jnp.int32)[None, :]
    q_hi, q_lo = split2(incoming[:, 0])
    zero = jnp.zeros((), jnp.bfloat16)
    qz = jnp.concatenate(
        [jnp.where(oh_z, q_hi[:, None], zero), jnp.where(oh_z, q_lo[:, None], zero)], axis=1
    )
    dparts = mm(oh_rows, qz)
    density = dparts[:, :GZ] + dparts[:, GZ:]
    dev_index = lax.axis_index("dom") * n_pme + lax.axis_index("pme")
    spectrum_rows = solve_field(density, devices, dev_index)
    picked = lax.dot_general(
        oh_rows, spectrum_rows, (((0,), (0,)), ((), ())), preferred_element_type=jnp.float32
    )
    cz, sz = dft_pair(GZ)
    ez_t = jnp.asarray(np.concatenate([cz, -sz], axis=1), jnp.bfloat16)
    ez_rows = mm(oh_z.astype(jnp.bfloat16), ez_t)
    sampled = jnp.sum(picked * ez_rows, axis=1)
    returned = lax.all_to_all(sampled, AXES, 0, 0, tiled=True)
    at_atoms = returned[where_to]
    energy_el = 0.5 * charge * at_atoms
    return (energy_ml, energy_el)


def solution(mesh):
    in_specs = (
        P(("dom", "pme"), None),
        P(None, ("dom", "pme")),
        P(("dom", "pme"), None),
        P(("dom", "pme"), None),
        P(("dom", "pme")),
        P(),
        P(),
        P(),
        P(),
        P(),
        P(),
        P(),
        P(),
    )
    out_specs = (P(("dom", "pme")), P(("dom", "pme")))
    return jax.shard_map(
        per_device, mesh=mesh, in_specs=in_specs, out_specs=out_specs, check_vma=False
    )
```

```python
import math

import jax
import jax.numpy as jnp
import numpy as np
from jax import lax
from jax.sharding import PartitionSpec as P

NB = 8
LAYERS = 2
GX = 256
GY = 256
GZ = 128


slab_depth = 3.0
radial_width = 0.75
ewald_beta = 1.2
norm_eps = 1e-05
highest = lax.Precision.HIGHEST
AXES = ("dom", "pme")


def to_bf16_exact(x):
    return lax.reduce_precision(x, exponent_bits=8, mantissa_bits=7)


def split2(x):
    hi = to_bf16_exact(x)
    lo = x - hi
    return hi.astype(jnp.bfloat16), lo.astype(jnp.bfloat16)


def split3(x):
    hi = to_bf16_exact(x)
    rest = x - hi
    mid = to_bf16_exact(rest)
    lo = rest - mid
    return hi.astype(jnp.bfloat16), mid.astype(jnp.bfloat16), lo.astype(jnp.bfloat16)


def halo(shard):
    devices = lax.axis_size(AXES)
    up = [(i, (i + 1) % devices) for i in range(devices)]
    down = [(j, i) for i, j in up]
    before = lax.ppermute(shard, AXES, up)
    after = lax.ppermute(shard, AXES, down)
    return jnp.concatenate([before, shard, after], axis=0)


def silu(x):
    return x * jax.nn.sigmoid(x)


def dft_pair(length):
    k = np.arange(length, dtype=np.int64)
    angle = (np.outer(k, k) % length).astype(np.float64) * (2.0 * math.pi / length)
    return np.cos(angle), np.sin(angle)


def wave_square(count, start, full):
    index = start + jnp.arange(count, dtype=jnp.int32)
    folded = jnp.where(index < full // 2, index, index - full).astype(jnp.float32)
    scaled = folded * (2.0 * math.pi / full)
    return scaled * scaled


def green(wave_x, wave_y, wave_z):
    ksq = wave_x[:, None, None] + wave_y[None, :, None] + wave_z[None, None, :]
    safe = jnp.where(ksq > 0, ksq, 1.0)
    return jnp.where(
        ksq > 0, 4.0 * math.pi * jnp.exp(-ksq / (4.0 * ewald_beta * ewald_beta)) / safe, 0.0
    )


def mm(a, b):
    return jnp.dot(a, b, preferred_element_type=jnp.float32)


def combine(p, forward):
    rows, cols = p.shape
    c, s = p[: rows // 2], p[rows // 2 :]
    c_re, c_im = c[:, : cols // 2], c[:, cols // 2 :]
    s_re, s_im = s[:, : cols // 2], s[:, cols // 2 :]
    if forward:
        return c_re + s_im, c_im - s_re
    return c_re - s_im, c_im + s_re


def regroup(parts, split, perm, shape, axis):
    moved = [x.astype(jnp.bfloat16).reshape(split).transpose(perm).reshape(shape) for x in parts]
    return jnp.concatenate(moved, axis=axis)


def solve_field(density, devices, dev_index):
    xps = GX // devices
    kyls = GY // devices
    cz, sz = dft_pair(GZ)
    fa = jnp.asarray(np.concatenate([cz, -sz], axis=1), jnp.bfloat16)
    d_hi, d_lo = split2(density)
    a = mm(d_hi, fa) + mm(d_lo, fa)
    a_re = a[:, :GZ].reshape(GY, xps, GZ).astype(jnp.bfloat16)
    a_im = a[:, GZ:].reshape(GY, xps, GZ).astype(jnp.bfloat16)
    cy, sy = dft_pair(GY)
    fy = jnp.asarray(np.concatenate([cy, sy], axis=0), jnp.bfloat16)
    p = jnp.einsum("ky,ypz->kpz", fy, a_re, preferred_element_type=jnp.float32)
    q = jnp.einsum("ky,ypz->kpz", fy, a_im, preferred_element_type=jnp.float32)
    y_re = p[:GY] + q[GY:]
    y_im = q[:GY] - p[GY:]

    def by_dest(t):
        return t.reshape(devices, kyls, xps, GZ).transpose(0, 2, 1, 3)

    sent = jnp.stack([by_dest(y_re), by_dest(y_im)], axis=2).astype(jnp.bfloat16)
    r2 = lax.all_to_all(sent, AXES, 0, 0, tiled=True)
    cx, sx = dft_pair(GX)
    fx = jnp.asarray(np.concatenate([cx, sx], axis=0), jnp.bfloat16)
    p2 = jnp.einsum("kpx,pxrjz->krjz", fx.reshape(2 * GX, devices, xps), r2, preferred_element_type=jnp.float32)
    z_re = p2[:GX, 0] + p2[GX:, 1]
    z_im = p2[:GX, 1] - p2[GX:, 0]
    kernel = green(
        wave_square(GX, 0, GX), wave_square(kyls, dev_index * kyls, GY), wave_square(GZ, 0, GZ)
    ) * (1.0 / (GX * GY * GZ))
    z = jnp.stack([z_re * kernel, z_im * kernel], axis=1).astype(jnp.bfloat16)
    p3 = jnp.einsum("xk,krjz->xrjz", fx, z, preferred_element_type=jnp.float32)
    w_re = p3[:GX, 0] - p3[GX:, 1]
    w_im = p3[:GX, 1] + p3[GX:, 0]
    back = jnp.stack(
        [w_re.reshape(devices, xps, kyls, GZ), w_im.reshape(devices, xps, kyls, GZ)], axis=2
    ).astype(jnp.bfloat16)
    r3 = lax.all_to_all(back, AXES, 0, 0, tiled=True)
    r3 = r3.transpose(2, 1, 0, 3, 4).reshape(2 * xps, GY, GZ)
    p4 = jnp.einsum("yk,bkz->ybz", fy, r3, preferred_element_type=jnp.float32).reshape(2 * GY, 2, xps, GZ)
    v_re = p4[:GY, 0] - p4[GY:, 1]
    v_im = p4[:GY, 1] + p4[GY:, 0]
    return jnp.concatenate([v_re, v_im], axis=-1).reshape(GY * xps, 2 * GZ).astype(jnp.bfloat16)


def gnn_layer(hidden, gathered, unit_w, radial_parts, w_self, w_nbr, w_rad, w_msg, w_out, gain):
    atoms, width = hidden.shape
    fanout = gathered.shape[0] // atoms
    gathered_h = gathered[:, :width]
    r_hi, r_lo = radial_parts
    w_hi, w_lo = split2(w_rad)
    lhs = jnp.concatenate([gathered_h, r_hi, r_lo, r_hi], axis=1)
    rhs = jnp.concatenate([w_nbr, w_hi, w_hi, w_lo], axis=0)
    own_term = mm(hidden, w_self)
    pre = mm(lhs, rhs).reshape(atoms, fanout, width) + own_term[:, None, :]
    message = silu(pre).astype(jnp.bfloat16)
    parts = jnp.einsum("akc,akf->acf", unit_w, message, preferred_element_type=jnp.float32)
    sums = jnp.concatenate([parts[:, :1], parts[:, 1:4] + parts[:, 4:7]], axis=1)
    s_hi, s_lo = split2(sums.reshape(atoms * 4, width))
    mixed = (mm(s_hi, w_msg) + mm(s_lo, w_msg)).reshape(atoms, 4, width) / fanout
    total = mixed[:, 0] + jnp.sum(mixed[:, 1:] * mixed[:, 1:], axis=1)
    normed = total * lax.rsqrt(jnp.mean(total * total, axis=-1, keepdims=True) + norm_eps) * gain
    active = silu(normed).astype(jnp.bfloat16)
    update = mm(active, w_out)
    return (hidden.astype(jnp.float32) + update).astype(jnp.bfloat16)


def per_device(
    feats,
    coords,
    nbrs,
    owner,
    cell,
    w_self,
    w_nbr,
    w_rad,
    w_msg,
    w_out,
    norm_gain,
    w_charge,
    w_energy,
):
    atoms, width = feats.shape
    fanout = nbrs.shape[1]
    n_dom = lax.axis_size("dom")
    n_pme = lax.axis_size("pme")
    devices = n_dom * n_pme
    wide_rows = 3 * atoms
    pos_own = coords.T
    p_hi, p_mid, p_lo = split3(pos_own)
    wide0 = halo(jnp.concatenate([feats, p_hi, p_mid, p_lo], axis=1))
    flat_nbrs = nbrs.reshape(-1)
    onehot = (flat_nbrs[:, None] == jnp.arange(wide_rows, dtype=jnp.int32)[None, :]).astype(
        jnp.bfloat16
    )
    hidden = feats
    unit_w = None
    radial_parts = None
    for layer_idx in range(LAYERS):
        table = wide0 if layer_idx == 0 else halo(hidden)
        gathered = jnp.dot(onehot, table, preferred_element_type=jnp.bfloat16)
        if layer_idx == 0:
            gp = gathered[:, width:].astype(jnp.float32)
            pos_j = gp[:, 0:3] + gp[:, 3:6] + gp[:, 6:9]
            lift = jnp.where(flat_nbrs < atoms, -slab_depth, jnp.where(flat_nbrs >= 2 * atoms, slab_depth, 0.0))
            pos_j = pos_j.at[:, 2].add(lift)
            delta = pos_j.reshape(atoms, fanout, 3) - pos_own[:, None, :]
            dist = jnp.sqrt(jnp.sum(delta * delta, axis=-1) + 1.0)
            centres = radial_width * (jnp.arange(NB, dtype=jnp.float32) + 1.0)
            radial = jnp.exp(-jnp.square((dist[:, :, None] - centres) / radial_width))
            radial_parts = split2(radial.reshape(atoms * fanout, NB))
            unit = delta / dist[:, :, None]
            u_hi, u_lo = split2(unit)
            unit_w = jnp.concatenate(
                [jnp.ones((atoms, fanout, 1), jnp.bfloat16), u_hi, u_lo, jnp.zeros((atoms, fanout, 1), jnp.bfloat16)],
                axis=-1,
            )
        hidden = gnn_layer(
            hidden,
            gathered,
            unit_w,
            radial_parts,
            w_self[layer_idx],
            w_nbr[layer_idx],
            w_rad[layer_idx],
            w_msg[layer_idx],
            w_out[layer_idx],
            norm_gain[layer_idx],
        )
    flat_hidden = hidden.astype(jnp.float32)
    readout = jnp.dot(flat_hidden, jnp.stack([w_energy, w_charge], axis=1), precision=highest)
    energy_ml = readout[:, 0]
    charge = readout[:, 1]
    capacity = max(2, 2 * atoms // devices) * n_pme
    bx = GX // n_dom
    by = GY // n_pme
    xps = GX // devices
    dest_owner = owner[:, 0]
    grid_x = dest_owner // n_pme * bx + cell // (by * GZ)
    grid_y = dest_owner % n_pme * by + cell // GZ % by
    grid_z = cell % GZ
    dest = grid_x // xps
    slab_cell = (grid_y * xps + grid_x % xps) * GZ + grid_z
    matches = (dest[:, None] == jnp.arange(devices, dtype=jnp.int32)[None, :]).astype(jnp.int32)
    slot = jnp.sum((jnp.cumsum(matches, axis=0) - matches) * matches, axis=1)
    where_to = dest * capacity + slot
    payload = jnp.stack([charge, slab_cell.astype(jnp.float32)], axis=1)
    outgoing = jnp.zeros((devices * capacity, 2), jnp.float32).at[where_to].set(payload)
    incoming = lax.all_to_all(outgoing, AXES, 0, 0, tiled=True)
    cells_here = incoming[:, 1].astype(jnp.int32)
    rows_here = cells_here // GZ
    z_here = cells_here % GZ
    n_rows = GY * xps
    oh_rows = (jnp.arange(n_rows, dtype=jnp.int32)[:, None] == rows_here[None, :]).astype(jnp.bfloat16)
    oh_z = z_here[:, None] == jnp.arange(GZ, dtype=jnp.int32)[None, :]
    q_hi, q_lo = split2(incoming[:, 0])
    zero = jnp.zeros((), jnp.bfloat16)
    qz = jnp.concatenate(
        [jnp.where(oh_z, q_hi[:, None], zero), jnp.where(oh_z, q_lo[:, None], zero)], axis=1
    )
    dparts = mm(oh_rows, qz)
    density = dparts[:, :GZ] + dparts[:, GZ:]
    dev_index = lax.axis_index("dom") * n_pme + lax.axis_index("pme")
    spectrum_rows = solve_field(density, devices, dev_index)
    picked = lax.dot_general(
        oh_rows, spectrum_rows, (((0,), (0,)), ((), ())), preferred_element_type=jnp.float32
    )
    cz, sz = dft_pair(GZ)
    ez_t = jnp.asarray(np.concatenate([cz, -sz], axis=1), jnp.bfloat16)
    ez_rows = mm(oh_z.astype(jnp.bfloat16), ez_t)
    sampled = jnp.sum(picked * ez_rows, axis=1)
    returned = lax.all_to_all(sampled, AXES, 0, 0, tiled=True)
    at_atoms = returned[where_to]
    energy_el = 0.5 * charge * at_atoms
    return (energy_ml, energy_el)


def solution(mesh):
    in_specs = (
        P(("dom", "pme"), None),
        P(None, ("dom", "pme")),
        P(("dom", "pme"), None),
        P(("dom", "pme"), None),
        P(("dom", "pme")),
        P(),
        P(),
        P(),
        P(),
        P(),
        P(),
        P(),
        P(),
    )
    out_specs = (P(("dom", "pme")), P(("dom", "pme")))
    return jax.shard_map(
        per_device, mesh=mesh, in_specs=in_specs, out_specs=out_specs, check_vma=False
    )
```

```python
import math

import jax
import jax.numpy as jnp
import numpy as np
from jax import lax
from jax.sharding import PartitionSpec as P

NB = 8
LAYERS = 2
GX = 256
GY = 256
GZ = 128


slab_depth = 3.0
radial_width = 0.75
ewald_beta = 1.2
norm_eps = 1e-05
highest = lax.Precision.HIGHEST
AXES = ("dom", "pme")


def to_bf16_exact(x):
    return lax.reduce_precision(x, exponent_bits=8, mantissa_bits=7)


def split2(x):
    hi = to_bf16_exact(x)
    lo = x - hi
    return hi.astype(jnp.bfloat16), lo.astype(jnp.bfloat16)


def split3(x):
    hi = to_bf16_exact(x)
    rest = x - hi
    mid = to_bf16_exact(rest)
    lo = rest - mid
    return hi.astype(jnp.bfloat16), mid.astype(jnp.bfloat16), lo.astype(jnp.bfloat16)


def halo(shard):
    devices = lax.axis_size(AXES)
    up = [(i, (i + 1) % devices) for i in range(devices)]
    down = [(j, i) for i, j in up]
    before = lax.ppermute(shard, AXES, up)
    after = lax.ppermute(shard, AXES, down)
    return jnp.concatenate([before, shard, after], axis=0)


def silu(x):
    return x * jax.nn.sigmoid(x)


def dft_pair(length):
    k = np.arange(length, dtype=np.int64)
    angle = (np.outer(k, k) % length).astype(np.float64) * (2.0 * math.pi / length)
    return np.cos(angle), np.sin(angle)


def wave_square(count, start, full):
    index = start + jnp.arange(count, dtype=jnp.int32)
    folded = jnp.where(index < full // 2, index, index - full).astype(jnp.float32)
    scaled = folded * (2.0 * math.pi / full)
    return scaled * scaled


def green(wave_x, wave_y, wave_z):
    ksq = wave_x[:, None, None] + wave_y[None, :, None] + wave_z[None, None, :]
    safe = jnp.where(ksq > 0, ksq, 1.0)
    return jnp.where(
        ksq > 0, 4.0 * math.pi * jnp.exp(-ksq / (4.0 * ewald_beta * ewald_beta)) / safe, 0.0
    )


def mm(a, b):
    return jnp.dot(a, b, preferred_element_type=jnp.float32)


def combine(p, forward):
    rows, cols = p.shape
    c, s = p[: rows // 2], p[rows // 2 :]
    c_re, c_im = c[:, : cols // 2], c[:, cols // 2 :]
    s_re, s_im = s[:, : cols // 2], s[:, cols // 2 :]
    if forward:
        return c_re + s_im, c_im - s_re
    return c_re - s_im, c_im + s_re


def regroup(parts, split, perm, shape, axis):
    moved = [x.astype(jnp.bfloat16).reshape(split).transpose(perm).reshape(shape) for x in parts]
    return jnp.concatenate(moved, axis=axis)


def solve_field(density, devices, dev_index):
    xps = GX // devices
    kyls = GY // devices
    cz, sz = dft_pair(GZ)
    fa = jnp.asarray(np.concatenate([cz, -sz], axis=1), jnp.bfloat16)
    d_hi, d_lo = split2(density)
    a = mm(d_hi, fa) + mm(d_lo, fa)
    a_re = a[:, :GZ].reshape(GY, xps, GZ).astype(jnp.bfloat16)
    a_im = a[:, GZ:].reshape(GY, xps, GZ).astype(jnp.bfloat16)
    cy, sy = dft_pair(GY)
    fy = jnp.asarray(np.concatenate([cy, sy], axis=0), jnp.bfloat16)
    p = jnp.einsum("ky,ypz->kpz", fy, a_re, preferred_element_type=jnp.float32)
    q = jnp.einsum("ky,ypz->kpz", fy, a_im, preferred_element_type=jnp.float32)
    y_re = p[:GY] + q[GY:]
    y_im = q[:GY] - p[GY:]

    def by_dest(t):
        return t.reshape(devices, kyls, xps, GZ).transpose(0, 2, 1, 3)

    sent = jnp.stack([by_dest(y_re), by_dest(y_im)], axis=2).astype(jnp.bfloat16)
    r2 = lax.all_to_all(sent, AXES, 0, 0, tiled=True)
    cx, sx = dft_pair(GX)
    fx = jnp.asarray(np.concatenate([cx, sx], axis=0), jnp.bfloat16)
    p2 = jnp.einsum("kpx,pxrjz->krjz", fx.reshape(2 * GX, devices, xps), r2, preferred_element_type=jnp.float32)
    z_re = p2[:GX, 0] + p2[GX:, 1]
    z_im = p2[:GX, 1] - p2[GX:, 0]
    kernel = green(
        wave_square(GX, 0, GX), wave_square(kyls, dev_index * kyls, GY), wave_square(GZ, 0, GZ)
    ) * (1.0 / (GX * GY * GZ))
    z = jnp.stack([z_re * kernel, z_im * kernel], axis=1).astype(jnp.bfloat16)
    p3 = jnp.einsum("xk,krjz->xrjz", fx, z, preferred_element_type=jnp.float32)
    w_re = p3[:GX, 0] - p3[GX:, 1]
    w_im = p3[:GX, 1] + p3[GX:, 0]
    back = jnp.stack(
        [w_re.reshape(devices, xps, kyls, GZ), w_im.reshape(devices, xps, kyls, GZ)], axis=2
    ).astype(jnp.bfloat16)
    r3 = lax.all_to_all(back, AXES, 0, 0, tiled=True)
    r3 = r3.transpose(2, 1, 0, 3, 4).reshape(2 * xps, GY, GZ)
    p4 = jnp.einsum("yk,bkz->ybz", fy, r3, preferred_element_type=jnp.float32).reshape(2 * GY, 2, xps, GZ)
    v_re = p4[:GY, 0] - p4[GY:, 1]
    v_im = p4[:GY, 1] + p4[GY:, 0]
    return jnp.concatenate([v_re, v_im], axis=-1).reshape(GY * xps, 2 * GZ).astype(jnp.bfloat16)


def gnn_layer(hidden, gathered, unit_w, radial_parts, w_self, w_nbr, w_rad, w_msg, w_out, gain):
    atoms, width = hidden.shape
    fanout = gathered.shape[0] // atoms
    gathered_h = gathered[:, :width]
    r_hi, r_lo = radial_parts
    w_hi, w_lo = split2(w_rad)
    lhs = jnp.concatenate([gathered_h, r_hi, r_lo, r_hi], axis=1)
    rhs = jnp.concatenate([w_nbr, w_hi, w_hi, w_lo], axis=0)
    own_term = mm(hidden, w_self)
    pre = mm(lhs, rhs).reshape(atoms, fanout, width) + own_term[:, None, :]
    message = silu(pre).astype(jnp.bfloat16)
    parts = jnp.einsum("akc,akf->acf", unit_w, message, preferred_element_type=jnp.float32)
    sums = jnp.concatenate([parts[:, :1], parts[:, 1:4] + parts[:, 4:7]], axis=1)
    s_hi, s_lo = split2(sums.reshape(atoms * 4, width))
    mixed = (mm(s_hi, w_msg) + mm(s_lo, w_msg)).reshape(atoms, 4, width) / fanout
    total = mixed[:, 0] + jnp.sum(mixed[:, 1:] * mixed[:, 1:], axis=1)
    normed = total * lax.rsqrt(jnp.mean(total * total, axis=-1, keepdims=True) + norm_eps) * gain
    active = silu(normed).astype(jnp.bfloat16)
    update = mm(active, w_out)
    return (hidden.astype(jnp.float32) + update).astype(jnp.bfloat16)


def per_device(
    feats,
    coords,
    nbrs,
    owner,
    cell,
    w_self,
    w_nbr,
    w_rad,
    w_msg,
    w_out,
    norm_gain,
    w_charge,
    w_energy,
):
    atoms, width = feats.shape
    fanout = nbrs.shape[1]
    n_dom = lax.axis_size("dom")
    n_pme = lax.axis_size("pme")
    devices = n_dom * n_pme
    wide_rows = 3 * atoms
    pos_own = coords.T
    p_hi, p_mid, p_lo = split3(pos_own)
    wide0 = halo(jnp.concatenate([feats, p_hi, p_mid, p_lo], axis=1))
    flat_nbrs = nbrs.reshape(-1)
    onehot = (flat_nbrs[:, None] == jnp.arange(wide_rows, dtype=jnp.int32)[None, :]).astype(
        jnp.bfloat16
    )
    hidden = feats
    unit_w = None
    radial_parts = None
    for layer_idx in range(LAYERS):
        table = wide0 if layer_idx == 0 else halo(hidden)
        gathered = jnp.dot(onehot, table, preferred_element_type=jnp.bfloat16)
        if layer_idx == 0:
            gp = gathered[:, width:].astype(jnp.float32)
            pos_j = gp[:, 0:3] + gp[:, 3:6] + gp[:, 6:9]
            lift = jnp.where(flat_nbrs < atoms, -slab_depth, jnp.where(flat_nbrs >= 2 * atoms, slab_depth, 0.0))
            pos_j = pos_j.at[:, 2].add(lift)
            delta = pos_j.reshape(atoms, fanout, 3) - pos_own[:, None, :]
            dist = jnp.sqrt(jnp.sum(delta * delta, axis=-1) + 1.0)
            centres = radial_width * (jnp.arange(NB, dtype=jnp.float32) + 1.0)
            radial = jnp.exp(-jnp.square((dist[:, :, None] - centres) / radial_width))
            radial_parts = split2(radial.reshape(atoms * fanout, NB))
            unit = delta / dist[:, :, None]
            u_hi, u_lo = split2(unit)
            unit_w = jnp.concatenate(
                [jnp.ones((atoms, fanout, 1), jnp.bfloat16), u_hi, u_lo, jnp.zeros((atoms, fanout, 1), jnp.bfloat16)],
                axis=-1,
            )
        hidden = gnn_layer(
            hidden,
            gathered,
            unit_w,
            radial_parts,
            w_self[layer_idx],
            w_nbr[layer_idx],
            w_rad[layer_idx],
            w_msg[layer_idx],
            w_out[layer_idx],
            norm_gain[layer_idx],
        )
    flat_hidden = hidden.astype(jnp.float32)
    readout = jnp.dot(flat_hidden, jnp.stack([w_energy, w_charge], axis=1), precision=highest)
    energy_ml = readout[:, 0]
    charge = readout[:, 1]
    capacity = max(2, 2 * atoms // devices) * n_pme
    bx = GX // n_dom
    by = GY // n_pme
    xps = GX // devices
    dest_owner = owner[:, 0]
    grid_x = dest_owner // n_pme * bx + cell // (by * GZ)
    grid_y = dest_owner % n_pme * by + cell // GZ % by
    grid_z = cell % GZ
    dest = grid_x // xps
    slab_cell = (grid_y * xps + grid_x % xps) * GZ + grid_z
    matches = (dest[:, None] == jnp.arange(devices, dtype=jnp.int32)[None, :]).astype(jnp.int32)
    slot = jnp.sum((jnp.cumsum(matches, axis=0) - matches) * matches, axis=1)
    where_to = dest * capacity + slot
    row_tag = (jnp.arange(atoms, dtype=jnp.int32) + 1).astype(jnp.float32)
    payload = jnp.stack([charge, slab_cell.astype(jnp.float32), row_tag], axis=1)
    outgoing = jnp.zeros((devices * capacity, 3), jnp.float32).at[where_to].set(payload)
    incoming = lax.all_to_all(outgoing, AXES, 0, 0, tiled=True)
    cells_here = incoming[:, 1].astype(jnp.int32)
    rows_here = cells_here // GZ
    z_here = cells_here % GZ
    n_rows = GY * xps
    oh_rows = (jnp.arange(n_rows, dtype=jnp.int32)[:, None] == rows_here[None, :]).astype(jnp.bfloat16)
    oh_z = z_here[:, None] == jnp.arange(GZ, dtype=jnp.int32)[None, :]
    q_hi, q_lo = split2(incoming[:, 0])
    zero = jnp.zeros((), jnp.bfloat16)
    qz = jnp.concatenate(
        [jnp.where(oh_z, q_hi[:, None], zero), jnp.where(oh_z, q_lo[:, None], zero)], axis=1
    )
    dparts = mm(oh_rows, qz)
    density = dparts[:, :GZ] + dparts[:, GZ:]
    dev_index = lax.axis_index("dom") * n_pme + lax.axis_index("pme")
    spectrum_rows = solve_field(density, devices, dev_index)
    picked = lax.dot_general(
        oh_rows, spectrum_rows, (((0,), (0,)), ((), ())), preferred_element_type=jnp.float32
    )
    cz, sz = dft_pair(GZ)
    ez_t = jnp.asarray(np.concatenate([cz, -sz], axis=1), jnp.bfloat16)
    ez_rows = mm(oh_z.astype(jnp.bfloat16), ez_t)
    sampled = jnp.sum(picked * ez_rows, axis=1)
    rows_back = incoming[:, 2].astype(jnp.int32).reshape(devices, capacity) - 1
    hit = rows_back[:, :, None] == jnp.arange(atoms, dtype=jnp.int32)[None, None, :]
    spread = jnp.sum(jnp.where(hit, sampled.reshape(devices, capacity)[:, :, None], 0.0), axis=1)
    at_atoms = lax.psum_scatter(spread, AXES, scatter_dimension=0, tiled=True)[0]
    energy_el = 0.5 * charge * at_atoms
    return (energy_ml, energy_el)


def solution(mesh):
    in_specs = (
        P(("dom", "pme"), None),
        P(None, ("dom", "pme")),
        P(("dom", "pme"), None),
        P(("dom", "pme"), None),
        P(("dom", "pme")),
        P(),
        P(),
        P(),
        P(),
        P(),
        P(),
        P(),
        P(),
    )
    out_specs = (P(("dom", "pme")), P(("dom", "pme")))
    return jax.shard_map(
        per_device, mesh=mesh, in_specs=in_specs, out_specs=out_specs, check_vma=False
    )
```

```python
import math

import jax
import jax.numpy as jnp
import numpy as np
from jax import lax
from jax.sharding import PartitionSpec as P

NB = 8
LAYERS = 2
GX = 256
GY = 256
GZ = 128


slab_depth = 3.0
radial_width = 0.75
ewald_beta = 1.2
norm_eps = 1e-05
highest = lax.Precision.HIGHEST
AXES = ("dom", "pme")


def to_bf16_exact(x):
    return lax.reduce_precision(x, exponent_bits=8, mantissa_bits=7)


def split2(x):
    hi = to_bf16_exact(x)
    lo = x - hi
    return hi.astype(jnp.bfloat16), lo.astype(jnp.bfloat16)


def split3(x):
    hi = to_bf16_exact(x)
    rest = x - hi
    mid = to_bf16_exact(rest)
    lo = rest - mid
    return hi.astype(jnp.bfloat16), mid.astype(jnp.bfloat16), lo.astype(jnp.bfloat16)


def halo(shard):
    devices = lax.axis_size(AXES)
    up = [(i, (i + 1) % devices) for i in range(devices)]
    down = [(j, i) for i, j in up]
    before = lax.ppermute(shard, AXES, up)
    after = lax.ppermute(shard, AXES, down)
    return jnp.concatenate([before, shard, after], axis=0)


def silu(x):
    return x * jax.nn.sigmoid(x)


def dft_pair(length):
    k = np.arange(length, dtype=np.int64)
    angle = (np.outer(k, k) % length).astype(np.float64) * (2.0 * math.pi / length)
    return np.cos(angle), np.sin(angle)


def wave_square(count, start, full):
    index = start + jnp.arange(count, dtype=jnp.int32)
    folded = jnp.where(index < full // 2, index, index - full).astype(jnp.float32)
    scaled = folded * (2.0 * math.pi / full)
    return scaled * scaled


def green(wave_x, wave_y, wave_z):
    ksq = wave_x[:, None, None] + wave_y[None, :, None] + wave_z[None, None, :]
    safe = jnp.where(ksq > 0, ksq, 1.0)
    return jnp.where(
        ksq > 0, 4.0 * math.pi * jnp.exp(-ksq / (4.0 * ewald_beta * ewald_beta)) / safe, 0.0
    )


def mm(a, b):
    return jnp.dot(a, b, preferred_element_type=jnp.float32)


def combine(p, forward):
    rows, cols = p.shape
    c, s = p[: rows // 2], p[rows // 2 :]
    c_re, c_im = c[:, : cols // 2], c[:, cols // 2 :]
    s_re, s_im = s[:, : cols // 2], s[:, cols // 2 :]
    if forward:
        return c_re + s_im, c_im - s_re
    return c_re - s_im, c_im + s_re


def regroup(parts, split, perm, shape, axis):
    moved = [x.astype(jnp.bfloat16).reshape(split).transpose(perm).reshape(shape) for x in parts]
    return jnp.concatenate(moved, axis=axis)


def solve_field(density, devices, dev_index):
    xps = GX // devices
    kyls = GY // devices
    cz, sz = dft_pair(GZ)
    fa = jnp.asarray(np.concatenate([cz, -sz], axis=1), jnp.bfloat16)
    d_hi, d_lo = split2(density)
    a = mm(d_hi, fa) + mm(d_lo, fa)
    a_re = a[:, :GZ].reshape(GY, xps, GZ).astype(jnp.bfloat16)
    a_im = a[:, GZ:].reshape(GY, xps, GZ).astype(jnp.bfloat16)
    cy, sy = dft_pair(GY)
    fy = jnp.asarray(np.concatenate([cy, sy], axis=0), jnp.bfloat16)
    p = jnp.einsum("ky,ypz->kpz", fy, a_re, preferred_element_type=jnp.float32)
    q = jnp.einsum("ky,ypz->kpz", fy, a_im, preferred_element_type=jnp.float32)
    y_re = p[:GY] + q[GY:]
    y_im = q[:GY] - p[GY:]

    def by_dest(t):
        return t.reshape(devices, kyls, xps, GZ).transpose(0, 2, 1, 3)

    sent = jnp.stack([by_dest(y_re), by_dest(y_im)], axis=2).astype(jnp.bfloat16)
    r2 = lax.all_to_all(sent, AXES, 0, 0, tiled=True)
    cx, sx = dft_pair(GX)
    fx = jnp.asarray(np.concatenate([cx, sx], axis=0), jnp.bfloat16)
    p2 = jnp.einsum("kpx,pxrjz->krjz", fx.reshape(2 * GX, devices, xps), r2, preferred_element_type=jnp.float32)
    z_re = p2[:GX, 0] + p2[GX:, 1]
    z_im = p2[:GX, 1] - p2[GX:, 0]
    kernel = green(
        wave_square(GX, 0, GX), wave_square(kyls, dev_index * kyls, GY), wave_square(GZ, 0, GZ)
    ) * (1.0 / (GX * GY * GZ))
    z = jnp.stack([z_re * kernel, z_im * kernel], axis=1).astype(jnp.bfloat16)
    p3 = jnp.einsum("xk,krjz->xrjz", fx, z, preferred_element_type=jnp.float32)
    w_re = p3[:GX, 0] - p3[GX:, 1]
    w_im = p3[:GX, 1] + p3[GX:, 0]
    back = jnp.stack(
        [w_re.reshape(devices, xps, kyls, GZ), w_im.reshape(devices, xps, kyls, GZ)], axis=2
    ).astype(jnp.bfloat16)
    r3 = lax.all_to_all(back, AXES, 0, 0, tiled=True)
    r3 = r3.transpose(2, 1, 0, 3, 4).reshape(2 * xps, GY, GZ)
    p4 = jnp.einsum("yk,bkz->ybz", fy, r3, preferred_element_type=jnp.float32).reshape(2 * GY, 2, xps, GZ)
    v_re = p4[:GY, 0] - p4[GY:, 1]
    v_im = p4[:GY, 1] + p4[GY:, 0]
    return jnp.concatenate([v_re, v_im], axis=-1).reshape(GY * xps, 2 * GZ).astype(jnp.bfloat16)


def gnn_layer(hidden, gathered, unit_w, radial_parts, w_self, w_nbr, w_rad, w_msg, w_out, gain):
    atoms, width = hidden.shape
    fanout = gathered.shape[0] // atoms
    gathered_h = gathered[:, :width]
    r_hi, r_lo = radial_parts
    w_hi, w_lo = split2(w_rad)
    lhs = jnp.concatenate([gathered_h, r_hi, r_lo, r_hi], axis=1)
    rhs = jnp.concatenate([w_nbr, w_hi, w_hi, w_lo], axis=0)
    own_term = mm(hidden, w_self)
    pre = mm(lhs, rhs).reshape(atoms, fanout, width) + own_term[:, None, :]
    message = silu(pre).astype(jnp.bfloat16)
    parts = jnp.einsum("akc,akf->acf", unit_w, message, preferred_element_type=jnp.float32)
    sums = jnp.concatenate([parts[:, :1], parts[:, 1:4] + parts[:, 4:7]], axis=1)
    s_hi, s_lo = split2(sums.reshape(atoms * 4, width))
    mixed = (mm(s_hi, w_msg) + mm(s_lo, w_msg)).reshape(atoms, 4, width) / fanout
    total = mixed[:, 0] + jnp.sum(mixed[:, 1:] * mixed[:, 1:], axis=1)
    normed = total * lax.rsqrt(jnp.mean(total * total, axis=-1, keepdims=True) + norm_eps) * gain
    active = silu(normed).astype(jnp.bfloat16)
    update = mm(active, w_out)
    return (hidden.astype(jnp.float32) + update).astype(jnp.bfloat16)


def per_device(
    feats,
    coords,
    nbrs,
    owner,
    cell,
    w_self,
    w_nbr,
    w_rad,
    w_msg,
    w_out,
    norm_gain,
    w_charge,
    w_energy,
):
    atoms, width = feats.shape
    fanout = nbrs.shape[1]
    n_dom = lax.axis_size("dom")
    n_pme = lax.axis_size("pme")
    devices = n_dom * n_pme
    wide_rows = 3 * atoms
    pos_own = coords.T
    p_hi, p_mid, p_lo = split3(pos_own)
    wide0 = halo(jnp.concatenate([feats, p_hi, p_mid, p_lo], axis=1))
    flat_nbrs = nbrs.reshape(-1)
    onehot = (flat_nbrs[:, None] == jnp.arange(wide_rows, dtype=jnp.int32)[None, :]).astype(
        jnp.bfloat16
    )
    hidden = feats
    unit_w = None
    radial_parts = None
    for layer_idx in range(LAYERS):
        table = wide0 if layer_idx == 0 else halo(hidden)
        gathered = jnp.dot(onehot, table, preferred_element_type=jnp.bfloat16)
        if layer_idx == 0:
            gp = gathered[:, width:].astype(jnp.float32)
            pos_j = gp[:, 0:3] + gp[:, 3:6] + gp[:, 6:9]
            lift = jnp.where(flat_nbrs < atoms, -slab_depth, jnp.where(flat_nbrs >= 2 * atoms, slab_depth, 0.0))
            pos_j = pos_j + jnp.where(jnp.arange(3, dtype=jnp.int32) == 2, 1.0, 0.0)[None, :] * lift[:, None]
            delta = pos_j.reshape(atoms, fanout, 3) - pos_own[:, None, :]
            dist = jnp.sqrt(jnp.sum(delta * delta, axis=-1) + 1.0)
            centres = radial_width * (jnp.arange(NB, dtype=jnp.float32) + 1.0)
            radial = jnp.exp(-jnp.square((dist[:, :, None] - centres) / radial_width))
            radial_parts = split2(radial.reshape(atoms * fanout, NB))
            unit = delta / dist[:, :, None]
            u_hi, u_lo = split2(unit)
            unit_w = jnp.concatenate(
                [jnp.ones((atoms, fanout, 1), jnp.bfloat16), u_hi, u_lo, jnp.zeros((atoms, fanout, 1), jnp.bfloat16)],
                axis=-1,
            )
        hidden = gnn_layer(
            hidden,
            gathered,
            unit_w,
            radial_parts,
            w_self[layer_idx],
            w_nbr[layer_idx],
            w_rad[layer_idx],
            w_msg[layer_idx],
            w_out[layer_idx],
            norm_gain[layer_idx],
        )
    flat_hidden = hidden.astype(jnp.float32)
    readout = jnp.dot(flat_hidden, jnp.stack([w_energy, w_charge], axis=1), precision=highest)
    energy_ml = readout[:, 0]
    charge = readout[:, 1]
    capacity = max(2, 2 * atoms // devices) * n_pme
    bx = GX // n_dom
    by = GY // n_pme
    xps = GX // devices
    dest_owner = owner[:, 0]
    grid_x = dest_owner // n_pme * bx + cell // (by * GZ)
    grid_y = dest_owner % n_pme * by + cell // GZ % by
    grid_z = cell % GZ
    dest = grid_x // xps
    slab_cell = (grid_y * xps + grid_x % xps) * GZ + grid_z
    matches = (dest[:, None] == jnp.arange(devices, dtype=jnp.int32)[None, :]).astype(jnp.int32)
    slot = jnp.sum((jnp.cumsum(matches, axis=0) - matches) * matches, axis=1)
    where_to = dest * capacity + slot
    payload = jnp.stack([charge, slab_cell.astype(jnp.float32)], axis=1)
    outgoing = jnp.zeros((devices * capacity, 2), jnp.float32).at[where_to].set(payload)
    incoming = lax.all_to_all(outgoing, AXES, 0, 0, tiled=True)
    cells_here = incoming[:, 1].astype(jnp.int32)
    rows_here = cells_here // GZ
    z_here = cells_here % GZ
    n_rows = GY * xps
    oh_rows = (jnp.arange(n_rows, dtype=jnp.int32)[:, None] == rows_here[None, :]).astype(jnp.bfloat16)
    oh_z = z_here[:, None] == jnp.arange(GZ, dtype=jnp.int32)[None, :]
    q_hi, q_lo = split2(incoming[:, 0])
    zero = jnp.zeros((), jnp.bfloat16)
    qz = jnp.concatenate(
        [jnp.where(oh_z, q_hi[:, None], zero), jnp.where(oh_z, q_lo[:, None], zero)], axis=1
    )
    dparts = mm(oh_rows, qz)
    density = dparts[:, :GZ] + dparts[:, GZ:]
    dev_index = lax.axis_index("dom") * n_pme + lax.axis_index("pme")
    spectrum_rows = solve_field(density, devices, dev_index)
    picked = lax.dot_general(
        oh_rows, spectrum_rows, (((0,), (0,)), ((), ())), preferred_element_type=jnp.float32
    )
    cz, sz = dft_pair(GZ)
    ez_t = jnp.asarray(np.concatenate([cz, -sz], axis=1), jnp.bfloat16)
    ez_rows = mm(oh_z.astype(jnp.bfloat16), ez_t)
    sampled = jnp.sum(picked * ez_rows, axis=1)
    returned = lax.all_to_all(sampled, AXES, 0, 0, tiled=True)
    at_atoms = returned[where_to]
    energy_el = 0.5 * charge * at_atoms
    return (energy_ml, energy_el)


def solution(mesh):
    in_specs = (
        P(("dom", "pme"), None),
        P(None, ("dom", "pme")),
        P(("dom", "pme"), None),
        P(("dom", "pme"), None),
        P(("dom", "pme")),
        P(),
        P(),
        P(),
        P(),
        P(),
        P(),
        P(),
        P(),
    )
    out_specs = (P(("dom", "pme")), P(("dom", "pme")))
    return jax.shard_map(
        per_device, mesh=mesh, in_specs=in_specs, out_specs=out_specs, check_vma=False
    )
```

```python
import math

import jax
import jax.numpy as jnp
import numpy as np
from jax import lax
from jax.sharding import PartitionSpec as P

NB = 8
LAYERS = 2
GX = 256
GY = 256
GZ = 128


slab_depth = 3.0
radial_width = 0.75
ewald_beta = 1.2
norm_eps = 1e-05
highest = lax.Precision.HIGHEST
AXES = ("dom", "pme")


def to_bf16_exact(x):
    return lax.reduce_precision(x, exponent_bits=8, mantissa_bits=7)


def split2(x):
    hi = to_bf16_exact(x)
    lo = x - hi
    return hi.astype(jnp.bfloat16), lo.astype(jnp.bfloat16)


def split3(x):
    hi = to_bf16_exact(x)
    rest = x - hi
    mid = to_bf16_exact(rest)
    lo = rest - mid
    return hi.astype(jnp.bfloat16), mid.astype(jnp.bfloat16), lo.astype(jnp.bfloat16)


def halo(shard):
    devices = lax.axis_size(AXES)
    up = [(i, (i + 1) % devices) for i in range(devices)]
    down = [(j, i) for i, j in up]
    before = lax.ppermute(shard, AXES, up)
    after = lax.ppermute(shard, AXES, down)
    return jnp.concatenate([before, shard, after], axis=0)


def silu(x):
    return x * jax.nn.sigmoid(x)


def dft_pair(length):
    k = np.arange(length, dtype=np.int64)
    angle = (np.outer(k, k) % length).astype(np.float64) * (2.0 * math.pi / length)
    return np.cos(angle), np.sin(angle)


def wave_square(count, start, full):
    index = start + jnp.arange(count, dtype=jnp.int32)
    folded = jnp.where(index < full // 2, index, index - full).astype(jnp.float32)
    scaled = folded * (2.0 * math.pi / full)
    return scaled * scaled


def green(wave_x, wave_y, wave_z):
    ksq = wave_x[:, None, None] + wave_y[None, :, None] + wave_z[None, None, :]
    safe = jnp.where(ksq > 0, ksq, 1.0)
    return jnp.where(
        ksq > 0, 4.0 * math.pi * jnp.exp(-ksq / (4.0 * ewald_beta * ewald_beta)) / safe, 0.0
    )


def mm(a, b):
    return jnp.dot(a, b, preferred_element_type=jnp.float32)


def combine(p, forward):
    rows, cols = p.shape
    c, s = p[: rows // 2], p[rows // 2 :]
    c_re, c_im = c[:, : cols // 2], c[:, cols // 2 :]
    s_re, s_im = s[:, : cols // 2], s[:, cols // 2 :]
    if forward:
        return c_re + s_im, c_im - s_re
    return c_re - s_im, c_im + s_re


def regroup(parts, split, perm, shape, axis):
    moved = [x.astype(jnp.bfloat16).reshape(split).transpose(perm).reshape(shape) for x in parts]
    return jnp.concatenate(moved, axis=axis)


def solve_field(density, devices, dev_index):
    xps = GX // devices
    kyls = GY // devices
    cz, sz = dft_pair(GZ)
    fa = jnp.asarray(np.concatenate([cz, -sz], axis=1), jnp.bfloat16)
    d_hi, d_lo = split2(density)
    a = mm(d_hi, fa) + mm(d_lo, fa)
    a_re = a[:, :GZ].reshape(GY, xps, GZ).astype(jnp.bfloat16)
    a_im = a[:, GZ:].reshape(GY, xps, GZ).astype(jnp.bfloat16)
    cy, sy = dft_pair(GY)
    fy = jnp.asarray(np.concatenate([cy, sy], axis=0), jnp.bfloat16)
    fyb = jnp.asarray(np.block([[cy, sy], [-sy, cy]]), jnp.bfloat16)
    yy = jnp.einsum(
        "ky,ypz->kpz", fyb, jnp.concatenate([a_re, a_im], axis=0), preferred_element_type=jnp.float32
    )
    y_re = yy[:GY]
    y_im = yy[GY:]

    def by_dest(t):
        return t.reshape(devices, kyls, xps, GZ).transpose(0, 2, 1, 3)

    sent = jnp.stack([by_dest(y_re), by_dest(y_im)], axis=2).astype(jnp.bfloat16)
    r2 = lax.all_to_all(sent, AXES, 0, 0, tiled=True)
    cx, sx = dft_pair(GX)
    fx = jnp.asarray(np.concatenate([cx, sx], axis=0), jnp.bfloat16)
    p2 = jnp.einsum("kpx,pxrjz->krjz", fx.reshape(2 * GX, devices, xps), r2, preferred_element_type=jnp.float32)
    z_re = p2[:GX, 0] + p2[GX:, 1]
    z_im = p2[:GX, 1] - p2[GX:, 0]
    kernel = green(
        wave_square(GX, 0, GX), wave_square(kyls, dev_index * kyls, GY), wave_square(GZ, 0, GZ)
    ) * (1.0 / (GX * GY * GZ))
    z = jnp.stack([z_re * kernel, z_im * kernel], axis=1).astype(jnp.bfloat16)
    p3 = jnp.einsum("xk,krjz->xrjz", fx, z, preferred_element_type=jnp.float32)
    w_re = p3[:GX, 0] - p3[GX:, 1]
    w_im = p3[:GX, 1] + p3[GX:, 0]
    back = jnp.stack(
        [w_re.reshape(devices, xps, kyls, GZ), w_im.reshape(devices, xps, kyls, GZ)], axis=2
    ).astype(jnp.bfloat16)
    r3 = lax.all_to_all(back, AXES, 0, 0, tiled=True)
    r3 = r3.transpose(2, 1, 0, 3, 4).reshape(2 * xps, GY, GZ)
    p4 = jnp.einsum("yk,bkz->ybz", fy, r3, preferred_element_type=jnp.float32).reshape(2 * GY, 2, xps, GZ)
    v_re = p4[:GY, 0] - p4[GY:, 1]
    v_im = p4[:GY, 1] + p4[GY:, 0]
    return jnp.concatenate([v_re, v_im], axis=-1).reshape(GY * xps, 2 * GZ).astype(jnp.bfloat16)


def gnn_layer(hidden, gathered, unit_w, radial_parts, w_self, w_nbr, w_rad, w_msg, w_out, gain):
    atoms, width = hidden.shape
    fanout = gathered.shape[0] // atoms
    gathered_h = gathered[:, :width]
    r_hi, r_lo = radial_parts
    w_hi, w_lo = split2(w_rad)
    lhs = jnp.concatenate([gathered_h, r_hi, r_lo, r_hi], axis=1)
    rhs = jnp.concatenate([w_nbr, w_hi, w_hi, w_lo], axis=0)
    own_term = mm(hidden, w_self)
    pre = mm(lhs, rhs).reshape(atoms, fanout, width) + own_term[:, None, :]
    message = silu(pre).astype(jnp.bfloat16)
    parts = jnp.einsum("akc,akf->acf", unit_w, message, preferred_element_type=jnp.float32)
    sums = jnp.concatenate([parts[:, :1], parts[:, 1:4] + parts[:, 4:7]], axis=1)
    s_hi, s_lo = split2(sums.reshape(atoms * 4, width))
    mixed = (mm(s_hi, w_msg) + mm(s_lo, w_msg)).reshape(atoms, 4, width) / fanout
    total = mixed[:, 0] + jnp.sum(mixed[:, 1:] * mixed[:, 1:], axis=1)
    normed = total * lax.rsqrt(jnp.mean(total * total, axis=-1, keepdims=True) + norm_eps) * gain
    active = silu(normed).astype(jnp.bfloat16)
    update = mm(active, w_out)
    return (hidden.astype(jnp.float32) + update).astype(jnp.bfloat16)


def per_device(
    feats,
    coords,
    nbrs,
    owner,
    cell,
    w_self,
    w_nbr,
    w_rad,
    w_msg,
    w_out,
    norm_gain,
    w_charge,
    w_energy,
):
    atoms, width = feats.shape
    fanout = nbrs.shape[1]
    n_dom = lax.axis_size("dom")
    n_pme = lax.axis_size("pme")
    devices = n_dom * n_pme
    wide_rows = 3 * atoms
    pos_own = coords.T
    p_hi, p_mid, p_lo = split3(pos_own)
    wide0 = halo(jnp.concatenate([feats, p_hi, p_mid, p_lo], axis=1))
    flat_nbrs = nbrs.reshape(-1)
    onehot = (flat_nbrs[:, None] == jnp.arange(wide_rows, dtype=jnp.int32)[None, :]).astype(
        jnp.bfloat16
    )
    hidden = feats
    unit_w = None
    radial_parts = None
    for layer_idx in range(LAYERS):
        table = wide0 if layer_idx == 0 else halo(hidden)
        gathered = jnp.dot(onehot, table, preferred_element_type=jnp.bfloat16)
        if layer_idx == 0:
            gp = gathered[:, width:].astype(jnp.float32)
            pos_j = gp[:, 0:3] + gp[:, 3:6] + gp[:, 6:9]
            lift = jnp.where(flat_nbrs < atoms, -slab_depth, jnp.where(flat_nbrs >= 2 * atoms, slab_depth, 0.0))
            pos_j = pos_j + jnp.where(jnp.arange(3, dtype=jnp.int32) == 2, 1.0, 0.0)[None, :] * lift[:, None]
            delta = pos_j.reshape(atoms, fanout, 3) - pos_own[:, None, :]
            dist = jnp.sqrt(jnp.sum(delta * delta, axis=-1) + 1.0)
            centres = radial_width * (jnp.arange(NB, dtype=jnp.float32) + 1.0)
            radial = jnp.exp(-jnp.square((dist[:, :, None] - centres) / radial_width))
            radial_parts = split2(radial.reshape(atoms * fanout, NB))
            unit = delta / dist[:, :, None]
            u_hi, u_lo = split2(unit)
            unit_w = jnp.concatenate(
                [jnp.ones((atoms, fanout, 1), jnp.bfloat16), u_hi, u_lo, jnp.zeros((atoms, fanout, 1), jnp.bfloat16)],
                axis=-1,
            )
        hidden = gnn_layer(
            hidden,
            gathered,
            unit_w,
            radial_parts,
            w_self[layer_idx],
            w_nbr[layer_idx],
            w_rad[layer_idx],
            w_msg[layer_idx],
            w_out[layer_idx],
            norm_gain[layer_idx],
        )
    flat_hidden = hidden.astype(jnp.float32)
    readout = jnp.dot(flat_hidden, jnp.stack([w_energy, w_charge], axis=1), precision=highest)
    energy_ml = readout[:, 0]
    charge = readout[:, 1]
    capacity = max(2, 2 * atoms // devices) * n_pme
    bx = GX // n_dom
    by = GY // n_pme
    xps = GX // devices
    dest_owner = owner[:, 0]
    grid_x = dest_owner // n_pme * bx + cell // (by * GZ)
    grid_y = dest_owner % n_pme * by + cell // GZ % by
    grid_z = cell % GZ
    dest = grid_x // xps
    slab_cell = (grid_y * xps + grid_x % xps) * GZ + grid_z
    matches = (dest[:, None] == jnp.arange(devices, dtype=jnp.int32)[None, :]).astype(jnp.int32)
    slot = jnp.sum((jnp.cumsum(matches, axis=0) - matches) * matches, axis=1)
    where_to = dest * capacity + slot
    payload = jnp.stack([charge, slab_cell.astype(jnp.float32)], axis=1)
    outgoing = jnp.zeros((devices * capacity, 2), jnp.float32).at[where_to].set(payload)
    incoming = lax.all_to_all(outgoing, AXES, 0, 0, tiled=True)
    cells_here = incoming[:, 1].astype(jnp.int32)
    rows_here = cells_here // GZ
    z_here = cells_here % GZ
    n_rows = GY * xps
    oh_rows = (jnp.arange(n_rows, dtype=jnp.int32)[:, None] == rows_here[None, :]).astype(jnp.bfloat16)
    oh_z = z_here[:, None] == jnp.arange(GZ, dtype=jnp.int32)[None, :]
    q_hi, q_lo = split2(incoming[:, 0])
    zero = jnp.zeros((), jnp.bfloat16)
    qz = jnp.concatenate(
        [jnp.where(oh_z, q_hi[:, None], zero), jnp.where(oh_z, q_lo[:, None], zero)], axis=1
    )
    dparts = mm(oh_rows, qz)
    density = dparts[:, :GZ] + dparts[:, GZ:]
    dev_index = lax.axis_index("dom") * n_pme + lax.axis_index("pme")
    spectrum_rows = solve_field(density, devices, dev_index)
    picked = lax.dot_general(
        oh_rows, spectrum_rows, (((0,), (0,)), ((), ())), preferred_element_type=jnp.float32
    )
    cz, sz = dft_pair(GZ)
    ez_t = jnp.asarray(np.concatenate([cz, -sz], axis=1), jnp.bfloat16)
    ez_rows = mm(oh_z.astype(jnp.bfloat16), ez_t)
    sampled = jnp.sum(picked * ez_rows, axis=1)
    returned = lax.all_to_all(sampled, AXES, 0, 0, tiled=True)
    at_atoms = returned[where_to]
    energy_el = 0.5 * charge * at_atoms
    return (energy_ml, energy_el)


def solution(mesh):
    in_specs = (
        P(("dom", "pme"), None),
        P(None, ("dom", "pme")),
        P(("dom", "pme"), None),
        P(("dom", "pme"), None),
        P(("dom", "pme")),
        P(),
        P(),
        P(),
        P(),
        P(),
        P(),
        P(),
        P(),
    )
    out_specs = (P(("dom", "pme")), P(("dom", "pme")))
    return jax.shard_map(
        per_device, mesh=mesh, in_specs=in_specs, out_specs=out_specs, check_vma=False
    )
```

```python
import math

import jax
import jax.numpy as jnp
import numpy as np
from jax import lax
from jax.sharding import PartitionSpec as P

NB = 8
LAYERS = 2
GX = 256
GY = 256
GZ = 128


slab_depth = 3.0
radial_width = 0.75
ewald_beta = 1.2
norm_eps = 1e-05
highest = lax.Precision.HIGHEST
AXES = ("dom", "pme")


def to_bf16_exact(x):
    return lax.reduce_precision(x, exponent_bits=8, mantissa_bits=7)


def split2(x):
    hi = to_bf16_exact(x)
    lo = x - hi
    return hi.astype(jnp.bfloat16), lo.astype(jnp.bfloat16)


def split3(x):
    hi = to_bf16_exact(x)
    rest = x - hi
    mid = to_bf16_exact(rest)
    lo = rest - mid
    return hi.astype(jnp.bfloat16), mid.astype(jnp.bfloat16), lo.astype(jnp.bfloat16)


def halo(shard):
    devices = lax.axis_size(AXES)
    up = [(i, (i + 1) % devices) for i in range(devices)]
    down = [(j, i) for i, j in up]
    before = lax.ppermute(shard, AXES, up)
    after = lax.ppermute(shard, AXES, down)
    return jnp.concatenate([before, shard, after], axis=0)


def silu(x):
    return x * jax.nn.sigmoid(x)


def dft_pair(length):
    k = jnp.arange(length, dtype=jnp.int32)
    angle = (k[:, None] * k[None, :] % length).astype(jnp.float32) * (2.0 * math.pi / length)
    return jnp.cos(angle), jnp.sin(angle)


def wave_square(count, start, full):
    index = start + jnp.arange(count, dtype=jnp.int32)
    folded = jnp.where(index < full // 2, index, index - full).astype(jnp.float32)
    scaled = folded * (2.0 * math.pi / full)
    return scaled * scaled


def green(wave_x, wave_y, wave_z):
    ksq = wave_x[:, None, None] + wave_y[None, :, None] + wave_z[None, None, :]
    safe = jnp.where(ksq > 0, ksq, 1.0)
    return jnp.where(
        ksq > 0, 4.0 * math.pi * jnp.exp(-ksq / (4.0 * ewald_beta * ewald_beta)) / safe, 0.0
    )


def mm(a, b):
    return jnp.dot(a, b, preferred_element_type=jnp.float32)


def combine(p, forward):
    rows, cols = p.shape
    c, s = p[: rows // 2], p[rows // 2 :]
    c_re, c_im = c[:, : cols // 2], c[:, cols // 2 :]
    s_re, s_im = s[:, : cols // 2], s[:, cols // 2 :]
    if forward:
        return c_re + s_im, c_im - s_re
    return c_re - s_im, c_im + s_re


def regroup(parts, split, perm, shape, axis):
    moved = [x.astype(jnp.bfloat16).reshape(split).transpose(perm).reshape(shape) for x in parts]
    return jnp.concatenate(moved, axis=axis)


def solve_field(density, devices, dev_index):
    xps = GX // devices
    kyls = GY // devices
    cz, sz = dft_pair(GZ)
    fa = jnp.asarray(jnp.concatenate([cz, -sz], axis=1), jnp.bfloat16)
    d_hi, d_lo = split2(density)
    a = mm(d_hi, fa) + mm(d_lo, fa)
    a_re = a[:, :GZ].reshape(GY, xps, GZ).astype(jnp.bfloat16)
    a_im = a[:, GZ:].reshape(GY, xps, GZ).astype(jnp.bfloat16)
    cy, sy = dft_pair(GY)
    fy = jnp.asarray(jnp.concatenate([cy, sy], axis=0), jnp.bfloat16)
    p = jnp.einsum("ky,ypz->kpz", fy, a_re, preferred_element_type=jnp.float32)
    q = jnp.einsum("ky,ypz->kpz", fy, a_im, preferred_element_type=jnp.float32)
    y_re = p[:GY] + q[GY:]
    y_im = q[:GY] - p[GY:]

    def by_dest(t):
        return t.reshape(devices, kyls, xps, GZ).transpose(0, 2, 1, 3)

    sent = jnp.stack([by_dest(y_re), by_dest(y_im)], axis=2).astype(jnp.bfloat16)
    r2 = lax.all_to_all(sent, AXES, 0, 0, tiled=True)
    cx, sx = dft_pair(GX)
    fx = jnp.asarray(jnp.concatenate([cx, sx], axis=0), jnp.bfloat16)
    p2 = jnp.einsum("kpx,pxrjz->krjz", fx.reshape(2 * GX, devices, xps), r2, preferred_element_type=jnp.float32)
    z_re = p2[:GX, 0] + p2[GX:, 1]
    z_im = p2[:GX, 1] - p2[GX:, 0]
    kernel = green(
        wave_square(GX, 0, GX), wave_square(kyls, dev_index * kyls, GY), wave_square(GZ, 0, GZ)
    ) * (1.0 / (GX * GY * GZ))
    z = jnp.stack([z_re * kernel, z_im * kernel], axis=1).astype(jnp.bfloat16)
    p3 = jnp.einsum("xk,krjz->xrjz", fx, z, preferred_element_type=jnp.float32)
    w_re = p3[:GX, 0] - p3[GX:, 1]
    w_im = p3[:GX, 1] + p3[GX:, 0]
    back = jnp.stack(
        [w_re.reshape(devices, xps, kyls, GZ), w_im.reshape(devices, xps, kyls, GZ)], axis=2
    ).astype(jnp.bfloat16)
    r3 = lax.all_to_all(back, AXES, 0, 0, tiled=True)
    r3 = r3.transpose(2, 1, 0, 3, 4).reshape(2 * xps, GY, GZ)
    p4 = jnp.einsum("yk,bkz->ybz", fy, r3, preferred_element_type=jnp.float32).reshape(2 * GY, 2, xps, GZ)
    v_re = p4[:GY, 0] - p4[GY:, 1]
    v_im = p4[:GY, 1] + p4[GY:, 0]
    return jnp.concatenate([v_re, v_im], axis=-1).reshape(GY * xps, 2 * GZ).astype(jnp.bfloat16)


def gnn_layer(hidden, gathered, unit_w, radial_parts, w_self, w_nbr, w_rad, w_msg, w_out, gain):
    atoms, width = hidden.shape
    fanout = gathered.shape[0] // atoms
    gathered_h = gathered[:, :width]
    r_hi, r_lo = radial_parts
    w_hi, w_lo = split2(w_rad)
    lhs = jnp.concatenate([gathered_h, r_hi, r_lo, r_hi], axis=1)
    rhs = jnp.concatenate([w_nbr, w_hi, w_hi, w_lo], axis=0)
    own_term = mm(hidden, w_self)
    pre = mm(lhs, rhs).reshape(atoms, fanout, width) + own_term[:, None, :]
    message = silu(pre).astype(jnp.bfloat16)
    parts = jnp.einsum("akc,akf->acf", unit_w, message, preferred_element_type=jnp.float32)
    sums = jnp.concatenate([parts[:, :1], parts[:, 1:4] + parts[:, 4:7]], axis=1)
    s_hi, s_lo = split2(sums.reshape(atoms * 4, width))
    mixed = (mm(s_hi, w_msg) + mm(s_lo, w_msg)).reshape(atoms, 4, width) / fanout
    total = mixed[:, 0] + jnp.sum(mixed[:, 1:] * mixed[:, 1:], axis=1)
    normed = total * lax.rsqrt(jnp.mean(total * total, axis=-1, keepdims=True) + norm_eps) * gain
    active = silu(normed).astype(jnp.bfloat16)
    update = mm(active, w_out)
    return (hidden.astype(jnp.float32) + update).astype(jnp.bfloat16)


def per_device(
    feats,
    coords,
    nbrs,
    owner,
    cell,
    w_self,
    w_nbr,
    w_rad,
    w_msg,
    w_out,
    norm_gain,
    w_charge,
    w_energy,
):
    atoms, width = feats.shape
    fanout = nbrs.shape[1]
    n_dom = lax.axis_size("dom")
    n_pme = lax.axis_size("pme")
    devices = n_dom * n_pme
    wide_rows = 3 * atoms
    pos_own = coords.T
    p_hi, p_mid, p_lo = split3(pos_own)
    wide0 = halo(jnp.concatenate([feats, p_hi, p_mid, p_lo], axis=1))
    flat_nbrs = nbrs.reshape(-1)
    onehot = (flat_nbrs[:, None] == jnp.arange(wide_rows, dtype=jnp.int32)[None, :]).astype(
        jnp.bfloat16
    )
    hidden = feats
    unit_w = None
    radial_parts = None
    for layer_idx in range(LAYERS):
        table = wide0 if layer_idx == 0 else halo(hidden)
        gathered = jnp.dot(onehot, table, preferred_element_type=jnp.bfloat16)
        if layer_idx == 0:
            gp = gathered[:, width:].astype(jnp.float32)
            pos_j = gp[:, 0:3] + gp[:, 3:6] + gp[:, 6:9]
            lift = jnp.where(flat_nbrs < atoms, -slab_depth, jnp.where(flat_nbrs >= 2 * atoms, slab_depth, 0.0))
            pos_j = pos_j + jnp.where(jnp.arange(3, dtype=jnp.int32) == 2, 1.0, 0.0)[None, :] * lift[:, None]
            delta = pos_j.reshape(atoms, fanout, 3) - pos_own[:, None, :]
            dist = jnp.sqrt(jnp.sum(delta * delta, axis=-1) + 1.0)
            centres = radial_width * (jnp.arange(NB, dtype=jnp.float32) + 1.0)
            radial = jnp.exp(-jnp.square((dist[:, :, None] - centres) / radial_width))
            radial_parts = split2(radial.reshape(atoms * fanout, NB))
            unit = delta / dist[:, :, None]
            u_hi, u_lo = split2(unit)
            unit_w = jnp.concatenate(
                [jnp.ones((atoms, fanout, 1), jnp.bfloat16), u_hi, u_lo, jnp.zeros((atoms, fanout, 1), jnp.bfloat16)],
                axis=-1,
            )
        hidden = gnn_layer(
            hidden,
            gathered,
            unit_w,
            radial_parts,
            w_self[layer_idx],
            w_nbr[layer_idx],
            w_rad[layer_idx],
            w_msg[layer_idx],
            w_out[layer_idx],
            norm_gain[layer_idx],
        )
    flat_hidden = hidden.astype(jnp.float32)
    readout = jnp.dot(flat_hidden, jnp.stack([w_energy, w_charge], axis=1), precision=highest)
    energy_ml = readout[:, 0]
    charge = readout[:, 1]
    capacity = max(2, 2 * atoms // devices) * n_pme
    bx = GX // n_dom
    by = GY // n_pme
    xps = GX // devices
    dest_owner = owner[:, 0]
    grid_x = dest_owner // n_pme * bx + cell // (by * GZ)
    grid_y = dest_owner % n_pme * by + cell // GZ % by
    grid_z = cell % GZ
    dest = grid_x // xps
    slab_cell = (grid_y * xps + grid_x % xps) * GZ + grid_z
    matches = (dest[:, None] == jnp.arange(devices, dtype=jnp.int32)[None, :]).astype(jnp.int32)
    slot = jnp.sum((jnp.cumsum(matches, axis=0) - matches) * matches, axis=1)
    where_to = dest * capacity + slot
    payload = jnp.stack([charge, slab_cell.astype(jnp.float32)], axis=1)
    outgoing = jnp.zeros((devices * capacity, 2), jnp.float32).at[where_to].set(payload)
    incoming = lax.all_to_all(outgoing, AXES, 0, 0, tiled=True)
    cells_here = incoming[:, 1].astype(jnp.int32)
    rows_here = cells_here // GZ
    z_here = cells_here % GZ
    n_rows = GY * xps
    oh_rows = (jnp.arange(n_rows, dtype=jnp.int32)[:, None] == rows_here[None, :]).astype(jnp.bfloat16)
    oh_z = z_here[:, None] == jnp.arange(GZ, dtype=jnp.int32)[None, :]
    q_hi, q_lo = split2(incoming[:, 0])
    zero = jnp.zeros((), jnp.bfloat16)
    qz = jnp.concatenate(
        [jnp.where(oh_z, q_hi[:, None], zero), jnp.where(oh_z, q_lo[:, None], zero)], axis=1
    )
    dparts = mm(oh_rows, qz)
    density = dparts[:, :GZ] + dparts[:, GZ:]
    dev_index = lax.axis_index("dom") * n_pme + lax.axis_index("pme")
    spectrum_rows = solve_field(density, devices, dev_index)
    picked = lax.dot_general(
        oh_rows, spectrum_rows, (((0,), (0,)), ((), ())), preferred_element_type=jnp.float32
    )
    cz, sz = dft_pair(GZ)
    ez_t = jnp.asarray(jnp.concatenate([cz, -sz], axis=1), jnp.bfloat16)
    ez_rows = mm(oh_z.astype(jnp.bfloat16), ez_t)
    sampled = jnp.sum(picked * ez_rows, axis=1)
    returned = lax.all_to_all(sampled, AXES, 0, 0, tiled=True)
    at_atoms = returned[where_to]
    energy_el = 0.5 * charge * at_atoms
    return (energy_ml, energy_el)


def solution(mesh):
    in_specs = (
        P(("dom", "pme"), None),
        P(None, ("dom", "pme")),
        P(("dom", "pme"), None),
        P(("dom", "pme"), None),
        P(("dom", "pme")),
        P(),
        P(),
        P(),
        P(),
        P(),
        P(),
        P(),
        P(),
    )
    out_specs = (P(("dom", "pme")), P(("dom", "pme")))
    return jax.shard_map(
        per_device, mesh=mesh, in_specs=in_specs, out_specs=out_specs, check_vma=False
    )
```

```python
import math

import jax
import jax.numpy as jnp
import numpy as np
from jax import lax
from jax.sharding import PartitionSpec as P

NB = 8
LAYERS = 2
GX = 256
GY = 256
GZ = 128


slab_depth = 3.0
radial_width = 0.75
ewald_beta = 1.2
norm_eps = 1e-05
highest = lax.Precision.HIGHEST
AXES = ("dom", "pme")


def to_bf16_exact(x):
    return lax.reduce_precision(x, exponent_bits=8, mantissa_bits=7)


def split2(x):
    hi = to_bf16_exact(x)
    lo = x - hi
    return hi.astype(jnp.bfloat16), lo.astype(jnp.bfloat16)


def split3(x):
    hi = to_bf16_exact(x)
    rest = x - hi
    mid = to_bf16_exact(rest)
    lo = rest - mid
    return hi.astype(jnp.bfloat16), mid.astype(jnp.bfloat16), lo.astype(jnp.bfloat16)


def halo(shard):
    devices = lax.axis_size(AXES)
    up = [(i, (i + 1) % devices) for i in range(devices)]
    down = [(j, i) for i, j in up]
    before = lax.ppermute(shard, AXES, up)
    after = lax.ppermute(shard, AXES, down)
    return jnp.concatenate([before, shard, after], axis=0)


def silu(x):
    return x * jax.nn.sigmoid(x)


def dft_pair(length):
    k = np.arange(length, dtype=np.int64)
    angle = (np.outer(k, k) % length).astype(np.float64) * (2.0 * math.pi / length)
    return np.cos(angle), np.sin(angle)


def wave_square(count, start, full):
    index = start + jnp.arange(count, dtype=jnp.int32)
    folded = jnp.where(index < full // 2, index, index - full).astype(jnp.float32)
    scaled = folded * (2.0 * math.pi / full)
    return scaled * scaled


def green(wave_x, wave_y, wave_z):
    ksq = wave_x[:, None, None] + wave_y[None, :, None] + wave_z[None, None, :]
    safe = jnp.where(ksq > 0, ksq, 1.0)
    return jnp.where(
        ksq > 0, 4.0 * math.pi * jnp.exp(-ksq / (4.0 * ewald_beta * ewald_beta)) / safe, 0.0
    )


def mm(a, b):
    return jnp.dot(a, b, preferred_element_type=jnp.float32)


def combine(p, forward):
    rows, cols = p.shape
    c, s = p[: rows // 2], p[rows // 2 :]
    c_re, c_im = c[:, : cols // 2], c[:, cols // 2 :]
    s_re, s_im = s[:, : cols // 2], s[:, cols // 2 :]
    if forward:
        return c_re + s_im, c_im - s_re
    return c_re - s_im, c_im + s_re


def regroup(parts, split, perm, shape, axis):
    moved = [x.astype(jnp.bfloat16).reshape(split).transpose(perm).reshape(shape) for x in parts]
    return jnp.concatenate(moved, axis=axis)


def solve_field(density, devices, dev_index):
    xps = GX // devices
    kyls = GY // devices
    cz, sz = dft_pair(GZ)
    fa = jnp.asarray(np.concatenate([cz, -sz], axis=1), jnp.bfloat16)
    d_hi, d_lo = split2(density)
    a = mm(d_hi, fa) + mm(d_lo, fa)
    a_re = a[:, :GZ].reshape(GY, xps, GZ).astype(jnp.bfloat16)
    a_im = a[:, GZ:].reshape(GY, xps, GZ).astype(jnp.bfloat16)
    cy, sy = dft_pair(GY)
    fy = jnp.asarray(np.concatenate([cy, sy], axis=0), jnp.bfloat16)
    p = jnp.einsum("ky,ypz->kpz", fy, a_re, preferred_element_type=jnp.float32)
    q = jnp.einsum("ky,ypz->kpz", fy, a_im, preferred_element_type=jnp.float32)
    y_re = p[:GY] + q[GY:]
    y_im = q[:GY] - p[GY:]

    def by_dest(t):
        return t.reshape(devices, kyls, xps, GZ).transpose(0, 2, 1, 3)

    sent = jnp.stack([by_dest(y_re), by_dest(y_im)], axis=2).astype(jnp.bfloat16)
    r2 = lax.all_to_all(sent, AXES, 0, 0, tiled=True)
    cx, sx = dft_pair(GX)
    fx = jnp.asarray(np.concatenate([cx, sx], axis=0), jnp.bfloat16)
    p2 = jnp.einsum("kpx,pxrjz->krjz", fx.reshape(2 * GX, devices, xps), r2, preferred_element_type=jnp.float32)
    z_re = p2[:GX, 0] + p2[GX:, 1]
    z_im = p2[:GX, 1] - p2[GX:, 0]
    kernel = green(
        wave_square(GX, 0, GX), wave_square(kyls, dev_index * kyls, GY), wave_square(GZ, 0, GZ)
    ) * (1.0 / (GX * GY * GZ))
    z = jnp.stack([z_re * kernel, z_im * kernel], axis=1).astype(jnp.bfloat16)
    p3 = jnp.einsum("xk,krjz->xrjz", fx, z, preferred_element_type=jnp.float32)
    w_re = p3[:GX, 0] - p3[GX:, 1]
    w_im = p3[:GX, 1] + p3[GX:, 0]
    back = jnp.stack(
        [w_re.reshape(devices, xps, kyls, GZ), w_im.reshape(devices, xps, kyls, GZ)], axis=2
    ).astype(jnp.bfloat16)
    r3 = lax.all_to_all(back, AXES, 0, 0, tiled=True)
    r3 = r3.transpose(2, 1, 0, 3, 4).reshape(2 * xps, GY, GZ)
    p4 = jnp.einsum("yk,bkz->ybz", fy, r3, preferred_element_type=jnp.float32).reshape(2 * GY, 2, xps, GZ)
    v_re = p4[:GY, 0] - p4[GY:, 1]
    v_im = p4[:GY, 1] + p4[GY:, 0]
    return jnp.concatenate([v_re, v_im], axis=-1).reshape(GY * xps, 2 * GZ).astype(jnp.bfloat16)


def gnn_layer(hidden, gathered, unit_w, radial_parts, w_self, w_nbr, w_rad, w_msg, w_out, gain):
    atoms, width = hidden.shape
    fanout = gathered.shape[0] // atoms
    gathered_h = gathered[:, :width]
    r_hi, r_lo = radial_parts
    w_hi, w_lo = split2(w_rad)
    lhs = jnp.concatenate([gathered_h, r_hi, r_lo, r_hi], axis=1)
    rhs = jnp.concatenate([w_nbr, w_hi, w_hi, w_lo], axis=0)
    own_term = mm(hidden, w_self)
    pre = mm(lhs, rhs).reshape(atoms, fanout, width) + own_term[:, None, :]
    message = silu(pre).astype(jnp.bfloat16)
    parts = jnp.einsum("akc,akf->acf", unit_w, message, preferred_element_type=jnp.float32)
    sums = jnp.concatenate([parts[:, :1], parts[:, 1:4] + parts[:, 4:7]], axis=1)
    s_hi, s_lo = split2(sums.reshape(atoms * 4, width))
    mixed = (mm(s_hi, w_msg) + mm(s_lo, w_msg)).reshape(atoms, 4, width) / fanout
    total = mixed[:, 0] + jnp.sum(mixed[:, 1:] * mixed[:, 1:], axis=1)
    normed = total * lax.rsqrt(jnp.mean(total * total, axis=-1, keepdims=True) + norm_eps) * gain
    active = silu(normed).astype(jnp.bfloat16)
    update = mm(active, w_out)
    return (hidden.astype(jnp.float32) + update).astype(jnp.bfloat16)


def per_device(
    feats,
    coords,
    nbrs,
    owner,
    cell,
    w_self,
    w_nbr,
    w_rad,
    w_msg,
    w_out,
    norm_gain,
    w_charge,
    w_energy,
):
    atoms, width = feats.shape
    fanout = nbrs.shape[1]
    n_dom = lax.axis_size("dom")
    n_pme = lax.axis_size("pme")
    devices = n_dom * n_pme
    wide_rows = 3 * atoms
    pos_own = coords.T
    p_hi, p_mid, p_lo = split3(pos_own)
    wide0 = halo(jnp.concatenate([feats, p_hi, p_mid, p_lo], axis=1))
    flat_nbrs = nbrs.reshape(-1)
    def onehot_for(layer_idx):
        shifted = flat_nbrs + layer_idx * wide_rows
        rows = jnp.arange(wide_rows, dtype=jnp.int32) + layer_idx * wide_rows
        return (shifted[:, None] == rows[None, :]).astype(jnp.bfloat16)

    hidden = feats
    unit_w = None
    radial_parts = None
    for layer_idx in range(LAYERS):
        table = wide0 if layer_idx == 0 else halo(hidden)
        gathered = jnp.dot(onehot_for(layer_idx), table, preferred_element_type=jnp.bfloat16)
        if layer_idx == 0:
            gp = gathered[:, width:].astype(jnp.float32)
            pos_j = gp[:, 0:3] + gp[:, 3:6] + gp[:, 6:9]
            lift = jnp.where(flat_nbrs < atoms, -slab_depth, jnp.where(flat_nbrs >= 2 * atoms, slab_depth, 0.0))
            pos_j = pos_j + jnp.where(jnp.arange(3, dtype=jnp.int32) == 2, 1.0, 0.0)[None, :] * lift[:, None]
            delta = pos_j.reshape(atoms, fanout, 3) - pos_own[:, None, :]
            dist = jnp.sqrt(jnp.sum(delta * delta, axis=-1) + 1.0)
            centres = radial_width * (jnp.arange(NB, dtype=jnp.float32) + 1.0)
            radial = jnp.exp(-jnp.square((dist[:, :, None] - centres) / radial_width))
            radial_parts = split2(radial.reshape(atoms * fanout, NB))
            unit = delta / dist[:, :, None]
            u_hi, u_lo = split2(unit)
            unit_w = jnp.concatenate(
                [jnp.ones((atoms, fanout, 1), jnp.bfloat16), u_hi, u_lo, jnp.zeros((atoms, fanout, 1), jnp.bfloat16)],
                axis=-1,
            )
        hidden = gnn_layer(
            hidden,
            gathered,
            unit_w,
            radial_parts,
            w_self[layer_idx],
            w_nbr[layer_idx],
            w_rad[layer_idx],
            w_msg[layer_idx],
            w_out[layer_idx],
            norm_gain[layer_idx],
        )
    flat_hidden = hidden.astype(jnp.float32)
    readout = jnp.dot(flat_hidden, jnp.stack([w_energy, w_charge], axis=1), precision=highest)
    energy_ml = readout[:, 0]
    charge = readout[:, 1]
    capacity = max(2, 2 * atoms // devices) * n_pme
    bx = GX // n_dom
    by = GY // n_pme
    xps = GX // devices
    dest_owner = owner[:, 0]
    grid_x = dest_owner // n_pme * bx + cell // (by * GZ)
    grid_y = dest_owner % n_pme * by + cell // GZ % by
    grid_z = cell % GZ
    dest = grid_x // xps
    slab_cell = (grid_y * xps + grid_x % xps) * GZ + grid_z
    matches = (dest[:, None] == jnp.arange(devices, dtype=jnp.int32)[None, :]).astype(jnp.int32)
    slot = jnp.sum((jnp.cumsum(matches, axis=0) - matches) * matches, axis=1)
    where_to = dest * capacity + slot
    payload = jnp.stack([charge, slab_cell.astype(jnp.float32)], axis=1)
    outgoing = jnp.zeros((devices * capacity, 2), jnp.float32).at[where_to].set(payload)
    incoming = lax.all_to_all(outgoing, AXES, 0, 0, tiled=True)
    cells_here = incoming[:, 1].astype(jnp.int32)
    rows_here = cells_here // GZ
    z_here = cells_here % GZ
    n_rows = GY * xps
    oh_rows = (jnp.arange(n_rows, dtype=jnp.int32)[:, None] == rows_here[None, :]).astype(jnp.bfloat16)
    oh_z = z_here[:, None] == jnp.arange(GZ, dtype=jnp.int32)[None, :]
    q_hi, q_lo = split2(incoming[:, 0])
    zero = jnp.zeros((), jnp.bfloat16)
    qz = jnp.concatenate(
        [jnp.where(oh_z, q_hi[:, None], zero), jnp.where(oh_z, q_lo[:, None], zero)], axis=1
    )
    dparts = mm(oh_rows, qz)
    density = dparts[:, :GZ] + dparts[:, GZ:]
    dev_index = lax.axis_index("dom") * n_pme + lax.axis_index("pme")
    spectrum_rows = solve_field(density, devices, dev_index)
    picked = lax.dot_general(
        oh_rows, spectrum_rows, (((0,), (0,)), ((), ())), preferred_element_type=jnp.float32
    )
    cz, sz = dft_pair(GZ)
    ez_t = jnp.asarray(np.concatenate([cz, -sz], axis=1), jnp.bfloat16)
    ez_rows = mm(oh_z.astype(jnp.bfloat16), ez_t)
    sampled = jnp.sum(picked * ez_rows, axis=1)
    returned = lax.all_to_all(sampled, AXES, 0, 0, tiled=True)
    at_atoms = returned[where_to]
    energy_el = 0.5 * charge * at_atoms
    return (energy_ml, energy_el)


def solution(mesh):
    in_specs = (
        P(("dom", "pme"), None),
        P(None, ("dom", "pme")),
        P(("dom", "pme"), None),
        P(("dom", "pme"), None),
        P(("dom", "pme")),
        P(),
        P(),
        P(),
        P(),
        P(),
        P(),
        P(),
        P(),
    )
    out_specs = (P(("dom", "pme")), P(("dom", "pme")))
    return jax.shard_map(
        per_device, mesh=mesh, in_specs=in_specs, out_specs=out_specs, check_vma=False
    )
```

```python
import math

import jax
import jax.numpy as jnp
import numpy as np
from jax import lax
from jax.sharding import PartitionSpec as P

NB = 8
LAYERS = 2
GX = 256
GY = 256
GZ = 128


slab_depth = 3.0
radial_width = 0.75
ewald_beta = 1.2
norm_eps = 1e-05
highest = lax.Precision.HIGHEST
AXES = ("dom", "pme")


def to_bf16_exact(x):
    return lax.reduce_precision(x, exponent_bits=8, mantissa_bits=7)


def split2(x):
    hi = to_bf16_exact(x)
    lo = x - hi
    return hi.astype(jnp.bfloat16), lo.astype(jnp.bfloat16)


def split3(x):
    hi = to_bf16_exact(x)
    rest = x - hi
    mid = to_bf16_exact(rest)
    lo = rest - mid
    return hi.astype(jnp.bfloat16), mid.astype(jnp.bfloat16), lo.astype(jnp.bfloat16)


def halo(shard):
    devices = lax.axis_size(AXES)
    up = [(i, (i + 1) % devices) for i in range(devices)]
    down = [(j, i) for i, j in up]
    before = lax.ppermute(shard, AXES, up)
    after = lax.ppermute(shard, AXES, down)
    return jnp.concatenate([before, shard, after], axis=0)


def silu(x):
    return x * jax.nn.sigmoid(x)


def dft_pair(length):
    k = np.arange(length, dtype=np.int64)
    angle = (np.outer(k, k) % length).astype(np.float64) * (2.0 * math.pi / length)
    return np.cos(angle), np.sin(angle)


def wave_square(count, start, full):
    index = start + jnp.arange(count, dtype=jnp.int32)
    folded = jnp.where(index < full // 2, index, index - full).astype(jnp.float32)
    scaled = folded * (2.0 * math.pi / full)
    return scaled * scaled


def green(wave_x, wave_y, wave_z):
    ksq = wave_x[:, None, None] + wave_y[None, :, None] + wave_z[None, None, :]
    safe = jnp.where(ksq > 0, ksq, 1.0)
    return jnp.where(
        ksq > 0, 4.0 * math.pi * jnp.exp(-ksq / (4.0 * ewald_beta * ewald_beta)) / safe, 0.0
    )


def mm(a, b):
    return jnp.dot(a, b, preferred_element_type=jnp.float32)


def combine(p, forward):
    rows, cols = p.shape
    c, s = p[: rows // 2], p[rows // 2 :]
    c_re, c_im = c[:, : cols // 2], c[:, cols // 2 :]
    s_re, s_im = s[:, : cols // 2], s[:, cols // 2 :]
    if forward:
        return c_re + s_im, c_im - s_re
    return c_re - s_im, c_im + s_re


def regroup(parts, split, perm, shape, axis):
    moved = [x.astype(jnp.bfloat16).reshape(split).transpose(perm).reshape(shape) for x in parts]
    return jnp.concatenate(moved, axis=axis)


def solve_field(density, devices, dev_index):
    xps = GX // devices
    kyls = GY // devices
    cz, sz = dft_pair(GZ)
    fa = jnp.asarray(np.concatenate([cz, -sz], axis=1), jnp.bfloat16)
    d_hi, d_lo = split2(density)
    a = mm(d_hi, fa) + mm(d_lo, fa)
    a_re = a[:, :GZ].reshape(GY, xps, GZ).astype(jnp.bfloat16)
    a_im = a[:, GZ:].reshape(GY, xps, GZ).astype(jnp.bfloat16)
    cy, sy = dft_pair(GY)
    fy = jnp.asarray(np.concatenate([cy, sy], axis=0), jnp.bfloat16)
    p = jnp.einsum("ky,ypz->kpz", fy, a_re, preferred_element_type=jnp.float32)
    q = jnp.einsum("ky,ypz->kpz", fy, a_im, preferred_element_type=jnp.float32)
    y_re = p[:GY] + q[GY:]
    y_im = q[:GY] - p[GY:]

    def by_dest(t):
        return t.reshape(devices, kyls, xps, GZ).transpose(0, 2, 1, 3)

    sent = jnp.stack([by_dest(y_re), by_dest(y_im)], axis=2).astype(jnp.bfloat16)
    r2 = lax.all_to_all(sent, AXES, 0, 0, tiled=True)
    cx, sx = dft_pair(GX)
    fx = jnp.asarray(np.concatenate([cx, sx], axis=0), jnp.bfloat16)
    p2 = jnp.einsum("kpx,pxrjz->krjz", fx.reshape(2 * GX, devices, xps), r2, preferred_element_type=jnp.float32)
    z_re = p2[:GX, 0] + p2[GX:, 1]
    z_im = p2[:GX, 1] - p2[GX:, 0]
    kernel = green(
        wave_square(GX, 0, GX), wave_square(kyls, dev_index * kyls, GY), wave_square(GZ, 0, GZ)
    ) * (1.0 / (GX * GY * GZ))
    z = jnp.stack([z_re * kernel, z_im * kernel], axis=1).astype(jnp.bfloat16)
    p3 = jnp.einsum("xk,krjz->xrjz", fx, z, preferred_element_type=jnp.float32)
    w_re = p3[:GX, 0] - p3[GX:, 1]
    w_im = p3[:GX, 1] + p3[GX:, 0]
    back = jnp.stack(
        [w_re.reshape(devices, xps, kyls, GZ), w_im.reshape(devices, xps, kyls, GZ)], axis=2
    ).astype(jnp.bfloat16)
    r3 = lax.all_to_all(back, AXES, 0, 0, tiled=True)
    r3 = r3.transpose(2, 1, 0, 3, 4).reshape(2 * xps, GY, GZ)
    p4 = jnp.einsum("yk,bkz->ybz", fy, r3, preferred_element_type=jnp.float32).reshape(2 * GY, 2, xps, GZ)
    v_re = p4[:GY, 0] - p4[GY:, 1]
    v_im = p4[:GY, 1] + p4[GY:, 0]
    return jnp.concatenate([v_re, v_im], axis=-1).reshape(GY * xps, 2 * GZ).astype(jnp.bfloat16)


def gnn_layer(hidden, gathered, unit_w, radial_parts, w_self, w_nbr, w_rad, w_msg, w_out, gain):
    atoms, width = hidden.shape
    fanout = gathered.shape[0] // atoms
    gathered_h = gathered[:, :width]
    r_hi, r_lo = radial_parts
    w_hi, w_lo = split2(w_rad)
    lhs = jnp.concatenate([gathered_h, r_hi, r_lo, r_hi], axis=1)
    rhs = jnp.concatenate([w_nbr, w_hi, w_hi, w_lo], axis=0)
    own_term = mm(hidden, w_self)
    pre = mm(lhs, rhs).reshape(atoms, fanout, width) + own_term[:, None, :]
    message = silu(pre).astype(jnp.bfloat16)
    parts = jnp.einsum("akc,akf->acf", unit_w, message, preferred_element_type=jnp.float32)
    sums = jnp.concatenate([parts[:, :1], parts[:, 1:4] + parts[:, 4:7]], axis=1)
    s_hi, s_lo = split2(sums.reshape(atoms * 4, width))
    mixed = (mm(s_hi, w_msg) + mm(s_lo, w_msg)).reshape(atoms, 4, width) / fanout
    total = mixed[:, 0] + jnp.sum(mixed[:, 1:] * mixed[:, 1:], axis=1)
    normed = total * lax.rsqrt(jnp.mean(total * total, axis=-1, keepdims=True) + norm_eps) * gain
    active = silu(normed).astype(jnp.bfloat16)
    update = mm(active, w_out)
    return (hidden.astype(jnp.float32) + update).astype(jnp.bfloat16)


def per_device(
    feats,
    coords,
    nbrs,
    owner,
    cell,
    w_self,
    w_nbr,
    w_rad,
    w_msg,
    w_out,
    norm_gain,
    w_charge,
    w_energy,
):
    atoms, width = feats.shape
    fanout = nbrs.shape[1]
    n_dom = lax.axis_size("dom")
    n_pme = lax.axis_size("pme")
    devices = n_dom * n_pme
    wide_rows = 3 * atoms
    pos_own = coords.T
    p_hi, p_mid, p_lo = split3(pos_own)
    wide0 = halo(jnp.concatenate([feats, p_hi, p_mid, p_lo], axis=1))
    flat_nbrs = nbrs.reshape(-1)
    onehot = (flat_nbrs[:, None] == jnp.arange(wide_rows, dtype=jnp.int32)[None, :]).astype(
        jnp.bfloat16
    )
    hidden = feats
    unit_w = None
    radial_parts = None
    for layer_idx in range(LAYERS):
        table = wide0 if layer_idx == 0 else halo(hidden)
        gathered = jnp.dot(onehot, table, preferred_element_type=jnp.bfloat16)
        if layer_idx == 0:
            gp = gathered[:, width:].astype(jnp.float32)
            pos_j = gp[:, 0:3] + gp[:, 3:6] + gp[:, 6:9]
            lift = jnp.where(flat_nbrs < atoms, -slab_depth, jnp.where(flat_nbrs >= 2 * atoms, slab_depth, 0.0))
            pos_j = pos_j + jnp.where(jnp.arange(3, dtype=jnp.int32) == 2, 1.0, 0.0)[None, :] * lift[:, None]
            delta = pos_j.reshape(atoms, fanout, 3) - pos_own[:, None, :]
            dist = jnp.sqrt(jnp.sum(delta * delta, axis=-1) + 1.0)
            centres = radial_width * (jnp.arange(NB, dtype=jnp.float32) + 1.0)
            radial = jnp.exp(-jnp.square((dist[:, :, None] - centres) / radial_width))
            radial_parts = split2(radial.reshape(atoms * fanout, NB))
            unit = delta / dist[:, :, None]
            u_hi, u_lo = split2(unit)
            unit_w = jnp.concatenate(
                [jnp.ones((atoms, fanout, 1), jnp.bfloat16), u_hi, u_lo, jnp.zeros((atoms, fanout, 1), jnp.bfloat16)],
                axis=-1,
            )
        hidden = gnn_layer(
            hidden,
            gathered,
            unit_w,
            radial_parts,
            w_self[layer_idx],
            w_nbr[layer_idx],
            w_rad[layer_idx],
            w_msg[layer_idx],
            w_out[layer_idx],
            norm_gain[layer_idx],
        )
    flat_hidden = hidden.astype(jnp.float32)
    readout = jnp.dot(flat_hidden, jnp.stack([w_energy, w_charge], axis=1), precision=highest)
    energy_ml = readout[:, 0]
    charge = readout[:, 1]
    capacity = max(2, 2 * atoms // devices) * n_pme
    bx = GX // n_dom
    by = GY // n_pme
    xps = GX // devices
    dest_owner = owner[:, 0]
    grid_x = dest_owner // n_pme * bx + cell // (by * GZ)
    grid_y = dest_owner % n_pme * by + cell // GZ % by
    grid_z = cell % GZ
    dest = grid_x // xps
    slab_cell = (grid_y * xps + grid_x % xps) * GZ + grid_z
    matches = (dest[:, None] == jnp.arange(devices, dtype=jnp.int32)[None, :]).astype(jnp.int32)
    slot = jnp.sum((jnp.cumsum(matches, axis=0) - matches) * matches, axis=1)
    where_to = dest * capacity + slot
    payload = jnp.stack([charge, slab_cell.astype(jnp.float32)], axis=1)
    outgoing = jnp.zeros((devices * capacity, 2), jnp.float32).at[where_to].set(payload)
    incoming = lax.all_to_all(outgoing, AXES, 0, 0, tiled=True)
    cells_here = incoming[:, 1].astype(jnp.int32)
    rows_here = cells_here // GZ
    z_here = cells_here % GZ
    n_rows = GY * xps
    oh_rows = (jnp.arange(n_rows, dtype=jnp.int32)[:, None] == rows_here[None, :]).astype(jnp.bfloat16)
    oh_z = z_here[:, None] == jnp.arange(GZ, dtype=jnp.int32)[None, :]
    q_hi, q_lo = split2(incoming[:, 0])
    zero = jnp.zeros((), jnp.bfloat16)
    qz = jnp.concatenate(
        [jnp.where(oh_z, q_hi[:, None], zero), jnp.where(oh_z, q_lo[:, None], zero)], axis=1
    )
    dparts = mm(oh_rows, qz)
    density = dparts[:, :GZ] + dparts[:, GZ:]
    dev_index = lax.axis_index("dom") * n_pme + lax.axis_index("pme")
    spectrum_rows = solve_field(density, devices, dev_index)
    oh_slots = (rows_here[:, None] == jnp.arange(n_rows, dtype=jnp.int32)[None, :]).astype(jnp.bfloat16)
    picked = mm(oh_slots, spectrum_rows)
    cz, sz = dft_pair(GZ)
    ez_t = jnp.asarray(np.concatenate([cz, -sz], axis=1), jnp.bfloat16)
    ez_rows = mm(oh_z.astype(jnp.bfloat16), ez_t)
    sampled = jnp.sum(picked * ez_rows, axis=1)
    returned = lax.all_to_all(sampled, AXES, 0, 0, tiled=True)
    at_atoms = returned[where_to]
    energy_el = 0.5 * charge * at_atoms
    return (energy_ml, energy_el)


def solution(mesh):
    in_specs = (
        P(("dom", "pme"), None),
        P(None, ("dom", "pme")),
        P(("dom", "pme"), None),
        P(("dom", "pme"), None),
        P(("dom", "pme")),
        P(),
        P(),
        P(),
        P(),
        P(),
        P(),
        P(),
        P(),
    )
    out_specs = (P(("dom", "pme")), P(("dom", "pme")))
    return jax.shard_map(
        per_device, mesh=mesh, in_specs=in_specs, out_specs=out_specs, check_vma=False
    )
```

```python
import math

import jax
import jax.numpy as jnp
import numpy as np
from jax import lax
from jax.sharding import PartitionSpec as P

NB = 8
LAYERS = 2
GX = 256
GY = 256
GZ = 128


slab_depth = 3.0
radial_width = 0.75
ewald_beta = 1.2
norm_eps = 1e-05
highest = lax.Precision.HIGHEST
AXES = ("dom", "pme")


def to_bf16_exact(x):
    return lax.reduce_precision(x, exponent_bits=8, mantissa_bits=7)


def split2(x):
    hi = to_bf16_exact(x)
    lo = x - hi
    return hi.astype(jnp.bfloat16), lo.astype(jnp.bfloat16)


def split3(x):
    hi = to_bf16_exact(x)
    rest = x - hi
    mid = to_bf16_exact(rest)
    lo = rest - mid
    return hi.astype(jnp.bfloat16), mid.astype(jnp.bfloat16), lo.astype(jnp.bfloat16)


def halo(shard):
    devices = lax.axis_size(AXES)
    up = [(i, (i + 1) % devices) for i in range(devices)]
    down = [(j, i) for i, j in up]
    before = lax.ppermute(shard, AXES, up)
    after = lax.ppermute(shard, AXES, down)
    return jnp.concatenate([before, shard, after], axis=0)


def silu(x):
    return x * jax.nn.sigmoid(x)


def dft_pair(length):
    k = np.arange(length, dtype=np.int64)
    angle = (np.outer(k, k) % length).astype(np.float64) * (2.0 * math.pi / length)
    return np.cos(angle), np.sin(angle)


def wave_square(count, start, full):
    index = start + jnp.arange(count, dtype=jnp.int32)
    folded = jnp.where(index < full // 2, index, index - full).astype(jnp.float32)
    scaled = folded * (2.0 * math.pi / full)
    return scaled * scaled


def green(wave_x, wave_y, wave_z):
    ksq = wave_x[:, None, None] + wave_y[None, :, None] + wave_z[None, None, :]
    safe = jnp.where(ksq > 0, ksq, 1.0)
    return jnp.where(
        ksq > 0, 4.0 * math.pi * jnp.exp(-ksq / (4.0 * ewald_beta * ewald_beta)) / safe, 0.0
    )


def mm(a, b):
    return jnp.dot(a, b, preferred_element_type=jnp.float32)


def combine(p, forward):
    rows, cols = p.shape
    c, s = p[: rows // 2], p[rows // 2 :]
    c_re, c_im = c[:, : cols // 2], c[:, cols // 2 :]
    s_re, s_im = s[:, : cols // 2], s[:, cols // 2 :]
    if forward:
        return c_re + s_im, c_im - s_re
    return c_re - s_im, c_im + s_re


def regroup(parts, split, perm, shape, axis):
    moved = [x.astype(jnp.bfloat16).reshape(split).transpose(perm).reshape(shape) for x in parts]
    return jnp.concatenate(moved, axis=axis)


def solve_field(density, devices, dev_index):
    xps = GX // devices
    kyls = GY // devices
    cz, sz = dft_pair(GZ)
    fa = jnp.asarray(np.concatenate([cz, -sz], axis=1), jnp.bfloat16)
    d_hi, d_lo = split2(density)
    a = mm(d_hi, fa) + mm(d_lo, fa)
    a_re = a[:, :GZ].reshape(GY, xps, GZ).astype(jnp.bfloat16)
    a_im = a[:, GZ:].reshape(GY, xps, GZ).astype(jnp.bfloat16)
    cy, sy = dft_pair(GY)
    fy = jnp.asarray(np.concatenate([cy, sy], axis=0), jnp.bfloat16)
    p = jnp.einsum("ky,ypz->kpz", fy, a_re, preferred_element_type=jnp.bfloat16)
    q = jnp.einsum("ky,ypz->kpz", fy, a_im, preferred_element_type=jnp.bfloat16)
    y_re = p[:GY] + q[GY:]
    y_im = q[:GY] - p[GY:]

    def by_dest(t):
        return t.reshape(devices, kyls, xps, GZ).transpose(0, 2, 1, 3)

    sent = jnp.stack([by_dest(y_re), by_dest(y_im)], axis=2).astype(jnp.bfloat16)
    r2 = lax.all_to_all(sent, AXES, 0, 0, tiled=True)
    cx, sx = dft_pair(GX)
    fx = jnp.asarray(np.concatenate([cx, sx], axis=0), jnp.bfloat16)
    p2 = jnp.einsum("kpx,pxrjz->krjz", fx.reshape(2 * GX, devices, xps), r2, preferred_element_type=jnp.bfloat16)
    z_re = p2[:GX, 0] + p2[GX:, 1]
    z_im = p2[:GX, 1] - p2[GX:, 0]
    kernel = green(
        wave_square(GX, 0, GX), wave_square(kyls, dev_index * kyls, GY), wave_square(GZ, 0, GZ)
    ) * (1.0 / (GX * GY * GZ))
    z = jnp.stack([z_re * kernel, z_im * kernel], axis=1).astype(jnp.bfloat16)
    p3 = jnp.einsum("xk,krjz->xrjz", fx, z, preferred_element_type=jnp.bfloat16)
    w_re = p3[:GX, 0] - p3[GX:, 1]
    w_im = p3[:GX, 1] + p3[GX:, 0]
    back = jnp.stack(
        [w_re.reshape(devices, xps, kyls, GZ), w_im.reshape(devices, xps, kyls, GZ)], axis=2
    ).astype(jnp.bfloat16)
    r3 = lax.all_to_all(back, AXES, 0, 0, tiled=True)
    r3 = r3.transpose(2, 1, 0, 3, 4).reshape(2 * xps, GY, GZ)
    p4 = jnp.einsum("yk,bkz->ybz", fy, r3, preferred_element_type=jnp.bfloat16).reshape(2 * GY, 2, xps, GZ)
    v_re = p4[:GY, 0] - p4[GY:, 1]
    v_im = p4[:GY, 1] + p4[GY:, 0]
    return jnp.concatenate([v_re, v_im], axis=-1).reshape(GY * xps, 2 * GZ).astype(jnp.bfloat16)


def gnn_layer(hidden, gathered, unit_w, radial_parts, w_self, w_nbr, w_rad, w_msg, w_out, gain):
    atoms, width = hidden.shape
    fanout = gathered.shape[0] // atoms
    gathered_h = gathered[:, :width]
    r_hi, r_lo = radial_parts
    w_hi, w_lo = split2(w_rad)
    lhs = jnp.concatenate([gathered_h, r_hi, r_lo, r_hi], axis=1)
    rhs = jnp.concatenate([w_nbr, w_hi, w_hi, w_lo], axis=0)
    own_term = mm(hidden, w_self)
    pre = mm(lhs, rhs).reshape(atoms, fanout, width) + own_term[:, None, :]
    message = silu(pre).astype(jnp.bfloat16)
    parts = jnp.einsum("akc,akf->acf", unit_w, message, preferred_element_type=jnp.float32)
    sums = jnp.concatenate([parts[:, :1], parts[:, 1:4] + parts[:, 4:7]], axis=1)
    s_hi, s_lo = split2(sums.reshape(atoms * 4, width))
    mixed = (mm(s_hi, w_msg) + mm(s_lo, w_msg)).reshape(atoms, 4, width) / fanout
    total = mixed[:, 0] + jnp.sum(mixed[:, 1:] * mixed[:, 1:], axis=1)
    normed = total * lax.rsqrt(jnp.mean(total * total, axis=-1, keepdims=True) + norm_eps) * gain
    active = silu(normed).astype(jnp.bfloat16)
    update = mm(active, w_out)
    return (hidden.astype(jnp.float32) + update).astype(jnp.bfloat16)


def per_device(
    feats,
    coords,
    nbrs,
    owner,
    cell,
    w_self,
    w_nbr,
    w_rad,
    w_msg,
    w_out,
    norm_gain,
    w_charge,
    w_energy,
):
    atoms, width = feats.shape
    fanout = nbrs.shape[1]
    n_dom = lax.axis_size("dom")
    n_pme = lax.axis_size("pme")
    devices = n_dom * n_pme
    wide_rows = 3 * atoms
    pos_own = coords.T
    p_hi, p_mid, p_lo = split3(pos_own)
    wide0 = halo(jnp.concatenate([feats, p_hi, p_mid, p_lo], axis=1))
    flat_nbrs = nbrs.reshape(-1)
    onehot = (flat_nbrs[:, None] == jnp.arange(wide_rows, dtype=jnp.int32)[None, :]).astype(
        jnp.bfloat16
    )
    hidden = feats
    unit_w = None
    radial_parts = None
    for layer_idx in range(LAYERS):
        table = wide0 if layer_idx == 0 else halo(hidden)
        gathered = jnp.dot(onehot, table, preferred_element_type=jnp.bfloat16)
        if layer_idx == 0:
            gp = gathered[:, width:].astype(jnp.float32)
            pos_j = gp[:, 0:3] + gp[:, 3:6] + gp[:, 6:9]
            lift = jnp.where(flat_nbrs < atoms, -slab_depth, jnp.where(flat_nbrs >= 2 * atoms, slab_depth, 0.0))
            pos_j = pos_j + jnp.where(jnp.arange(3, dtype=jnp.int32) == 2, 1.0, 0.0)[None, :] * lift[:, None]
            delta = pos_j.reshape(atoms, fanout, 3) - pos_own[:, None, :]
            dist = jnp.sqrt(jnp.sum(delta * delta, axis=-1) + 1.0)
            centres = radial_width * (jnp.arange(NB, dtype=jnp.float32) + 1.0)
            radial = jnp.exp(-jnp.square((dist[:, :, None] - centres) / radial_width))
            radial_parts = split2(radial.reshape(atoms * fanout, NB))
            unit = delta / dist[:, :, None]
            u_hi, u_lo = split2(unit)
            unit_w = jnp.concatenate(
                [jnp.ones((atoms, fanout, 1), jnp.bfloat16), u_hi, u_lo, jnp.zeros((atoms, fanout, 1), jnp.bfloat16)],
                axis=-1,
            )
        hidden = gnn_layer(
            hidden,
            gathered,
            unit_w,
            radial_parts,
            w_self[layer_idx],
            w_nbr[layer_idx],
            w_rad[layer_idx],
            w_msg[layer_idx],
            w_out[layer_idx],
            norm_gain[layer_idx],
        )
    flat_hidden = hidden.astype(jnp.float32)
    readout = jnp.dot(flat_hidden, jnp.stack([w_energy, w_charge], axis=1), precision=highest)
    energy_ml = readout[:, 0]
    charge = readout[:, 1]
    capacity = max(2, 2 * atoms // devices) * n_pme
    bx = GX // n_dom
    by = GY // n_pme
    xps = GX // devices
    dest_owner = owner[:, 0]
    grid_x = dest_owner // n_pme * bx + cell // (by * GZ)
    grid_y = dest_owner % n_pme * by + cell // GZ % by
    grid_z = cell % GZ
    dest = grid_x // xps
    slab_cell = (grid_y * xps + grid_x % xps) * GZ + grid_z
    matches = (dest[:, None] == jnp.arange(devices, dtype=jnp.int32)[None, :]).astype(jnp.int32)
    slot = jnp.sum((jnp.cumsum(matches, axis=0) - matches) * matches, axis=1)
    where_to = dest * capacity + slot
    payload = jnp.stack([charge, slab_cell.astype(jnp.float32)], axis=1)
    outgoing = jnp.zeros((devices * capacity, 2), jnp.float32).at[where_to].set(payload)
    incoming = lax.all_to_all(outgoing, AXES, 0, 0, tiled=True)
    cells_here = incoming[:, 1].astype(jnp.int32)
    rows_here = cells_here // GZ
    z_here = cells_here % GZ
    n_rows = GY * xps
    oh_rows = (jnp.arange(n_rows, dtype=jnp.int32)[:, None] == rows_here[None, :]).astype(jnp.bfloat16)
    oh_z = z_here[:, None] == jnp.arange(GZ, dtype=jnp.int32)[None, :]
    q_hi, q_lo = split2(incoming[:, 0])
    zero = jnp.zeros((), jnp.bfloat16)
    qz = jnp.concatenate(
        [jnp.where(oh_z, q_hi[:, None], zero), jnp.where(oh_z, q_lo[:, None], zero)], axis=1
    )
    dparts = mm(oh_rows, qz)
    density = dparts[:, :GZ] + dparts[:, GZ:]
    dev_index = lax.axis_index("dom") * n_pme + lax.axis_index("pme")
    spectrum_rows = solve_field(density, devices, dev_index)
    picked = lax.dot_general(
        oh_rows, spectrum_rows, (((0,), (0,)), ((), ())), preferred_element_type=jnp.float32
    )
    cz, sz = dft_pair(GZ)
    ez_t = jnp.asarray(np.concatenate([cz, -sz], axis=1), jnp.bfloat16)
    ez_rows = mm(oh_z.astype(jnp.bfloat16), ez_t)
    sampled = jnp.sum(picked * ez_rows, axis=1)
    returned = lax.all_to_all(sampled, AXES, 0, 0, tiled=True)
    at_atoms = returned[where_to]
    energy_el = 0.5 * charge * at_atoms
    return (energy_ml, energy_el)


def solution(mesh):
    in_specs = (
        P(("dom", "pme"), None),
        P(None, ("dom", "pme")),
        P(("dom", "pme"), None),
        P(("dom", "pme"), None),
        P(("dom", "pme")),
        P(),
        P(),
        P(),
        P(),
        P(),
        P(),
        P(),
        P(),
    )
    out_specs = (P(("dom", "pme")), P(("dom", "pme")))
    return jax.shard_map(
        per_device, mesh=mesh, in_specs=in_specs, out_specs=out_specs, check_vma=False
    )
```

```python
import math

import jax
import jax.numpy as jnp
import numpy as np
from jax import lax
from jax.sharding import PartitionSpec as P

NB = 8
LAYERS = 2
GX = 256
GY = 256
GZ = 128


slab_depth = 3.0
radial_width = 0.75
ewald_beta = 1.2
norm_eps = 1e-05
highest = lax.Precision.HIGHEST
AXES = ("dom", "pme")


def to_bf16_exact(x):
    return lax.reduce_precision(x, exponent_bits=8, mantissa_bits=7)


def split2(x):
    hi = to_bf16_exact(x)
    lo = x - hi
    return hi.astype(jnp.bfloat16), lo.astype(jnp.bfloat16)


def split3(x):
    hi = to_bf16_exact(x)
    rest = x - hi
    mid = to_bf16_exact(rest)
    lo = rest - mid
    return hi.astype(jnp.bfloat16), mid.astype(jnp.bfloat16), lo.astype(jnp.bfloat16)


def halo(shard):
    devices = lax.axis_size(AXES)
    up = [(i, (i + 1) % devices) for i in range(devices)]
    down = [(j, i) for i, j in up]
    before = lax.ppermute(shard, AXES, up)
    after = lax.ppermute(shard, AXES, down)
    return jnp.concatenate([before, shard, after], axis=0)


def silu(x):
    return x * jax.nn.sigmoid(x)


def dft_pair(length):
    k = np.arange(length, dtype=np.int64)
    angle = (np.outer(k, k) % length).astype(np.float64) * (2.0 * math.pi / length)
    return np.cos(angle), np.sin(angle)


def wave_square(count, start, full):
    index = start + jnp.arange(count, dtype=jnp.int32)
    folded = jnp.where(index < full // 2, index, index - full).astype(jnp.float32)
    scaled = folded * (2.0 * math.pi / full)
    return scaled * scaled


def green(wave_x, wave_y, wave_z):
    ksq = wave_x[:, None, None] + wave_y[None, :, None] + wave_z[None, None, :]
    safe = jnp.where(ksq > 0, ksq, 1.0)
    return jnp.where(
        ksq > 0, 4.0 * math.pi * jnp.exp(-ksq / (4.0 * ewald_beta * ewald_beta)) / safe, 0.0
    )


def mm(a, b):
    return jnp.dot(a, b, preferred_element_type=jnp.float32)


def combine(p, forward):
    rows, cols = p.shape
    c, s = p[: rows // 2], p[rows // 2 :]
    c_re, c_im = c[:, : cols // 2], c[:, cols // 2 :]
    s_re, s_im = s[:, : cols // 2], s[:, cols // 2 :]
    if forward:
        return c_re + s_im, c_im - s_re
    return c_re - s_im, c_im + s_re


def regroup(parts, split, perm, shape, axis):
    moved = [x.astype(jnp.bfloat16).reshape(split).transpose(perm).reshape(shape) for x in parts]
    return jnp.concatenate(moved, axis=axis)


def solve_field(density, devices, dev_index):
    xps = GX // devices
    kyls = GY // devices
    cz, sz = dft_pair(GZ)
    fa = jnp.asarray(np.concatenate([cz, -sz], axis=1), jnp.bfloat16)
    d_hi, d_lo = split2(density)
    a = jnp.dot(
        jnp.concatenate([d_hi, d_lo], axis=1), jnp.concatenate([fa, fa], axis=0),
        preferred_element_type=jnp.bfloat16,
    )
    a_re = a[:, :GZ].reshape(GY, xps, GZ)
    a_im = a[:, GZ:].reshape(GY, xps, GZ)
    cy, sy = dft_pair(GY)
    fy = jnp.asarray(np.concatenate([cy, sy], axis=0), jnp.bfloat16)
    p = jnp.einsum("ky,ypz->kpz", fy, a_re, preferred_element_type=jnp.bfloat16)
    q = jnp.einsum("ky,ypz->kpz", fy, a_im, preferred_element_type=jnp.bfloat16)
    y_re = p[:GY] + q[GY:]
    y_im = q[:GY] - p[GY:]

    def by_dest(t):
        return t.reshape(devices, kyls, xps, GZ).transpose(0, 2, 1, 3)

    sent = jnp.stack([by_dest(y_re), by_dest(y_im)], axis=2).astype(jnp.bfloat16)
    r2 = lax.all_to_all(sent, AXES, 0, 0, tiled=True)
    cx, sx = dft_pair(GX)
    fx = jnp.asarray(np.concatenate([cx, sx], axis=0), jnp.bfloat16)
    p2 = jnp.einsum("kpx,pxrjz->krjz", fx.reshape(2 * GX, devices, xps), r2, preferred_element_type=jnp.bfloat16)
    z_re = p2[:GX, 0] + p2[GX:, 1]
    z_im = p2[:GX, 1] - p2[GX:, 0]
    kernel = green(
        wave_square(GX, 0, GX), wave_square(kyls, dev_index * kyls, GY), wave_square(GZ, 0, GZ)
    ) * (1.0 / (GX * GY * GZ))
    z = jnp.stack([z_re * kernel, z_im * kernel], axis=1).astype(jnp.bfloat16)
    p3 = jnp.einsum("xk,krjz->xrjz", fx, z, preferred_element_type=jnp.bfloat16)
    w_re = p3[:GX, 0] - p3[GX:, 1]
    w_im = p3[:GX, 1] + p3[GX:, 0]
    back = jnp.stack(
        [w_re.reshape(devices, xps, kyls, GZ), w_im.reshape(devices, xps, kyls, GZ)], axis=2
    ).astype(jnp.bfloat16)
    r3 = lax.all_to_all(back, AXES, 0, 0, tiled=True)
    r3 = r3.transpose(2, 1, 0, 3, 4).reshape(2 * xps, GY, GZ)
    p4 = jnp.einsum("yk,bkz->ybz", fy, r3, preferred_element_type=jnp.bfloat16).reshape(2 * GY, 2, xps, GZ)
    v_re = p4[:GY, 0] - p4[GY:, 1]
    v_im = p4[:GY, 1] + p4[GY:, 0]
    return jnp.concatenate([v_re, v_im], axis=-1).reshape(GY * xps, 2 * GZ).astype(jnp.bfloat16)


def gnn_layer(hidden, gathered, unit_w, radial_parts, w_self, w_nbr, w_rad, w_msg, w_out, gain):
    atoms, width = hidden.shape
    fanout = gathered.shape[0] // atoms
    gathered_h = gathered[:, :width]
    r_hi, r_lo = radial_parts
    w_hi, w_lo = split2(w_rad)
    lhs = jnp.concatenate([gathered_h, r_hi, r_lo, r_hi], axis=1)
    rhs = jnp.concatenate([w_nbr, w_hi, w_hi, w_lo], axis=0)
    own_term = mm(hidden, w_self)
    pre = mm(lhs, rhs).reshape(atoms, fanout, width) + own_term[:, None, :]
    message = silu(pre).astype(jnp.bfloat16)
    parts = jnp.einsum("akc,akf->acf", unit_w, message, preferred_element_type=jnp.float32)
    sums = jnp.concatenate([parts[:, :1], parts[:, 1:4] + parts[:, 4:7]], axis=1)
    s_hi, s_lo = split2(sums.reshape(atoms * 4, width))
    mixed = (mm(s_hi, w_msg) + mm(s_lo, w_msg)).reshape(atoms, 4, width) / fanout
    total = mixed[:, 0] + jnp.sum(mixed[:, 1:] * mixed[:, 1:], axis=1)
    normed = total * lax.rsqrt(jnp.mean(total * total, axis=-1, keepdims=True) + norm_eps) * gain
    active = silu(normed).astype(jnp.bfloat16)
    update = mm(active, w_out)
    return (hidden.astype(jnp.float32) + update).astype(jnp.bfloat16)


def per_device(
    feats,
    coords,
    nbrs,
    owner,
    cell,
    w_self,
    w_nbr,
    w_rad,
    w_msg,
    w_out,
    norm_gain,
    w_charge,
    w_energy,
):
    atoms, width = feats.shape
    fanout = nbrs.shape[1]
    n_dom = lax.axis_size("dom")
    n_pme = lax.axis_size("pme")
    devices = n_dom * n_pme
    wide_rows = 3 * atoms
    pos_own = coords.T
    p_hi, p_mid, p_lo = split3(pos_own)
    wide0 = halo(jnp.concatenate([feats, p_hi, p_mid, p_lo], axis=1))
    flat_nbrs = nbrs.reshape(-1)
    onehot = (flat_nbrs[:, None] == jnp.arange(wide_rows, dtype=jnp.int32)[None, :]).astype(
        jnp.bfloat16
    )
    hidden = feats
    unit_w = None
    radial_parts = None
    for layer_idx in range(LAYERS):
        table = wide0 if layer_idx == 0 else halo(hidden)
        gathered = jnp.dot(onehot, table, preferred_element_type=jnp.bfloat16)
        if layer_idx == 0:
            gp = gathered[:, width:].astype(jnp.float32)
            pos_j = gp[:, 0:3] + gp[:, 3:6] + gp[:, 6:9]
            lift = jnp.where(flat_nbrs < atoms, -slab_depth, jnp.where(flat_nbrs >= 2 * atoms, slab_depth, 0.0))
            pos_j = pos_j + jnp.where(jnp.arange(3, dtype=jnp.int32) == 2, 1.0, 0.0)[None, :] * lift[:, None]
            delta = pos_j.reshape(atoms, fanout, 3) - pos_own[:, None, :]
            dist = jnp.sqrt(jnp.sum(delta * delta, axis=-1) + 1.0)
            centres = radial_width * (jnp.arange(NB, dtype=jnp.float32) + 1.0)
            radial = jnp.exp(-jnp.square((dist[:, :, None] - centres) / radial_width))
            radial_parts = split2(radial.reshape(atoms * fanout, NB))
            unit = delta / dist[:, :, None]
            u_hi, u_lo = split2(unit)
            unit_w = jnp.concatenate(
                [jnp.ones((atoms, fanout, 1), jnp.bfloat16), u_hi, u_lo, jnp.zeros((atoms, fanout, 1), jnp.bfloat16)],
                axis=-1,
            )
        hidden = gnn_layer(
            hidden,
            gathered,
            unit_w,
            radial_parts,
            w_self[layer_idx],
            w_nbr[layer_idx],
            w_rad[layer_idx],
            w_msg[layer_idx],
            w_out[layer_idx],
            norm_gain[layer_idx],
        )
    flat_hidden = hidden.astype(jnp.float32)
    readout = jnp.dot(flat_hidden, jnp.stack([w_energy, w_charge], axis=1), precision=highest)
    energy_ml = readout[:, 0]
    charge = readout[:, 1]
    capacity = max(2, 2 * atoms // devices) * n_pme
    bx = GX // n_dom
    by = GY // n_pme
    xps = GX // devices
    dest_owner = owner[:, 0]
    grid_x = dest_owner // n_pme * bx + cell // (by * GZ)
    grid_y = dest_owner % n_pme * by + cell // GZ % by
    grid_z = cell % GZ
    dest = grid_x // xps
    slab_cell = (grid_y * xps + grid_x % xps) * GZ + grid_z
    matches = (dest[:, None] == jnp.arange(devices, dtype=jnp.int32)[None, :]).astype(jnp.int32)
    slot = jnp.sum((jnp.cumsum(matches, axis=0) - matches) * matches, axis=1)
    where_to = dest * capacity + slot
    payload = jnp.stack([charge, slab_cell.astype(jnp.float32)], axis=1)
    outgoing = jnp.zeros((devices * capacity, 2), jnp.float32).at[where_to].set(payload)
    incoming = lax.all_to_all(outgoing, AXES, 0, 0, tiled=True)
    cells_here = incoming[:, 1].astype(jnp.int32)
    rows_here = cells_here // GZ
    z_here = cells_here % GZ
    n_rows = GY * xps
    oh_rows = (jnp.arange(n_rows, dtype=jnp.int32)[:, None] == rows_here[None, :]).astype(jnp.bfloat16)
    oh_z = z_here[:, None] == jnp.arange(GZ, dtype=jnp.int32)[None, :]
    q_hi, q_lo = split2(incoming[:, 0])
    zero = jnp.zeros((), jnp.bfloat16)
    qz = jnp.concatenate(
        [jnp.where(oh_z, q_hi[:, None], zero), jnp.where(oh_z, q_lo[:, None], zero)], axis=1
    )
    dparts = mm(oh_rows, qz)
    density = dparts[:, :GZ] + dparts[:, GZ:]
    dev_index = lax.axis_index("dom") * n_pme + lax.axis_index("pme")
    spectrum_rows = solve_field(density, devices, dev_index)
    picked = lax.dot_general(
        oh_rows, spectrum_rows, (((0,), (0,)), ((), ())), preferred_element_type=jnp.bfloat16
    )
    cz, sz = dft_pair(GZ)
    ez_t = jnp.asarray(np.concatenate([cz, -sz], axis=1), jnp.bfloat16)
    ez_rows = jnp.dot(oh_z.astype(jnp.bfloat16), ez_t, preferred_element_type=jnp.bfloat16)
    sampled = jnp.sum(picked.astype(jnp.float32) * ez_rows.astype(jnp.float32), axis=1)
    returned = lax.all_to_all(sampled, AXES, 0, 0, tiled=True)
    at_atoms = returned[where_to]
    energy_el = 0.5 * charge * at_atoms
    return (energy_ml, energy_el)


def solution(mesh):
    in_specs = (
        P(("dom", "pme"), None),
        P(None, ("dom", "pme")),
        P(("dom", "pme"), None),
        P(("dom", "pme"), None),
        P(("dom", "pme")),
        P(),
        P(),
        P(),
        P(),
        P(),
        P(),
        P(),
        P(),
    )
    out_specs = (P(("dom", "pme")), P(("dom", "pme")))
    return jax.shard_map(
        per_device, mesh=mesh, in_specs=in_specs, out_specs=out_specs, check_vma=False
    )
```

```python
import math

import jax
import jax.numpy as jnp
import numpy as np
from jax import lax
from jax.sharding import PartitionSpec as P

NB = 8
LAYERS = 2
GX = 256
GY = 256
GZ = 128


slab_depth = 3.0
radial_width = 0.75
ewald_beta = 1.2
norm_eps = 1e-05
highest = lax.Precision.HIGHEST
AXES = ("dom", "pme")


def to_bf16_exact(x):
    return lax.reduce_precision(x, exponent_bits=8, mantissa_bits=7)


def split2(x):
    hi = to_bf16_exact(x)
    lo = x - hi
    return hi.astype(jnp.bfloat16), lo.astype(jnp.bfloat16)


def split3(x):
    hi = to_bf16_exact(x)
    rest = x - hi
    mid = to_bf16_exact(rest)
    lo = rest - mid
    return hi.astype(jnp.bfloat16), mid.astype(jnp.bfloat16), lo.astype(jnp.bfloat16)


def halo(shard):
    devices = lax.axis_size(AXES)
    up = [(i, (i + 1) % devices) for i in range(devices)]
    down = [(j, i) for i, j in up]
    before = lax.ppermute(shard, AXES, up)
    after = lax.ppermute(shard, AXES, down)
    return jnp.concatenate([before, shard, after], axis=0)


def silu(x):
    return x * jax.nn.sigmoid(x)


def dft_pair(length):
    k = np.arange(length, dtype=np.int64)
    angle = (np.outer(k, k) % length).astype(np.float64) * (2.0 * math.pi / length)
    return np.cos(angle), np.sin(angle)


def wave_square(count, start, full):
    index = start + jnp.arange(count, dtype=jnp.int32)
    folded = jnp.where(index < full // 2, index, index - full).astype(jnp.float32)
    scaled = folded * (2.0 * math.pi / full)
    return scaled * scaled


def green(wave_x, wave_y, wave_z):
    ksq = wave_x[:, None, None] + wave_y[None, :, None] + wave_z[None, None, :]
    safe = jnp.where(ksq > 0, ksq, 1.0)
    return jnp.where(
        ksq > 0, 4.0 * math.pi * jnp.exp(-ksq / (4.0 * ewald_beta * ewald_beta)) / safe, 0.0
    )


def mm(a, b):
    return jnp.dot(a, b, preferred_element_type=jnp.float32)


def combine(p, forward):
    rows, cols = p.shape
    c, s = p[: rows // 2], p[rows // 2 :]
    c_re, c_im = c[:, : cols // 2], c[:, cols // 2 :]
    s_re, s_im = s[:, : cols // 2], s[:, cols // 2 :]
    if forward:
        return c_re + s_im, c_im - s_re
    return c_re - s_im, c_im + s_re


def regroup(parts, split, perm, shape, axis):
    moved = [x.astype(jnp.bfloat16).reshape(split).transpose(perm).reshape(shape) for x in parts]
    return jnp.concatenate(moved, axis=axis)


def solve_field(density, devices, dev_index):
    xps = GX // devices
    kyls = GY // devices
    cz, sz = dft_pair(GZ)
    fa = jnp.asarray(np.concatenate([cz, -sz], axis=1), jnp.bfloat16)
    a = jnp.dot(
        density, jnp.concatenate([fa, fa], axis=0),
        preferred_element_type=jnp.bfloat16,
    )
    a_re = a[:, :GZ].reshape(GY, xps, GZ)
    a_im = a[:, GZ:].reshape(GY, xps, GZ)
    cy, sy = dft_pair(GY)
    fy = jnp.asarray(np.concatenate([cy, sy], axis=0), jnp.bfloat16)
    p = jnp.einsum("ky,ypz->kpz", fy, a_re, preferred_element_type=jnp.bfloat16)
    q = jnp.einsum("ky,ypz->kpz", fy, a_im, preferred_element_type=jnp.bfloat16)
    y_re = p[:GY] + q[GY:]
    y_im = q[:GY] - p[GY:]

    def by_dest(t):
        return t.reshape(devices, kyls, xps, GZ).transpose(0, 2, 1, 3)

    sent = jnp.stack([by_dest(y_re), by_dest(y_im)], axis=2).astype(jnp.bfloat16)
    r2 = lax.all_to_all(sent, AXES, 0, 0, tiled=True)
    cx, sx = dft_pair(GX)
    fx = jnp.asarray(np.concatenate([cx, sx], axis=0), jnp.bfloat16)
    p2 = jnp.einsum("kpx,pxrjz->krjz", fx.reshape(2 * GX, devices, xps), r2, preferred_element_type=jnp.bfloat16)
    z_re = p2[:GX, 0] + p2[GX:, 1]
    z_im = p2[:GX, 1] - p2[GX:, 0]
    kernel = green(
        wave_square(GX, 0, GX), wave_square(kyls, dev_index * kyls, GY), wave_square(GZ, 0, GZ)
    ) * (1.0 / (GX * GY * GZ))
    z = jnp.stack([z_re * kernel, z_im * kernel], axis=1).astype(jnp.bfloat16)
    p3 = jnp.einsum("xk,krjz->xrjz", fx, z, preferred_element_type=jnp.bfloat16)
    w_re = p3[:GX, 0] - p3[GX:, 1]
    w_im = p3[:GX, 1] + p3[GX:, 0]
    back = jnp.stack(
        [w_re.reshape(devices, xps, kyls, GZ), w_im.reshape(devices, xps, kyls, GZ)], axis=2
    ).astype(jnp.bfloat16)
    r3 = lax.all_to_all(back, AXES, 0, 0, tiled=True)
    r3 = r3.transpose(2, 1, 0, 3, 4).reshape(2 * xps, GY, GZ)
    p4 = jnp.einsum("yk,bkz->ybz", fy, r3, preferred_element_type=jnp.bfloat16).reshape(2 * GY, 2, xps, GZ)
    v_re = p4[:GY, 0] - p4[GY:, 1]
    v_im = p4[:GY, 1] + p4[GY:, 0]
    return jnp.concatenate([v_re, v_im], axis=-1).reshape(GY * xps, 2 * GZ).astype(jnp.bfloat16)


def gnn_layer(hidden, gathered, unit_w, radial_parts, w_self, w_nbr, w_rad, w_msg, w_out, gain):
    atoms, width = hidden.shape
    fanout = gathered.shape[0] // atoms
    gathered_h = gathered[:, :width]
    r_hi, r_lo = radial_parts
    w_hi, w_lo = split2(w_rad)
    lhs = jnp.concatenate([gathered_h, r_hi, r_lo, r_hi], axis=1)
    rhs = jnp.concatenate([w_nbr, w_hi, w_hi, w_lo], axis=0)
    own_term = mm(hidden, w_self)
    pre = mm(lhs, rhs).reshape(atoms, fanout, width) + own_term[:, None, :]
    message = silu(pre).astype(jnp.bfloat16)
    parts = jnp.einsum("akc,akf->acf", unit_w, message, preferred_element_type=jnp.float32)
    sums = jnp.concatenate([parts[:, :1], parts[:, 1:4] + parts[:, 4:7]], axis=1)
    s_hi, s_lo = split2(sums.reshape(atoms * 4, width))
    mixed = (mm(s_hi, w_msg) + mm(s_lo, w_msg)).reshape(atoms, 4, width) / fanout
    total = mixed[:, 0] + jnp.sum(mixed[:, 1:] * mixed[:, 1:], axis=1)
    normed = total * lax.rsqrt(jnp.mean(total * total, axis=-1, keepdims=True) + norm_eps) * gain
    active = silu(normed).astype(jnp.bfloat16)
    update = mm(active, w_out)
    return (hidden.astype(jnp.float32) + update).astype(jnp.bfloat16)


def per_device(
    feats,
    coords,
    nbrs,
    owner,
    cell,
    w_self,
    w_nbr,
    w_rad,
    w_msg,
    w_out,
    norm_gain,
    w_charge,
    w_energy,
):
    atoms, width = feats.shape
    fanout = nbrs.shape[1]
    n_dom = lax.axis_size("dom")
    n_pme = lax.axis_size("pme")
    devices = n_dom * n_pme
    wide_rows = 3 * atoms
    pos_own = coords.T
    p_hi, p_mid, p_lo = split3(pos_own)
    wide0 = halo(jnp.concatenate([feats, p_hi, p_mid, p_lo], axis=1))
    flat_nbrs = nbrs.reshape(-1)
    onehot = (flat_nbrs[:, None] == jnp.arange(wide_rows, dtype=jnp.int32)[None, :]).astype(
        jnp.bfloat16
    )
    hidden = feats
    unit_w = None
    radial_parts = None
    for layer_idx in range(LAYERS):
        table = wide0 if layer_idx == 0 else halo(hidden)
        gathered = jnp.dot(onehot, table, preferred_element_type=jnp.bfloat16)
        if layer_idx == 0:
            gp = gathered[:, width:].astype(jnp.float32)
            pos_j = gp[:, 0:3] + gp[:, 3:6] + gp[:, 6:9]
            lift = jnp.where(flat_nbrs < atoms, -slab_depth, jnp.where(flat_nbrs >= 2 * atoms, slab_depth, 0.0))
            pos_j = pos_j + jnp.where(jnp.arange(3, dtype=jnp.int32) == 2, 1.0, 0.0)[None, :] * lift[:, None]
            delta = pos_j.reshape(atoms, fanout, 3) - pos_own[:, None, :]
            dist = jnp.sqrt(jnp.sum(delta * delta, axis=-1) + 1.0)
            centres = radial_width * (jnp.arange(NB, dtype=jnp.float32) + 1.0)
            radial = jnp.exp(-jnp.square((dist[:, :, None] - centres) / radial_width))
            radial_parts = split2(radial.reshape(atoms * fanout, NB))
            unit = delta / dist[:, :, None]
            u_hi, u_lo = split2(unit)
            unit_w = jnp.concatenate(
                [jnp.ones((atoms, fanout, 1), jnp.bfloat16), u_hi, u_lo, jnp.zeros((atoms, fanout, 1), jnp.bfloat16)],
                axis=-1,
            )
        hidden = gnn_layer(
            hidden,
            gathered,
            unit_w,
            radial_parts,
            w_self[layer_idx],
            w_nbr[layer_idx],
            w_rad[layer_idx],
            w_msg[layer_idx],
            w_out[layer_idx],
            norm_gain[layer_idx],
        )
    flat_hidden = hidden.astype(jnp.float32)
    readout = jnp.dot(flat_hidden, jnp.stack([w_energy, w_charge], axis=1), precision=highest)
    energy_ml = readout[:, 0]
    charge = readout[:, 1]
    capacity = max(2, 2 * atoms // devices) * n_pme
    bx = GX // n_dom
    by = GY // n_pme
    xps = GX // devices
    dest_owner = owner[:, 0]
    grid_x = dest_owner // n_pme * bx + cell // (by * GZ)
    grid_y = dest_owner % n_pme * by + cell // GZ % by
    grid_z = cell % GZ
    dest = grid_x // xps
    slab_cell = (grid_y * xps + grid_x % xps) * GZ + grid_z
    matches = (dest[:, None] == jnp.arange(devices, dtype=jnp.int32)[None, :]).astype(jnp.int32)
    slot = jnp.sum((jnp.cumsum(matches, axis=0) - matches) * matches, axis=1)
    where_to = dest * capacity + slot
    payload = jnp.stack([charge, slab_cell.astype(jnp.float32)], axis=1)
    outgoing = jnp.zeros((devices * capacity, 2), jnp.float32).at[where_to].set(payload)
    incoming = lax.all_to_all(outgoing, AXES, 0, 0, tiled=True)
    cells_here = incoming[:, 1].astype(jnp.int32)
    rows_here = cells_here // GZ
    z_here = cells_here % GZ
    n_rows = GY * xps
    oh_rows = (jnp.arange(n_rows, dtype=jnp.int32)[:, None] == rows_here[None, :]).astype(jnp.bfloat16)
    oh_z = z_here[:, None] == jnp.arange(GZ, dtype=jnp.int32)[None, :]
    q_hi, q_lo = split2(incoming[:, 0])
    zero = jnp.zeros((), jnp.bfloat16)
    qz = jnp.concatenate(
        [jnp.where(oh_z, q_hi[:, None], zero), jnp.where(oh_z, q_lo[:, None], zero)], axis=1
    )
    density = jnp.dot(oh_rows, qz, preferred_element_type=jnp.bfloat16)
    dev_index = lax.axis_index("dom") * n_pme + lax.axis_index("pme")
    spectrum_rows = solve_field(density, devices, dev_index)
    picked = lax.dot_general(
        oh_rows, spectrum_rows, (((0,), (0,)), ((), ())), preferred_element_type=jnp.bfloat16
    )
    cz, sz = dft_pair(GZ)
    ez_t = jnp.asarray(np.concatenate([cz, -sz], axis=1), jnp.bfloat16)
    ez_rows = jnp.dot(oh_z.astype(jnp.bfloat16), ez_t, preferred_element_type=jnp.bfloat16)
    sampled = jnp.sum(picked.astype(jnp.float32) * ez_rows.astype(jnp.float32), axis=1)
    returned = lax.all_to_all(sampled, AXES, 0, 0, tiled=True)
    at_atoms = returned[where_to]
    energy_el = 0.5 * charge * at_atoms
    return (energy_ml, energy_el)


def solution(mesh):
    in_specs = (
        P(("dom", "pme"), None),
        P(None, ("dom", "pme")),
        P(("dom", "pme"), None),
        P(("dom", "pme"), None),
        P(("dom", "pme")),
        P(),
        P(),
        P(),
        P(),
        P(),
        P(),
        P(),
        P(),
    )
    out_specs = (P(("dom", "pme")), P(("dom", "pme")))
    return jax.shard_map(
        per_device, mesh=mesh, in_specs=in_specs, out_specs=out_specs, check_vma=False
    )
```

```python
import math

import jax
import jax.numpy as jnp
import numpy as np
from jax import lax
from jax.sharding import PartitionSpec as P

NB = 8
LAYERS = 2
GX = 256
GY = 256
GZ = 128


slab_depth = 3.0
radial_width = 0.75
ewald_beta = 1.2
norm_eps = 1e-05
highest = lax.Precision.HIGHEST
AXES = ("dom", "pme")


def to_bf16_exact(x):
    return lax.reduce_precision(x, exponent_bits=8, mantissa_bits=7)


def split2(x):
    hi = to_bf16_exact(x)
    lo = x - hi
    return hi.astype(jnp.bfloat16), lo.astype(jnp.bfloat16)


def split3(x):
    hi = to_bf16_exact(x)
    rest = x - hi
    mid = to_bf16_exact(rest)
    lo = rest - mid
    return hi.astype(jnp.bfloat16), mid.astype(jnp.bfloat16), lo.astype(jnp.bfloat16)


def halo(shard):
    devices = lax.axis_size(AXES)
    up = [(i, (i + 1) % devices) for i in range(devices)]
    down = [(j, i) for i, j in up]
    before = lax.ppermute(shard, AXES, up)
    after = lax.ppermute(shard, AXES, down)
    return jnp.concatenate([before, shard, after], axis=0)


def silu(x):
    return x * jax.nn.sigmoid(x)


def dft_pair(length):
    k = np.arange(length, dtype=np.int64)
    angle = (np.outer(k, k) % length).astype(np.float64) * (2.0 * math.pi / length)
    return np.cos(angle), np.sin(angle)


def wave_square(count, start, full):
    index = start + jnp.arange(count, dtype=jnp.int32)
    folded = jnp.where(index < full // 2, index, index - full).astype(jnp.float32)
    scaled = folded * (2.0 * math.pi / full)
    return scaled * scaled


def green(wave_x, wave_y, wave_z):
    ksq = wave_x[:, None, None] + wave_y[None, :, None] + wave_z[None, None, :]
    safe = jnp.where(ksq > 0, ksq, 1.0)
    return jnp.where(
        ksq > 0, 4.0 * math.pi * jnp.exp(-ksq / (4.0 * ewald_beta * ewald_beta)) / safe, 0.0
    )


def mm(a, b):
    return jnp.dot(a, b, preferred_element_type=jnp.float32)


def combine(p, forward):
    rows, cols = p.shape
    c, s = p[: rows // 2], p[rows // 2 :]
    c_re, c_im = c[:, : cols // 2], c[:, cols // 2 :]
    s_re, s_im = s[:, : cols // 2], s[:, cols // 2 :]
    if forward:
        return c_re + s_im, c_im - s_re
    return c_re - s_im, c_im + s_re


def regroup(parts, split, perm, shape, axis):
    moved = [x.astype(jnp.bfloat16).reshape(split).transpose(perm).reshape(shape) for x in parts]
    return jnp.concatenate(moved, axis=axis)


def solve_field(density, devices, dev_index):
    xps = GX // devices
    kyls = GY // devices
    cz, sz = dft_pair(GZ)
    fa = jnp.asarray(np.concatenate([cz, -sz], axis=1), jnp.bfloat16)
    a = jnp.dot(
        density, jnp.concatenate([fa, fa], axis=0),
        preferred_element_type=jnp.bfloat16,
    )
    a_re = a[:, :GZ].reshape(GY, xps, GZ)
    a_im = a[:, GZ:].reshape(GY, xps, GZ)
    cy, sy = dft_pair(GY)
    fy = jnp.asarray(np.concatenate([cy, sy], axis=0), jnp.bfloat16)
    p = jnp.einsum("ky,ypz->kpz", fy, a_re, preferred_element_type=jnp.bfloat16)
    q = jnp.einsum("ky,ypz->kpz", fy, a_im, preferred_element_type=jnp.bfloat16)
    y_re = p[:GY] + q[GY:]
    y_im = q[:GY] - p[GY:]

    def by_dest(t):
        return t.reshape(devices, kyls, xps, GZ).transpose(0, 2, 1, 3)

    sent = jnp.stack([by_dest(y_re), by_dest(y_im)], axis=2).astype(jnp.bfloat16)
    r2 = lax.all_to_all(sent, AXES, 0, 0, tiled=True)
    cx, sx = dft_pair(GX)
    fx = jnp.asarray(np.concatenate([cx, sx], axis=0), jnp.bfloat16)
    p2 = jnp.einsum("kpx,pxrjz->krjz", fx.reshape(2 * GX, devices, xps), r2, preferred_element_type=jnp.bfloat16)
    z_re = p2[:GX, 0] + p2[GX:, 1]
    z_im = p2[:GX, 1] - p2[GX:, 0]
    kernel = green(
        wave_square(GX, 0, GX), wave_square(kyls, dev_index * kyls, GY), wave_square(GZ, 0, GZ)
    ) * (1.0 / (GX * GY * GZ))
    z = jnp.stack([z_re * kernel, z_im * kernel], axis=1).astype(jnp.bfloat16)
    p3 = jnp.einsum("xk,krjz->xrjz", fx, z, preferred_element_type=jnp.bfloat16)
    w_re = p3[:GX, 0] - p3[GX:, 1]
    w_im = p3[:GX, 1] + p3[GX:, 0]
    back = jnp.stack(
        [w_re.reshape(devices, xps, kyls, GZ), w_im.reshape(devices, xps, kyls, GZ)], axis=2
    ).astype(jnp.bfloat16)
    r3 = lax.all_to_all(back, AXES, 0, 0, tiled=True)
    r3 = r3.transpose(2, 1, 0, 3, 4).reshape(2 * xps, GY, GZ)
    p4 = jnp.einsum("yk,bkz->ybz", fy, r3, preferred_element_type=jnp.bfloat16).reshape(2 * GY, 2, xps, GZ)
    v_re = p4[:GY, 0] - p4[GY:, 1]
    v_im = p4[:GY, 1] + p4[GY:, 0]
    return jnp.concatenate([v_re, v_im], axis=-1).reshape(GY * xps, 2 * GZ).astype(jnp.bfloat16)


def gnn_layer(hidden, gathered, unit_w, radial_parts, w_self, w_nbr, w_rad, w_msg, w_out, gain):
    atoms, width = hidden.shape
    fanout = gathered.shape[0] // atoms
    gathered_h = gathered[:, :width]
    r_hi, r_lo = radial_parts
    w_hi, w_lo = split2(w_rad)
    lhs = jnp.concatenate([gathered_h, r_hi, r_lo, r_hi], axis=1)
    rhs = jnp.concatenate([w_nbr, w_hi, w_hi, w_lo], axis=0)
    own_term = mm(hidden, w_self)
    pre = mm(lhs, rhs).reshape(atoms, fanout, width) + own_term[:, None, :]
    message = silu(pre).astype(jnp.bfloat16)
    parts = jnp.einsum("akc,akf->acf", unit_w, message, preferred_element_type=jnp.float32)
    sums = jnp.concatenate([parts[:, :1], parts[:, 1:4] + parts[:, 4:7]], axis=1)
    s_hi, s_lo = split2(sums.reshape(atoms * 4, width))
    mixed = mm(jnp.concatenate([s_hi, s_lo], axis=1), jnp.concatenate([w_msg, w_msg], axis=0)).reshape(atoms, 4, width) / fanout
    total = mixed[:, 0] + jnp.sum(mixed[:, 1:] * mixed[:, 1:], axis=1)
    normed = total * lax.rsqrt(jnp.mean(total * total, axis=-1, keepdims=True) + norm_eps) * gain
    active = silu(normed).astype(jnp.bfloat16)
    update = mm(active, w_out)
    return (hidden.astype(jnp.float32) + update).astype(jnp.bfloat16)


def per_device(
    feats,
    coords,
    nbrs,
    owner,
    cell,
    w_self,
    w_nbr,
    w_rad,
    w_msg,
    w_out,
    norm_gain,
    w_charge,
    w_energy,
):
    atoms, width = feats.shape
    fanout = nbrs.shape[1]
    n_dom = lax.axis_size("dom")
    n_pme = lax.axis_size("pme")
    devices = n_dom * n_pme
    wide_rows = 3 * atoms
    pos_own = coords.T
    p_hi, p_mid, p_lo = split3(pos_own)
    wide0 = halo(jnp.concatenate([feats, p_hi, p_mid, p_lo], axis=1))
    flat_nbrs = nbrs.reshape(-1)
    onehot = (flat_nbrs[:, None] == jnp.arange(wide_rows, dtype=jnp.int32)[None, :]).astype(
        jnp.bfloat16
    )
    hidden = feats
    unit_w = None
    radial_parts = None
    for layer_idx in range(LAYERS):
        table = wide0 if layer_idx == 0 else halo(hidden)
        gathered = jnp.dot(onehot, table, preferred_element_type=jnp.bfloat16)
        if layer_idx == 0:
            gp = gathered[:, width:].astype(jnp.float32)
            pos_j = gp[:, 0:3] + gp[:, 3:6] + gp[:, 6:9]
            lift = jnp.where(flat_nbrs < atoms, -slab_depth, jnp.where(flat_nbrs >= 2 * atoms, slab_depth, 0.0))
            pos_j = pos_j + jnp.where(jnp.arange(3, dtype=jnp.int32) == 2, 1.0, 0.0)[None, :] * lift[:, None]
            delta = pos_j.reshape(atoms, fanout, 3) - pos_own[:, None, :]
            dist = jnp.sqrt(jnp.sum(delta * delta, axis=-1) + 1.0)
            centres = radial_width * (jnp.arange(NB, dtype=jnp.float32) + 1.0)
            radial = jnp.exp(-jnp.square((dist[:, :, None] - centres) / radial_width))
            radial_parts = split2(radial.reshape(atoms * fanout, NB))
            unit = delta / dist[:, :, None]
            u_hi, u_lo = split2(unit)
            unit_w = jnp.concatenate(
                [jnp.ones((atoms, fanout, 1), jnp.bfloat16), u_hi, u_lo, jnp.zeros((atoms, fanout, 1), jnp.bfloat16)],
                axis=-1,
            )
        hidden = gnn_layer(
            hidden,
            gathered,
            unit_w,
            radial_parts,
            w_self[layer_idx],
            w_nbr[layer_idx],
            w_rad[layer_idx],
            w_msg[layer_idx],
            w_out[layer_idx],
            norm_gain[layer_idx],
        )
    flat_hidden = hidden.astype(jnp.float32)
    readout = jnp.dot(flat_hidden, jnp.stack([w_energy, w_charge], axis=1), precision=highest)
    energy_ml = readout[:, 0]
    charge = readout[:, 1]
    capacity = max(2, 2 * atoms // devices) * n_pme
    bx = GX // n_dom
    by = GY // n_pme
    xps = GX // devices
    dest_owner = owner[:, 0]
    grid_x = dest_owner // n_pme * bx + cell // (by * GZ)
    grid_y = dest_owner % n_pme * by + cell // GZ % by
    grid_z = cell % GZ
    dest = grid_x // xps
    slab_cell = (grid_y * xps + grid_x % xps) * GZ + grid_z
    matches = (dest[:, None] == jnp.arange(devices, dtype=jnp.int32)[None, :]).astype(jnp.int32)
    slot = jnp.sum((jnp.cumsum(matches, axis=0) - matches) * matches, axis=1)
    where_to = dest * capacity + slot
    payload = jnp.stack([charge, slab_cell.astype(jnp.float32)], axis=1)
    outgoing = jnp.zeros((devices * capacity, 2), jnp.float32).at[where_to].set(payload)
    incoming = lax.all_to_all(outgoing, AXES, 0, 0, tiled=True)
    cells_here = incoming[:, 1].astype(jnp.int32)
    rows_here = cells_here // GZ
    z_here = cells_here % GZ
    n_rows = GY * xps
    oh_rows = (jnp.arange(n_rows, dtype=jnp.int32)[:, None] == rows_here[None, :]).astype(jnp.bfloat16)
    oh_z = z_here[:, None] == jnp.arange(GZ, dtype=jnp.int32)[None, :]
    q_hi, q_lo = split2(incoming[:, 0])
    zero = jnp.zeros((), jnp.bfloat16)
    qz = jnp.concatenate(
        [jnp.where(oh_z, q_hi[:, None], zero), jnp.where(oh_z, q_lo[:, None], zero)], axis=1
    )
    density = jnp.dot(oh_rows, qz, preferred_element_type=jnp.bfloat16)
    dev_index = lax.axis_index("dom") * n_pme + lax.axis_index("pme")
    spectrum_rows = solve_field(density, devices, dev_index)
    picked = lax.dot_general(
        oh_rows, spectrum_rows, (((0,), (0,)), ((), ())), preferred_element_type=jnp.bfloat16
    )
    cz, sz = dft_pair(GZ)
    ez_t = jnp.asarray(np.concatenate([cz, -sz], axis=1), jnp.bfloat16)
    ez_rows = jnp.dot(oh_z.astype(jnp.bfloat16), ez_t, preferred_element_type=jnp.bfloat16)
    sampled = jnp.sum(picked.astype(jnp.float32) * ez_rows.astype(jnp.float32), axis=1)
    returned = lax.all_to_all(sampled, AXES, 0, 0, tiled=True)
    at_atoms = returned[where_to]
    energy_el = 0.5 * charge * at_atoms
    return (energy_ml, energy_el)


def solution(mesh):
    in_specs = (
        P(("dom", "pme"), None),
        P(None, ("dom", "pme")),
        P(("dom", "pme"), None),
        P(("dom", "pme"), None),
        P(("dom", "pme")),
        P(),
        P(),
        P(),
        P(),
        P(),
        P(),
        P(),
        P(),
    )
    out_specs = (P(("dom", "pme")), P(("dom", "pme")))
    return jax.shard_map(
        per_device, mesh=mesh, in_specs=in_specs, out_specs=out_specs, check_vma=False
    )
```
